128 devices in a mesh: blk: 4 (over y_hi, core), feat: 32 (over y_lo, z, x).
Axes of the slice: x: 4, y: 4 (y_hi: 2, y_lo: 2; y = y_hi * 2 + y_lo), z: 4, core: 2. Of those that a mesh axis runs over, the one named last changes fastest.
Arguments:
- features_t: bfloat16 [128, 32768], P('feat', 'blk'), may hold values from -6 to 6
- weight: bfloat16 [128, 128], replicated, may hold values from -0.5 to 0.5
- tile_values: bfloat16 [32768, 128, 128], P(('blk', 'feat')), may hold values from -0.0625 to 0.0625
- tile_col: int32 [32768], P(('blk', 'feat')), may hold values from 0 to 255, as said below
- tile_count: int32 [1024], P(('blk', 'feat')), may hold values from 1 to 32, as said below
- grad_out: bfloat16 [32768, 128], P(('blk', 'feat')), may hold values from -6 to 6
Outputs:
- activations: bfloat16 [32768, 128], P(('blk', 'feat'))
- grad_features: bfloat16 [128, 32768], P('feat', 'blk')
- grad_weight: float32 [128, 128], P('feat')
The draws below stay inside these ranges and needn't reach their ends.
Inputs may be any that keep to these rules, and one draw needn't show every extreme that they name: `tile_count`: live slots of one tile row of one device for one column block; the first that many slots are live, and in every draw some entry equals 32. `tile_col`: the slots of column block c hold tile columns c * 64 to c * 64 + 63; columns may repeat within a tile row.
All inputs are finite; a program needn't handle non-finite values.
Results may differ from the reference program's by a relative error of at most 0.013.
Values may be sent and summed in bfloat16 or wider, within the bound.
No kernel may reach another device: no remote copies, remote signals or barrier semaphores. Data moves between devices by JAX's collectives and lax.ppermute only.
A program may use at most 128 MiB of HBM per device.

```python
import jax
import jax.numpy as jnp
from jax import lax

F = 128
H = 128
TILE = 128
ROWS_DEV = 256
SR = 32
NODES = 32768
TR = 2
N_TC = 64
N_BLK = 4
N_FEAT = 32


def draw_tile_count(key, part):
    device_count = NODES // ROWS_DEV
    per_device = N_BLK * TR
    key_heavy, key_large, key_small, key_spot = jax.random.split(key, 4)
    heavy = jax.random.randint(key_heavy, (device_count, 1), 0, 4) == 0
    large_counts = jax.random.randint(key_large, (device_count, per_device), SR // 2, SR + 1)
    small_counts = jax.random.randint(key_small, (device_count, per_device), 1, SR // 4 + 1)
    counts = jnp.where(heavy, large_counts, small_counts).reshape(-1)
    total = device_count * per_device
    spot = jax.random.randint(key_spot, (), 0, total)
    position = jnp.arange(total).astype(jnp.int32)
    counts = jnp.where(position == spot, SR, counts)
    counts = jnp.where(position == (spot + 1) % total, 1, counts)
    return counts.astype(jnp.int32)


def draw_tile_col(key, part):
    device_count = NODES // ROWS_DEV
    total = device_count * N_BLK * TR * SR
    position = jnp.arange(total).astype(jnp.int32)
    slot_index = position % SR
    row_index = position // SR % TR
    block_index = position // (SR * TR) % N_BLK
    device_index = position // (SR * TR * N_BLK)
    random_cols = jax.random.randint(key, (total,), 0, N_TC)
    local_cols = jnp.where(slot_index == 0, (device_index * TR + row_index) % N_TC, random_cols)
    return (block_index * N_TC + local_cols).astype(jnp.int32)


def steps_of(stream_key, dims, shards, low, largest):
    level, own = 1.0, jax.random.fold_in(stream_key, 6)
    for axis_at, parts in shards:
        steps = jnp.exp(jax.random.uniform(jax.random.fold_in(own, axis_at), (parts,), jnp.float32, low / len(shards), largest / len(shards)))
        level = level * jnp.repeat(steps, dims[axis_at] // parts).reshape([-1 if axis == axis_at else 1 for axis in range(len(dims))])
    return level


def gaussian(rng, dims, deviation, reach, cuts=(), held_as=jnp.bfloat16):
    gain = steps_of(rng, dims, cuts, -0.22, 0.18) if cuts else 1.0
    entries = jax.random.normal(rng, dims, jnp.float32) * deviation * gain
    return jnp.minimum(jnp.maximum(entries, -reach), reach).astype(held_as)


def setup_inputs(seed: int = 0) -> dict:
    arg_keys = jax.random.split(jax.random.key(seed), 7)
    features_t = gaussian(arg_keys[0], (F, NODES), 1.0, 6.0, ((0, 32), (1, 4)))
    weight = gaussian(arg_keys[1], (F, H), F ** -0.5, 0.5)
    tile_values = gaussian(arg_keys[2], (NODES // TILE * N_BLK * SR, TILE, TILE), (TILE * N_BLK * SR // 2) ** -0.5, 0.0625, ((0, 128),))
    tile_col = draw_tile_col(jax.random.fold_in(arg_keys[6], 71), 0)
    tile_count = draw_tile_count(jax.random.fold_in(arg_keys[6], 71), 0)
    grad_out = gaussian(arg_keys[5], (NODES, H), 1.0, 6.0, ((0, 128),))
    return {"features_t": features_t, "weight": weight, "tile_values": tile_values, "tile_col": tile_col, "tile_count": tile_count, "grad_out": grad_out}


def reference(features_t, weight, tile_values, tile_col, tile_count, grad_out):
    device_count = N_BLK * N_FEAT
    node_count = features_t.shape[1]
    tile_stack = tile_values.reshape(device_count, N_BLK, TR, SR, TILE, TILE)
    slot_index = jnp.arange(SR).astype(jnp.int32)
    live_mask = slot_index[None, None, None, :] < tile_count.reshape(device_count, N_BLK, TR, 1)
    tile_stack = jnp.where(live_mask[..., None, None], tile_stack, jnp.zeros((), jnp.bfloat16))
    tile_cols = tile_col.reshape(device_count, N_BLK, TR, SR)
    projected = jnp.dot(features_t.T, weight, preferred_element_type=jnp.float32).astype(jnp.bfloat16)
    projected_tiles = projected.reshape(node_count // TILE, TILE, H)

    def forward_one(tile_pair):
        tiles_here, cols_here = tile_pair
        picked = jnp.take(projected_tiles, cols_here, axis=0).astype(jnp.float32)
        return jnp.einsum('crsij,crsjh->rih', tiles_here.astype(jnp.float32), picked)
    pre_act = lax.map(forward_one, (tile_stack, tile_cols)).reshape(node_count, H)
    sigmoid_y = jax.nn.sigmoid(pre_act)
    activations = (pre_act * sigmoid_y).astype(jnp.bfloat16)
    grad_pre = (grad_out.astype(jnp.float32) * sigmoid_y * (1.0 + pre_act * (1.0 - sigmoid_y))).astype(jnp.bfloat16)
    grad_rows = grad_pre.reshape(device_count, TR, TILE, H)

    def backward_one(column_total, triple):
        tiles_here, cols_here, grad_here = triple
        contrib = jnp.einsum('crsij,rih->crsjh', tiles_here.astype(jnp.float32), grad_here.astype(jnp.float32))
        return (column_total.at[cols_here.reshape(-1)].add(contrib.reshape(-1, TILE, H)), None)
    start_total = jnp.zeros((node_count // TILE, TILE, H), jnp.float32)
    grad_hidden, _ = lax.scan(backward_one, start_total, (tile_stack, tile_cols, grad_rows))
    grad_hidden = grad_hidden.reshape(node_count, H).astype(jnp.bfloat16)
    grad_weight = jnp.dot(features_t, grad_hidden, preferred_element_type=jnp.float32) * lax.rsqrt(jnp.float32(node_count))
    grad_features = jnp.dot(weight, grad_hidden.T, preferred_element_type=jnp.float32).astype(jnp.bfloat16)
    return (activations, grad_features, grad_weight)
```

```python
import jax
import jax.numpy as jnp
from jax import lax
from jax.sharding import PartitionSpec as P


def shifted(block, axis, distance):
    devices = range(lax.axis_size(axis))
    route = [((i - distance) % len(devices), i) for i in devices]
    return lax.ppermute(block, axis, route)


def swapped(block, axis, mask):
    count = lax.axis_size(axis)
    return lax.ppermute(block, axis, [(i, i ^ mask) for i in range(count)])


def gather_rows(block, axis):
    count = lax.axis_size(axis)
    index = lax.axis_index(axis)
    mask = 1
    while mask < count:
        other = swapped(block, axis, mask)
        upper = (index // mask) % 2 == 1
        block = jnp.where(
            upper,
            jnp.concatenate([other, block], axis=0),
            jnp.concatenate([block, other], axis=0),
        )
        mask *= 2
    return block


def scatter_rows(total, axis, wire_type):
    count = lax.axis_size(axis)
    index = lax.axis_index(axis)
    mask = count // 2
    while mask >= 1:
        half = total.shape[0] // 2
        lower, upper_part = total[:half], total[half:]
        upper = (index // mask) % 2 == 1
        keep = jnp.where(upper, upper_part, lower)
        send = jnp.where(upper, lower, upper_part)
        got = swapped(send.astype(wire_type), axis, mask)
        total = keep + got.astype(jnp.float32)
        mask //= 2
    return total


def body(features_t, weight, tile_values, tile_col, tile_count, grad_out):
    cycle_size = lax.axis_size("blk")
    hidden_width = weight.shape[1]
    tile_size = tile_values.shape[1]
    rows_own = grad_out.shape[0]
    tile_rows = rows_own // tile_size
    block_rows = features_t.shape[1]
    block_tiles = block_rows // tile_size
    slot_count = tile_values.shape[0] // (cycle_size * tile_rows)
    feat_id = lax.axis_index("feat")
    blk_id = lax.axis_index("blk")
    slot_index = lax.broadcasted_iota(jnp.int32, (cycle_size, tile_rows, slot_count), 2)
    live_mask = slot_index < tile_count.reshape(cycle_size, tile_rows, 1)
    tile_stack = tile_values.reshape(cycle_size, tile_rows, slot_count, tile_size, tile_size)
    tile_stack = jnp.where(live_mask[..., None, None], tile_stack, jnp.zeros((), jnp.bfloat16))
    local_cols = (tile_col % block_tiles).reshape(cycle_size, tile_rows, slot_count)
    features_block = gather_rows(features_t, "feat")
    projected = lax.dot_general(
        features_block,
        weight,
        (((0,), (0,)), ((), ())),
        preferred_element_type=jnp.float32,
    ).astype(jnp.bfloat16)

    def aggregate(block_value, block_id):
        block_tiles_view = block_value.reshape(block_tiles, tile_size, hidden_width)
        cols_here = lax.dynamic_index_in_dim(local_cols, block_id, 0, keepdims=False)
        tiles_here = lax.dynamic_index_in_dim(tile_stack, block_id, 0, keepdims=False)
        picked = jnp.take(block_tiles_view, cols_here, axis=0)
        return jnp.einsum("rsij,rsjh->rih", tiles_here, picked, preferred_element_type=jnp.float32)

    aggregate_sum = aggregate(projected, blk_id)
    moving = projected
    for turn_index in range(cycle_size - 1):
        moving = shifted(moving, "blk", 1)
        aggregate_sum = aggregate_sum + aggregate(moving, (blk_id - turn_index - 1) % cycle_size)
    pre_act = aggregate_sum.reshape(rows_own, hidden_width)
    sigmoid_y = jax.nn.sigmoid(pre_act)
    activations = (pre_act * sigmoid_y).astype(jnp.bfloat16)
    grad_pre = (
        grad_out.astype(jnp.float32) * sigmoid_y * (1.0 + pre_act * (1.0 - sigmoid_y))
    ).astype(jnp.bfloat16)
    grad_tiles = grad_pre.reshape(tile_rows, tile_size, hidden_width)

    def spread(block_id):
        tiles_here = lax.dynamic_index_in_dim(tile_stack, block_id, 0, keepdims=False)
        cols_here = lax.dynamic_index_in_dim(local_cols, block_id, 0, keepdims=False)
        contrib = jnp.einsum(
            "rsij,rih->rsjh", tiles_here, grad_tiles, preferred_element_type=jnp.float32
        )
        empty_block = jnp.zeros((block_tiles, tile_size, hidden_width), jnp.float32)
        return empty_block.at[cols_here.reshape(-1)].add(
            contrib.reshape(-1, tile_size, hidden_width)
        ).reshape(block_rows, hidden_width)

    block_total = spread(blk_id)
    for distance in range(1, cycle_size):
        outgoing = spread((blk_id + distance) % cycle_size).astype(jnp.bfloat16)
        block_total = block_total + shifted(outgoing, "blk", distance).astype(jnp.float32)
    grad_own = scatter_rows(block_total, "feat", jnp.bfloat16)
    grad_hidden = grad_own.astype(jnp.bfloat16)

    features_own = lax.dynamic_slice_in_dim(features_block, feat_id * rows_own, rows_own, 1)
    weight_term = jnp.dot(features_own, grad_hidden, preferred_element_type=jnp.float32)
    weight_part = scatter_rows(weight_term, "feat", jnp.float32)
    weight_part = weight_part + swapped(weight_part, "blk", 1)
    weight_part = weight_part + swapped(weight_part, "blk", 2)
    grad_weight = weight_part * lax.rsqrt(jnp.float32(block_rows * cycle_size))

    features_grad_local = lax.dot_general(
        weight, grad_hidden, (((1,), (1,)), ((), ())), preferred_element_type=jnp.float32
    ).astype(jnp.bfloat16)
    grad_features = lax.all_to_all(
        features_grad_local, "feat", split_axis=0, concat_axis=1, tiled=True
    )
    return (activations, grad_features, grad_weight)


def solution(mesh):
    placed = (
        P("feat", "blk"),
        P(),
        P(("blk", "feat"), None, None),
        P(("blk", "feat")),
        P(("blk", "feat")),
        P(("blk", "feat"), None),
    )
    return jax.shard_map(
        body,
        mesh=mesh,
        in_specs=placed,
        out_specs=(P(("blk", "feat"), None), P("feat", "blk"), P("feat", None)),
        check_vma=False,
    )
```

```python
import jax
import jax.numpy as jnp
from jax import lax
from jax.sharding import PartitionSpec as P
from jax.experimental import pallas as pl
from jax.experimental.pallas import tpu as pltpu


def shifted(block, axis, distance):
    devices = range(lax.axis_size(axis))
    route = [((i - distance) % len(devices), i) for i in devices]
    return lax.ppermute(block, axis, route)


def swapped(block, axis, mask):
    count = lax.axis_size(axis)
    return lax.ppermute(block, axis, [(i, i ^ mask) for i in range(count)])


def gather_rows(block, axis):
    count = lax.axis_size(axis)
    index = lax.axis_index(axis)
    mask = 1
    while mask < count:
        other = swapped(block, axis, mask)
        upper = (index // mask) % 2 == 1
        block = jnp.where(
            upper,
            jnp.concatenate([other, block], axis=0),
            jnp.concatenate([block, other], axis=0),
        )
        mask *= 2
    return block


def scatter_rows(total, axis, wire_type):
    count = lax.axis_size(axis)
    index = lax.axis_index(axis)
    mask = count // 2
    while mask >= 1:
        half = total.shape[0] // 2
        lower, upper_part = total[:half], total[half:]
        upper = (index // mask) % 2 == 1
        keep = jnp.where(upper, upper_part, lower)
        send = jnp.where(upper, lower, upper_part)
        got = swapped(send.astype(wire_type), axis, mask)
        total = keep + got.astype(jnp.float32)
        mask //= 2
    return total


def aggregate_kernel(block_ref, cols_ref, count_ref, tiles_ref, proj_ref, out_ref):
    row = pl.program_id(0)
    tile_rows = pl.num_programs(0)
    slot_count = tiles_ref.shape[0]
    base = block_ref[0] * tile_rows + row
    live = count_ref[base]

    def step(slot, total):
        col = cols_ref[base * slot_count + slot]
        return total + jnp.dot(tiles_ref[slot], proj_ref[col], preferred_element_type=jnp.float32)

    out_ref[...] = lax.fori_loop(0, live, step, jnp.zeros(out_ref.shape, jnp.float32))


def aggregate_block(block_id, cols, counts, tile_stack, block_value):
    blocks, tile_rows, slot_count, tile_size, _ = tile_stack.shape
    hidden_width = block_value.shape[-1]
    block_tiles = block_value.shape[0] // tile_size
    grid_spec = pltpu.PrefetchScalarGridSpec(
        num_scalar_prefetch=3,
        grid=(tile_rows,),
        in_specs=[
            pl.BlockSpec(
                (None, None, slot_count, tile_size, tile_size),
                lambda r, b, c, n: (b[0], r, 0, 0, 0),
            ),
            pl.BlockSpec(
                (block_tiles, tile_size, hidden_width), lambda r, b, c, n: (0, 0, 0)
            ),
        ],
        out_specs=pl.BlockSpec((None, tile_size, hidden_width), lambda r, b, c, n: (r, 0, 0)),
    )
    return pl.pallas_call(
        aggregate_kernel,
        grid_spec=grid_spec,
        out_shape=jax.ShapeDtypeStruct((tile_rows, tile_size, hidden_width), jnp.float32),
        compiler_params=pltpu.CompilerParams(dimension_semantics=("arbitrary",)),
    )(
        jnp.reshape(block_id, (1,)).astype(jnp.int32),
        cols,
        counts,
        tile_stack,
        block_value.reshape(block_tiles, tile_size, hidden_width),
    )


def spread_kernel(block_ref, cols_ref, count_ref, tiles_ref, grad_ref, out_ref, total_ref):
    row = pl.program_id(0)
    tile_rows = pl.num_programs(0)
    slot_count = tiles_ref.shape[0]
    base = block_ref[0] * tile_rows + row
    live = count_ref[base]

    @pl.when(row == 0)
    def _():
        total_ref[...] = jnp.zeros(total_ref.shape, jnp.float32)

    grad_rows = grad_ref[...]

    def step(slot, carry):
        col = cols_ref[base * slot_count + slot]
        total_ref[col] += lax.dot_general(
            tiles_ref[slot], grad_rows, (((0,), (0,)), ((), ())),
            preferred_element_type=jnp.float32,
        )
        return carry

    lax.fori_loop(0, live, step, 0)

    @pl.when(row == tile_rows - 1)
    def _():
        out_ref[...] = total_ref[...].astype(out_ref.dtype)


def spread_block(block_id, cols, counts, tile_stack, grad_tiles, block_tiles, out_type):
    blocks, tile_rows, slot_count, tile_size, _ = tile_stack.shape
    hidden_width = grad_tiles.shape[-1]
    grid_spec = pltpu.PrefetchScalarGridSpec(
        num_scalar_prefetch=3,
        grid=(tile_rows,),
        in_specs=[
            pl.BlockSpec(
                (None, None, slot_count, tile_size, tile_size),
                lambda r, b, c, n: (b[0], r, 0, 0, 0),
            ),
            pl.BlockSpec((None, tile_size, hidden_width), lambda r, b, c, n: (r, 0, 0)),
        ],
        out_specs=pl.BlockSpec(
            (block_tiles, tile_size, hidden_width), lambda r, b, c, n: (0, 0, 0)
        ),
        scratch_shapes=[pltpu.VMEM((block_tiles, tile_size, hidden_width), jnp.float32)],
    )
    out = pl.pallas_call(
        spread_kernel,
        grid_spec=grid_spec,
        out_shape=jax.ShapeDtypeStruct((block_tiles, tile_size, hidden_width), out_type),
        compiler_params=pltpu.CompilerParams(dimension_semantics=("arbitrary",)),
    )(
        jnp.reshape(block_id, (1,)).astype(jnp.int32),
        cols,
        counts,
        tile_stack,
        grad_tiles,
    )
    return out.reshape(block_tiles * tile_size, hidden_width)


def body(features_t, weight, tile_values, tile_col, tile_count, grad_out):
    cycle_size = lax.axis_size("blk")
    hidden_width = weight.shape[1]
    tile_size = tile_values.shape[1]
    rows_own = grad_out.shape[0]
    tile_rows = rows_own // tile_size
    block_rows = features_t.shape[1]
    block_tiles = block_rows // tile_size
    slot_count = tile_values.shape[0] // (cycle_size * tile_rows)
    feat_id = lax.axis_index("feat")
    blk_id = lax.axis_index("blk")
    tile_stack = tile_values.reshape(cycle_size, tile_rows, slot_count, tile_size, tile_size)
    local_cols = tile_col % block_tiles
    counts = tile_count
    features_block = gather_rows(features_t, "feat")
    projected = lax.dot_general(
        features_block,
        weight,
        (((0,), (0,)), ((), ())),
        preferred_element_type=jnp.float32,
    ).astype(jnp.bfloat16)

    aggregate_sum = aggregate_block(blk_id, local_cols, counts, tile_stack, projected)
    for distance in range(1, cycle_size):
        moving = shifted(projected, "blk", distance)
        aggregate_sum = aggregate_sum + aggregate_block(
            (blk_id - distance) % cycle_size, local_cols, counts, tile_stack, moving
        )
    pre_act = aggregate_sum.reshape(rows_own, hidden_width)
    sigmoid_y = jax.nn.sigmoid(pre_act)
    activations = (pre_act * sigmoid_y).astype(jnp.bfloat16)
    grad_pre = (
        grad_out.astype(jnp.float32) * sigmoid_y * (1.0 + pre_act * (1.0 - sigmoid_y))
    ).astype(jnp.bfloat16)
    grad_tiles = grad_pre.reshape(tile_rows, tile_size, hidden_width)

    block_total = None
    for distance in range(1, cycle_size):
        outgoing = spread_block(
            (blk_id + distance) % cycle_size, local_cols, counts, tile_stack, grad_tiles,
            block_tiles, jnp.bfloat16,
        )
        arrived = shifted(outgoing, "blk", distance).astype(jnp.float32)
        block_total = arrived if block_total is None else block_total + arrived
    block_total = block_total + spread_block(
        blk_id, local_cols, counts, tile_stack, grad_tiles, block_tiles, jnp.float32
    )
    grad_own = scatter_rows(block_total, "feat", jnp.bfloat16)
    grad_hidden = grad_own.astype(jnp.bfloat16)

    features_own = lax.dynamic_slice_in_dim(features_block, feat_id * rows_own, rows_own, 1)
    weight_term = jnp.dot(features_own, grad_hidden, preferred_element_type=jnp.float32)
    weight_part = scatter_rows(weight_term, "feat", jnp.float32)
    weight_part = weight_part + swapped(weight_part, "blk", 1)
    weight_part = weight_part + swapped(weight_part, "blk", 2)
    grad_weight = weight_part * lax.rsqrt(jnp.float32(block_rows * cycle_size))

    features_grad_local = lax.dot_general(
        weight, grad_hidden, (((1,), (1,)), ((), ())), preferred_element_type=jnp.float32
    ).astype(jnp.bfloat16)
    grad_features = lax.all_to_all(
        features_grad_local, "feat", split_axis=0, concat_axis=1, tiled=True
    )
    return (activations, grad_features, grad_weight)


def solution(mesh):
    placed = (
        P("feat", "blk"),
        P(),
        P(("blk", "feat"), None, None),
        P(("blk", "feat")),
        P(("blk", "feat")),
        P(("blk", "feat"), None),
    )
    return jax.shard_map(
        body,
        mesh=mesh,
        in_specs=placed,
        out_specs=(P(("blk", "feat"), None), P("feat", "blk"), P("feat", None)),
        check_vma=False,
    )
```

```python
import jax
import jax.numpy as jnp
from jax import lax
from jax.sharding import PartitionSpec as P
from jax.experimental import pallas as pl
from jax.experimental.pallas import tpu as pltpu

RING = 4
GATHER_ORDER = (("x", "z", "y"), ("y", "z", "x"))
BOTH = ("blk", "feat")


def place_of(blk, feat):
    return {
        "core": blk % 2,
        "y": (blk // 2) * 2 + feat // 16,
        "z": (feat // 4) % 4,
        "x": feat % 4,
    }


def linear_of(place):
    blk = (place["y"] // 2) * 2 + place["core"]
    feat = (place["y"] % 2) * 16 + place["z"] * 4 + place["x"]
    return blk * 32 + feat


def ring_shift(block, phase, distance):
    route = []
    for blk in range(4):
        for feat in range(32):
            place = place_of(blk, feat)
            axis = GATHER_ORDER[place["core"]][phase]
            target = dict(place)
            target[axis] = (place[axis] + distance) % RING
            route.append((linear_of(place), linear_of(target)))
    return lax.ppermute(block, BOTH, route)


def sibling(block):
    return lax.ppermute(block, "blk", [(i, i ^ 1) for i in range(lax.axis_size("blk"))])


def swapped(block, axis, mask):
    count = lax.axis_size(axis)
    return lax.ppermute(block, axis, [(i, i ^ mask) for i in range(count)])


def gather_phase(block, phase):
    half = block.shape[-2] // 2
    from_minus = ring_shift(block, phase, 1)
    from_plus = ring_shift(block, phase, -1)
    far_low = ring_shift(from_minus[..., :half, :], phase, 1)
    far_high = ring_shift(from_plus[..., half:, :], phase, -1)
    far = jnp.concatenate([far_low, far_high], axis=-2)
    return jnp.stack([block, from_plus, far, from_minus])


def reduce_phase(total, phase, wire_type):
    half = total.shape[-2] // 2
    far = total[2]
    got_minus = ring_shift(far[..., :half, :].astype(wire_type), phase, 1)
    got_plus = ring_shift(far[..., half:, :].astype(wire_type), phase, -1)
    ahead = total[1]
    ahead = jnp.concatenate(
        [ahead[..., :half, :] + got_minus.astype(jnp.float32), ahead[..., half:, :]], axis=-2
    )
    behind = total[3]
    behind = jnp.concatenate(
        [behind[..., :half, :], behind[..., half:, :] + got_plus.astype(jnp.float32)], axis=-2
    )
    from_minus = ring_shift(ahead.astype(wire_type), phase, 1)
    from_plus = ring_shift(behind.astype(wire_type), phase, -1)
    return total[0] + from_minus.astype(jnp.float32) + from_plus.astype(jnp.float32)


def scatter_rows(total, axis, wire_type):
    count = lax.axis_size(axis)
    index = lax.axis_index(axis)
    mask = count // 2
    while mask >= 1:
        half = total.shape[0] // 2
        lower, upper_part = total[:half], total[half:]
        upper = (index // mask) % 2 == 1
        keep = jnp.where(upper, upper_part, lower)
        send = jnp.where(upper, lower, upper_part)
        got = swapped(send.astype(wire_type), axis, mask)
        total = keep + got.astype(jnp.float32)
        mask //= 2
    return total


def aggregate_kernel(core_ref, where_ref, count_ref, tiles_ref, proj_ref, out_ref):
    row = pl.program_id(0)
    half_id = pl.program_id(1)
    tile_rows = pl.num_programs(0)
    slot_count = tiles_ref.shape[0]
    base = (half_id * 2 + core_ref[0]) * tile_rows + row
    live = count_ref[base]

    def step(slot, total):
        spot = where_ref[base * slot_count + slot]
        return total + jnp.dot(tiles_ref[slot], proj_ref[spot], preferred_element_type=jnp.float32)

    part = lax.fori_loop(0, live, step, jnp.zeros(out_ref.shape, jnp.float32))

    @pl.when(half_id == 0)
    def _():
        out_ref[...] = part

    @pl.when(half_id != 0)
    def _():
        out_ref[...] += part


def aggregate_pair(core_id, spots, counts, tile_stack, buffer):
    blocks, tile_rows, slot_count, tile_size, _ = tile_stack.shape
    hidden_width = buffer.shape[-1]
    grid_spec = pltpu.PrefetchScalarGridSpec(
        num_scalar_prefetch=3,
        grid=(tile_rows, blocks // 2),
        in_specs=[
            pl.BlockSpec(
                (None, None, slot_count, tile_size, tile_size),
                lambda r, h, c, w, n: (h * 2 + c[0], r, 0, 0, 0),
            ),
            pl.BlockSpec(buffer.shape, lambda r, h, c, w, n: (0, 0, 0)),
        ],
        out_specs=pl.BlockSpec((None, tile_size, hidden_width), lambda r, h, c, w, n: (r, 0, 0)),
    )
    return pl.pallas_call(
        aggregate_kernel,
        grid_spec=grid_spec,
        out_shape=jax.ShapeDtypeStruct((tile_rows, tile_size, hidden_width), jnp.float32),
        compiler_params=pltpu.CompilerParams(dimension_semantics=("arbitrary", "arbitrary")),
    )(jnp.reshape(core_id, (1,)).astype(jnp.int32), spots, counts, tile_stack, buffer)


def spread_kernel(core_ref, where_ref, count_ref, tiles_ref, grad_ref, out_ref, total_ref):
    row = pl.program_id(0)
    half_id = pl.program_id(1)
    tile_rows = pl.num_programs(0)
    halves = pl.num_programs(1)
    slot_count = tiles_ref.shape[0]
    base = (half_id * 2 + core_ref[0]) * tile_rows + row
    live = count_ref[base]

    @pl.when((row == 0) & (half_id == 0))
    def _():
        total_ref[...] = jnp.zeros(total_ref.shape, jnp.float32)

    grad_rows = grad_ref[...]

    def step(slot, carry):
        spot = where_ref[base * slot_count + slot]
        total_ref[spot] += lax.dot_general(
            tiles_ref[slot], grad_rows, (((0,), (0,)), ((), ())),
            preferred_element_type=jnp.float32,
        )
        return carry

    lax.fori_loop(0, live, step, 0)

    @pl.when((row == tile_rows - 1) & (half_id == halves - 1))
    def _():
        out_ref[...] = total_ref[...].astype(out_ref.dtype)


def spread_pair(core_id, spots, counts, tile_stack, grad_tiles, buffer_tiles, out_type):
    blocks, tile_rows, slot_count, tile_size, _ = tile_stack.shape
    hidden_width = grad_tiles.shape[-1]
    grid_spec = pltpu.PrefetchScalarGridSpec(
        num_scalar_prefetch=3,
        grid=(tile_rows, blocks // 2),
        in_specs=[
            pl.BlockSpec(
                (None, None, slot_count, tile_size, tile_size),
                lambda r, h, c, w, n: (h * 2 + c[0], r, 0, 0, 0),
            ),
            pl.BlockSpec((None, tile_size, hidden_width), lambda r, h, c, w, n: (r, 0, 0)),
        ],
        out_specs=pl.BlockSpec(
            (buffer_tiles, tile_size, hidden_width), lambda r, h, c, w, n: (0, 0, 0)
        ),
        scratch_shapes=[pltpu.VMEM((buffer_tiles, tile_size, hidden_width), jnp.float32)],
    )
    return pl.pallas_call(
        spread_kernel,
        grid_spec=grid_spec,
        out_shape=jax.ShapeDtypeStruct((buffer_tiles, tile_size, hidden_width), out_type),
        compiler_params=pltpu.CompilerParams(dimension_semantics=("arbitrary", "arbitrary")),
    )(jnp.reshape(core_id, (1,)).astype(jnp.int32), spots, counts, tile_stack, grad_tiles)


def buffer_spots(tile_col, blk_id, feat_id, block_tiles, tiles_per_device):
    own = place_of(blk_id, feat_id)
    block = tile_col // block_tiles
    local = tile_col % block_tiles
    source_feat = local // tiles_per_device
    part = local % tiles_per_device
    source = place_of(block, source_feat)
    rel = {axis: (source[axis] - own[axis]) % RING for axis in ("y", "z", "x")}
    chunk = jnp.where(
        source["core"] == 0,
        rel["y"] * 16 + rel["z"] * 4 + rel["x"],
        rel["x"] * 16 + rel["z"] * 4 + rel["y"],
    )
    return (chunk * tiles_per_device + part).astype(jnp.int32)


def body(features_t, weight, tile_values, tile_col, tile_count, grad_out):
    cycle_size = lax.axis_size("blk")
    hidden_width = weight.shape[1]
    tile_size = tile_values.shape[1]
    rows_own = grad_out.shape[0]
    tile_rows = rows_own // tile_size
    block_rows = features_t.shape[1]
    block_tiles = block_rows // tile_size
    slot_count = tile_values.shape[0] // (cycle_size * tile_rows)
    feat_id = lax.axis_index("feat")
    blk_id = lax.axis_index("blk")
    core_id = blk_id % 2
    tile_stack = tile_values.reshape(cycle_size, tile_rows, slot_count, tile_size, tile_size)
    spots = buffer_spots(tile_col, blk_id, feat_id, block_tiles, tile_rows)
    buffer_tiles = block_tiles * 2

    features_own = lax.all_to_all(features_t, "feat", split_axis=1, concat_axis=0, tiled=True)
    projected = lax.dot_general(
        features_own, weight, (((0,), (0,)), ((), ())), preferred_element_type=jnp.float32
    ).astype(jnp.bfloat16)

    gathered = projected
    for phase in range(3):
        gathered = gather_phase(gathered, phase)
    own_buffer = gathered.reshape(buffer_tiles, tile_size, hidden_width)
    other_buffer = sibling(own_buffer)
    aggregate_sum = aggregate_pair(core_id, spots, tile_count, tile_stack, own_buffer)
    aggregate_sum = aggregate_sum + aggregate_pair(
        1 - core_id, spots, tile_count, tile_stack, other_buffer
    )

    pre_act = aggregate_sum.reshape(rows_own, hidden_width)
    sigmoid_y = jax.nn.sigmoid(pre_act)
    activations = (pre_act * sigmoid_y).astype(jnp.bfloat16)
    grad_pre = (
        grad_out.astype(jnp.float32) * sigmoid_y * (1.0 + pre_act * (1.0 - sigmoid_y))
    ).astype(jnp.bfloat16)
    grad_tiles = grad_pre.reshape(tile_rows, tile_size, hidden_width)

    outgoing = spread_pair(
        1 - core_id, spots, tile_count, tile_stack, grad_tiles, buffer_tiles, jnp.bfloat16
    )
    arrived = sibling(outgoing)
    total = spread_pair(
        core_id, spots, tile_count, tile_stack, grad_tiles, buffer_tiles, jnp.float32
    )
    total = total + arrived.astype(jnp.float32)
    total = total.reshape(RING, RING, RING, rows_own, hidden_width)
    for phase in (2, 1, 0):
        total = reduce_phase(total, phase, jnp.bfloat16)
    grad_hidden = total.astype(jnp.bfloat16)

    weight_term = jnp.dot(features_own, grad_hidden, preferred_element_type=jnp.float32)
    weight_part = scatter_rows(weight_term, "feat", jnp.float32)
    weight_part = weight_part + swapped(weight_part, "blk", 1)
    weight_part = weight_part + swapped(weight_part, "blk", 2)
    grad_weight = weight_part * lax.rsqrt(jnp.float32(block_rows * cycle_size))

    features_grad_local = lax.dot_general(
        weight, grad_hidden, (((1,), (1,)), ((), ())), preferred_element_type=jnp.float32
    ).astype(jnp.bfloat16)
    grad_features = lax.all_to_all(
        features_grad_local, "feat", split_axis=0, concat_axis=1, tiled=True
    )
    return (activations, grad_features, grad_weight)


def solution(mesh):
    placed = (
        P("feat", "blk"),
        P(),
        P(("blk", "feat"), None, None),
        P(("blk", "feat")),
        P(("blk", "feat")),
        P(("blk", "feat"), None),
    )
    return jax.shard_map(
        body,
        mesh=mesh,
        in_specs=placed,
        out_specs=(P(("blk", "feat"), None), P("feat", "blk"), P("feat", None)),
        check_vma=False,
    )
```

```python
import jax
import jax.numpy as jnp
from jax import lax
from jax.sharding import PartitionSpec as P
from jax.experimental import pallas as pl
from jax.experimental.pallas import tpu as pltpu

RING = 4
GATHER_ORDER = (("x", "z", "y"), ("y", "z", "x"))
BOTH = ("blk", "feat")


def place_of(blk, feat):
    return {
        "core": blk % 2,
        "y": (blk // 2) * 2 + feat // 16,
        "z": (feat // 4) % 4,
        "x": feat % 4,
    }


def linear_of(place):
    blk = (place["y"] // 2) * 2 + place["core"]
    feat = (place["y"] % 2) * 16 + place["z"] * 4 + place["x"]
    return blk * 32 + feat


def ring_shift(block, phase, distance):
    route = []
    for blk in range(4):
        for feat in range(32):
            place = place_of(blk, feat)
            axis = GATHER_ORDER[place["core"]][phase]
            target = dict(place)
            target[axis] = (place[axis] + distance) % RING
            route.append((linear_of(place), linear_of(target)))
    return lax.ppermute(block, BOTH, route)


def sibling(block):
    return lax.ppermute(block, "blk", [(i, i ^ 1) for i in range(lax.axis_size("blk"))])


def swapped(block, axis, mask):
    count = lax.axis_size(axis)
    return lax.ppermute(block, axis, [(i, i ^ mask) for i in range(count)])


def gather_phase(block, phase):
    half = block.shape[-2] // 2
    from_minus = ring_shift(block, phase, 1)
    from_plus = ring_shift(block, phase, -1)
    far_low = ring_shift(from_minus[..., :half, :], phase, 1)
    far_high = ring_shift(from_plus[..., half:, :], phase, -1)
    far = jnp.concatenate([far_low, far_high], axis=-2)
    return jnp.stack([block, from_plus, far, from_minus])


def reduce_phase(total, phase, wire_type):
    half = total.shape[-2] // 2
    far = total[2]
    got_minus = ring_shift(far[..., :half, :].astype(wire_type), phase, 1)
    got_plus = ring_shift(far[..., half:, :].astype(wire_type), phase, -1)
    ahead = total[1]
    ahead = jnp.concatenate(
        [ahead[..., :half, :] + got_minus.astype(jnp.float32), ahead[..., half:, :]], axis=-2
    )
    behind = total[3]
    behind = jnp.concatenate(
        [behind[..., :half, :], behind[..., half:, :] + got_plus.astype(jnp.float32)], axis=-2
    )
    from_minus = ring_shift(ahead.astype(wire_type), phase, 1)
    from_plus = ring_shift(behind.astype(wire_type), phase, -1)
    return total[0] + from_minus.astype(jnp.float32) + from_plus.astype(jnp.float32)


def scatter_rows(total, axis, wire_type):
    count = lax.axis_size(axis)
    index = lax.axis_index(axis)
    mask = count // 2
    while mask >= 1:
        half = total.shape[0] // 2
        lower, upper_part = total[:half], total[half:]
        upper = (index // mask) % 2 == 1
        keep = jnp.where(upper, upper_part, lower)
        send = jnp.where(upper, lower, upper_part)
        got = swapped(send.astype(wire_type), axis, mask)
        total = keep + got.astype(jnp.float32)
        mask //= 2
    return total


def aggregate_kernel(core_ref, where_ref, count_ref, tiles_ref, proj_ref, out_ref, picked_ref):
    row = pl.program_id(0)
    half_id = pl.program_id(1)
    tile_rows = pl.num_programs(0)
    tile_size = proj_ref.shape[1]
    slot_count = tiles_ref.shape[1] // tile_size
    base = (half_id * 2 + core_ref[0]) * tile_rows + row
    live = count_ref[base]
    for slot in range(slot_count):
        piece = proj_ref[where_ref[base * slot_count + slot]]
        picked_ref[slot * tile_size:(slot + 1) * tile_size, :] = jnp.where(
            slot < live, piece, jnp.zeros_like(piece)
        )
    part = jnp.dot(tiles_ref[...], picked_ref[...], preferred_element_type=jnp.float32)

    @pl.when(half_id == 0)
    def _():
        out_ref[...] = part

    @pl.when(half_id != 0)
    def _():
        out_ref[...] += part


def aggregate_pair(core_id, spots, counts, tiles_wide, buffer):
    blocks, tile_rows, tile_size, wide = tiles_wide.shape
    hidden_width = buffer.shape[-1]
    grid_spec = pltpu.PrefetchScalarGridSpec(
        num_scalar_prefetch=3,
        grid=(tile_rows, blocks // 2),
        in_specs=[
            pl.BlockSpec((None, None, tile_size, wide), lambda r, h, c, w, n: (h * 2 + c[0], r, 0, 0)),
            pl.BlockSpec(buffer.shape, lambda r, h, c, w, n: (0, 0, 0)),
        ],
        out_specs=pl.BlockSpec((None, tile_size, hidden_width), lambda r, h, c, w, n: (r, 0, 0)),
        scratch_shapes=[pltpu.VMEM((wide, hidden_width), buffer.dtype)],
    )
    return pl.pallas_call(
        aggregate_kernel,
        grid_spec=grid_spec,
        out_shape=jax.ShapeDtypeStruct((tile_rows, tile_size, hidden_width), jnp.float32),
        compiler_params=pltpu.CompilerParams(dimension_semantics=("arbitrary", "arbitrary")),
    )(jnp.reshape(core_id, (1,)).astype(jnp.int32), spots, counts, tiles_wide, buffer)


def spread_kernel(core_ref, where_ref, count_ref, tiles_ref, grad_ref, out_ref, total_ref, terms_ref):
    row = pl.program_id(0)
    half_id = pl.program_id(1)
    tile_rows = pl.num_programs(0)
    halves = pl.num_programs(1)
    tile_size = grad_ref.shape[0]
    slot_count = tiles_ref.shape[0] // tile_size
    base = (half_id * 2 + core_ref[0]) * tile_rows + row
    live = count_ref[base]

    @pl.when((row == 0) & (half_id == 0))
    def _():
        total_ref[...] = jnp.zeros(total_ref.shape, jnp.float32)

    terms_ref[...] = jnp.dot(tiles_ref[...], grad_ref[...], preferred_element_type=jnp.float32)

    def step(slot, carry):
        spot = where_ref[base * slot_count + slot]
        start = pl.multiple_of(slot * tile_size, tile_size)
        total_ref[spot] += terms_ref[pl.ds(start, tile_size), :]
        return carry

    lax.fori_loop(0, live, step, 0)

    @pl.when((row == tile_rows - 1) & (half_id == halves - 1))
    def _():
        out_ref[...] = total_ref[...].astype(out_ref.dtype)


def spread_pair(core_id, spots, counts, tiles_tall, grad_tiles, buffer_tiles, out_type):
    blocks, tile_rows, tall, tile_size = tiles_tall.shape
    hidden_width = grad_tiles.shape[-1]
    grid_spec = pltpu.PrefetchScalarGridSpec(
        num_scalar_prefetch=3,
        grid=(tile_rows, blocks // 2),
        in_specs=[
            pl.BlockSpec((None, None, tall, tile_size), lambda r, h, c, w, n: (h * 2 + c[0], r, 0, 0)),
            pl.BlockSpec((None, tile_size, hidden_width), lambda r, h, c, w, n: (r, 0, 0)),
        ],
        out_specs=pl.BlockSpec(
            (buffer_tiles, tile_size, hidden_width), lambda r, h, c, w, n: (0, 0, 0)
        ),
        scratch_shapes=[
            pltpu.VMEM((buffer_tiles, tile_size, hidden_width), jnp.float32),
            pltpu.VMEM((tall, hidden_width), jnp.float32),
        ],
    )
    return pl.pallas_call(
        spread_kernel,
        grid_spec=grid_spec,
        out_shape=jax.ShapeDtypeStruct((buffer_tiles, tile_size, hidden_width), out_type),
        compiler_params=pltpu.CompilerParams(dimension_semantics=("arbitrary", "arbitrary")),
    )(jnp.reshape(core_id, (1,)).astype(jnp.int32), spots, counts, tiles_tall, grad_tiles)


def buffer_spots(tile_col, blk_id, feat_id, block_tiles, tiles_per_device):
    own = place_of(blk_id, feat_id)
    block = tile_col // block_tiles
    local = tile_col % block_tiles
    source_feat = local // tiles_per_device
    part = local % tiles_per_device
    source = place_of(block, source_feat)
    rel = {axis: (source[axis] - own[axis]) % RING for axis in ("y", "z", "x")}
    chunk = jnp.where(
        source["core"] == 0,
        rel["y"] * 16 + rel["z"] * 4 + rel["x"],
        rel["x"] * 16 + rel["z"] * 4 + rel["y"],
    )
    return (chunk * tiles_per_device + part).astype(jnp.int32)


def body(features_t, weight, tile_values, tile_col, tile_count, grad_out):
    cycle_size = lax.axis_size("blk")
    hidden_width = weight.shape[1]
    tile_size = tile_values.shape[1]
    rows_own = grad_out.shape[0]
    tile_rows = rows_own // tile_size
    block_rows = features_t.shape[1]
    block_tiles = block_rows // tile_size
    slot_count = tile_values.shape[0] // (cycle_size * tile_rows)
    feat_id = lax.axis_index("feat")
    blk_id = lax.axis_index("blk")
    core_id = blk_id % 2
    tile_stack = tile_values.reshape(cycle_size, tile_rows, slot_count, tile_size, tile_size)
    tiles_wide = tile_stack.transpose(0, 1, 3, 2, 4).reshape(
        cycle_size, tile_rows, tile_size, slot_count * tile_size
    )
    tiles_tall = tile_stack.transpose(0, 1, 2, 4, 3).reshape(
        cycle_size, tile_rows, slot_count * tile_size, tile_size
    )
    spots = buffer_spots(tile_col, blk_id, feat_id, block_tiles, tile_rows)
    buffer_tiles = block_tiles * 2

    features_own = lax.all_to_all(features_t, "feat", split_axis=1, concat_axis=0, tiled=True)
    projected = lax.dot_general(
        features_own, weight, (((0,), (0,)), ((), ())), preferred_element_type=jnp.float32
    ).astype(jnp.bfloat16)

    gathered = projected
    for phase in range(3):
        gathered = gather_phase(gathered, phase)
    own_buffer = gathered.reshape(buffer_tiles, tile_size, hidden_width)
    other_buffer = sibling(own_buffer)
    aggregate_sum = aggregate_pair(core_id, spots, tile_count, tiles_wide, own_buffer)
    aggregate_sum = aggregate_sum + aggregate_pair(
        1 - core_id, spots, tile_count, tiles_wide, other_buffer
    )

    pre_act = aggregate_sum.reshape(rows_own, hidden_width)
    sigmoid_y = jax.nn.sigmoid(pre_act)
    activations = (pre_act * sigmoid_y).astype(jnp.bfloat16)
    grad_pre = (
        grad_out.astype(jnp.float32) * sigmoid_y * (1.0 + pre_act * (1.0 - sigmoid_y))
    ).astype(jnp.bfloat16)
    grad_tiles = grad_pre.reshape(tile_rows, tile_size, hidden_width)

    outgoing = spread_pair(
        1 - core_id, spots, tile_count, tiles_tall, grad_tiles, buffer_tiles, jnp.bfloat16
    )
    arrived = sibling(outgoing)
    total = spread_pair(
        core_id, spots, tile_count, tiles_tall, grad_tiles, buffer_tiles, jnp.float32
    )
    total = total + arrived.astype(jnp.float32)
    total = total.reshape(RING, RING, RING, rows_own, hidden_width)
    for phase in (2, 1, 0):
        total = reduce_phase(total, phase, jnp.bfloat16)
    grad_hidden = total.astype(jnp.bfloat16)

    weight_term = jnp.dot(features_own, grad_hidden, preferred_element_type=jnp.float32)
    weight_part = scatter_rows(weight_term, "feat", jnp.float32)
    weight_part = weight_part + swapped(weight_part, "blk", 1)
    weight_part = weight_part + swapped(weight_part, "blk", 2)
    grad_weight = weight_part * lax.rsqrt(jnp.float32(block_rows * cycle_size))

    features_grad_local = lax.dot_general(
        weight, grad_hidden, (((1,), (1,)), ((), ())), preferred_element_type=jnp.float32
    ).astype(jnp.bfloat16)
    grad_features = lax.all_to_all(
        features_grad_local, "feat", split_axis=0, concat_axis=1, tiled=True
    )
    return (activations, grad_features, grad_weight)


def solution(mesh):
    placed = (
        P("feat", "blk"),
        P(),
        P(("blk", "feat"), None, None),
        P(("blk", "feat")),
        P(("blk", "feat")),
        P(("blk", "feat"), None),
    )
    return jax.shard_map(
        body,
        mesh=mesh,
        in_specs=placed,
        out_specs=(P(("blk", "feat"), None), P("feat", "blk"), P("feat", None)),
        check_vma=False,
    )
```

```python
import jax
import jax.numpy as jnp
from jax import lax
from jax.sharding import PartitionSpec as P
from jax.experimental import pallas as pl
from jax.experimental.pallas import tpu as pltpu

RING = 4
GATHER_ORDER = (("x", "z", "y"), ("y", "z", "x"))
BOTH = ("blk", "feat")


def place_of(blk, feat):
    return {
        "core": blk % 2,
        "y": (blk // 2) * 2 + feat // 16,
        "z": (feat // 4) % 4,
        "x": feat % 4,
    }


def linear_of(place):
    blk = (place["y"] // 2) * 2 + place["core"]
    feat = (place["y"] % 2) * 16 + place["z"] * 4 + place["x"]
    return blk * 32 + feat


def ring_shift(block, phase, distance):
    route = []
    for blk in range(4):
        for feat in range(32):
            place = place_of(blk, feat)
            axis = GATHER_ORDER[place["core"]][phase]
            target = dict(place)
            target[axis] = (place[axis] + distance) % RING
            route.append((linear_of(place), linear_of(target)))
    return lax.ppermute(block, BOTH, route)


def sibling(block):
    return lax.ppermute(block, "blk", [(i, i ^ 1) for i in range(lax.axis_size("blk"))])


def swapped(block, axis, mask):
    count = lax.axis_size(axis)
    return lax.ppermute(block, axis, [(i, i ^ mask) for i in range(count)])


def gather_phase(block, phase):
    half = block.shape[-2] // 2
    from_minus = ring_shift(block, phase, 1)
    from_plus = ring_shift(block, phase, -1)
    far_low = ring_shift(from_minus[..., :half, :], phase, 1)
    far_high = ring_shift(from_plus[..., half:, :], phase, -1)
    far = jnp.concatenate([far_low, far_high], axis=-2)
    return jnp.stack([block, from_plus, far, from_minus])


def reduce_phase(total, phase, wire_type):
    half = total.shape[-2] // 2
    far = total[2]
    got_minus = ring_shift(far[..., :half, :].astype(wire_type), phase, 1)
    got_plus = ring_shift(far[..., half:, :].astype(wire_type), phase, -1)
    ahead = total[1]
    ahead = jnp.concatenate(
        [ahead[..., :half, :] + got_minus.astype(jnp.float32), ahead[..., half:, :]], axis=-2
    )
    behind = total[3]
    behind = jnp.concatenate(
        [behind[..., :half, :], behind[..., half:, :] + got_plus.astype(jnp.float32)], axis=-2
    )
    from_minus = ring_shift(ahead.astype(wire_type), phase, 1)
    from_plus = ring_shift(behind.astype(wire_type), phase, -1)
    return total[0] + from_minus.astype(jnp.float32) + from_plus.astype(jnp.float32)


def scatter_rows(total, axis, wire_type):
    count = lax.axis_size(axis)
    index = lax.axis_index(axis)
    mask = count // 2
    while mask >= 1:
        half = total.shape[0] // 2
        lower, upper_part = total[:half], total[half:]
        upper = (index // mask) % 2 == 1
        keep = jnp.where(upper, upper_part, lower)
        send = jnp.where(upper, lower, upper_part)
        got = swapped(send.astype(wire_type), axis, mask)
        total = keep + got.astype(jnp.float32)
        mask //= 2
    return total


def aggregate_kernel(core_ref, where_ref, count_ref, tiles_ref, proj_ref, out_ref, wide_ref, picked_ref):
    row = pl.program_id(0)
    half_id = pl.program_id(1)
    tile_rows = pl.num_programs(0)
    slot_count, tile_size, _ = tiles_ref.shape
    base = (half_id * 2 + core_ref[0]) * tile_rows + row
    live = count_ref[base]
    for slot in range(slot_count):
        wide_ref[:, slot * tile_size:(slot + 1) * tile_size] = tiles_ref[slot]
        piece = proj_ref[where_ref[base * slot_count + slot]]
        picked_ref[slot * tile_size:(slot + 1) * tile_size, :] = jnp.where(
            slot < live, piece, jnp.zeros_like(piece)
        )
    part = jnp.dot(wide_ref[...], picked_ref[...], preferred_element_type=jnp.float32)

    @pl.when(half_id == 0)
    def _():
        out_ref[...] = part

    @pl.when(half_id != 0)
    def _():
        out_ref[...] += part


def aggregate_pair(core_id, spots, counts, tile_stack, buffer):
    blocks, tile_rows, slot_count, tile_size, _ = tile_stack.shape
    hidden_width = buffer.shape[-1]
    grid_spec = pltpu.PrefetchScalarGridSpec(
        num_scalar_prefetch=3,
        grid=(tile_rows, blocks // 2),
        in_specs=[
            pl.BlockSpec(
                (None, None, slot_count, tile_size, tile_size),
                lambda r, h, c, w, n: (h * 2 + c[0], r, 0, 0, 0),
            ),
            pl.BlockSpec(buffer.shape, lambda r, h, c, w, n: (0, 0, 0)),
        ],
        out_specs=pl.BlockSpec((None, tile_size, hidden_width), lambda r, h, c, w, n: (r, 0, 0)),
        scratch_shapes=[
            pltpu.VMEM((tile_size, slot_count * tile_size), tile_stack.dtype),
            pltpu.VMEM((slot_count * tile_size, hidden_width), buffer.dtype),
        ],
    )
    return pl.pallas_call(
        aggregate_kernel,
        grid_spec=grid_spec,
        out_shape=jax.ShapeDtypeStruct((tile_rows, tile_size, hidden_width), jnp.float32),
        compiler_params=pltpu.CompilerParams(dimension_semantics=("arbitrary", "arbitrary")),
    )(jnp.reshape(core_id, (1,)).astype(jnp.int32), spots, counts, tile_stack, buffer)


def spread_kernel(
    core_ref, where_ref, count_ref, tiles_ref, grad_ref, out_ref, total_ref, wide_ref, terms_ref
):
    row = pl.program_id(0)
    half_id = pl.program_id(1)
    tile_rows = pl.num_programs(0)
    halves = pl.num_programs(1)
    slot_count, tile_size, _ = tiles_ref.shape
    base = (half_id * 2 + core_ref[0]) * tile_rows + row
    live = count_ref[base]

    @pl.when((row == 0) & (half_id == 0))
    def _():
        total_ref[...] = jnp.zeros(total_ref.shape, jnp.float32)

    for slot in range(slot_count):
        wide_ref[:, slot * tile_size:(slot + 1) * tile_size] = tiles_ref[slot]
    terms_ref[...] = jnp.dot(grad_ref[...], wide_ref[...], preferred_element_type=jnp.float32)
    for slot in range(slot_count):
        spot = where_ref[base * slot_count + slot]

        @pl.when(slot < live)
        def _():
            total_ref[spot] += terms_ref[:, slot * tile_size:(slot + 1) * tile_size]

    @pl.when((row == tile_rows - 1) & (half_id == halves - 1))
    def _():
        out_ref[...] = total_ref[...].astype(out_ref.dtype)


def spread_pair(core_id, spots, counts, tile_stack, grad_turned, buffer_tiles, out_type):
    blocks, tile_rows, slot_count, tile_size, _ = tile_stack.shape
    hidden_width = grad_turned.shape[1]
    grid_spec = pltpu.PrefetchScalarGridSpec(
        num_scalar_prefetch=3,
        grid=(tile_rows, blocks // 2),
        in_specs=[
            pl.BlockSpec(
                (None, None, slot_count, tile_size, tile_size),
                lambda r, h, c, w, n: (h * 2 + c[0], r, 0, 0, 0),
            ),
            pl.BlockSpec((None, hidden_width, tile_size), lambda r, h, c, w, n: (r, 0, 0)),
        ],
        out_specs=pl.BlockSpec(
            (buffer_tiles, hidden_width, tile_size), lambda r, h, c, w, n: (0, 0, 0)
        ),
        scratch_shapes=[
            pltpu.VMEM((buffer_tiles, hidden_width, tile_size), jnp.float32),
            pltpu.VMEM((tile_size, slot_count * tile_size), tile_stack.dtype),
            pltpu.VMEM((hidden_width, slot_count * tile_size), jnp.float32),
        ],
    )
    return pl.pallas_call(
        spread_kernel,
        grid_spec=grid_spec,
        out_shape=jax.ShapeDtypeStruct((buffer_tiles, hidden_width, tile_size), out_type),
        compiler_params=pltpu.CompilerParams(dimension_semantics=("arbitrary", "arbitrary")),
    )(jnp.reshape(core_id, (1,)).astype(jnp.int32), spots, counts, tile_stack, grad_turned)


def buffer_spots(tile_col, blk_id, feat_id, block_tiles, tiles_per_device):
    own = place_of(blk_id, feat_id)
    block = tile_col // block_tiles
    local = tile_col % block_tiles
    source_feat = local // tiles_per_device
    part = local % tiles_per_device
    source = place_of(block, source_feat)
    rel = {axis: (source[axis] - own[axis]) % RING for axis in ("y", "z", "x")}
    chunk = jnp.where(
        source["core"] == 0,
        rel["y"] * 16 + rel["z"] * 4 + rel["x"],
        rel["x"] * 16 + rel["z"] * 4 + rel["y"],
    )
    return (chunk * tiles_per_device + part).astype(jnp.int32)


def body(features_t, weight, tile_values, tile_col, tile_count, grad_out):
    cycle_size = lax.axis_size("blk")
    hidden_width = weight.shape[1]
    tile_size = tile_values.shape[1]
    rows_own = grad_out.shape[0]
    tile_rows = rows_own // tile_size
    block_rows = features_t.shape[1]
    block_tiles = block_rows // tile_size
    slot_count = tile_values.shape[0] // (cycle_size * tile_rows)
    feat_id = lax.axis_index("feat")
    blk_id = lax.axis_index("blk")
    core_id = blk_id % 2
    tile_stack = tile_values.reshape(cycle_size, tile_rows, slot_count, tile_size, tile_size)
    spots = buffer_spots(tile_col, blk_id, feat_id, block_tiles, tile_rows)
    buffer_tiles = block_tiles * 2

    features_own = lax.all_to_all(features_t, "feat", split_axis=1, concat_axis=0, tiled=True)
    projected = lax.dot_general(
        features_own, weight, (((0,), (0,)), ((), ())), preferred_element_type=jnp.float32
    ).astype(jnp.bfloat16)

    gathered = projected
    for phase in range(3):
        gathered = gather_phase(gathered, phase)
    own_buffer = gathered.reshape(buffer_tiles, tile_size, hidden_width)
    other_buffer = sibling(own_buffer)
    aggregate_sum = aggregate_pair(core_id, spots, tile_count, tile_stack, own_buffer)
    aggregate_sum = aggregate_sum + aggregate_pair(
        1 - core_id, spots, tile_count, tile_stack, other_buffer
    )

    pre_act = aggregate_sum.reshape(rows_own, hidden_width)
    sigmoid_y = jax.nn.sigmoid(pre_act)
    activations = (pre_act * sigmoid_y).astype(jnp.bfloat16)
    grad_pre = (
        grad_out.astype(jnp.float32) * sigmoid_y * (1.0 + pre_act * (1.0 - sigmoid_y))
    ).astype(jnp.bfloat16)
    grad_turned = grad_pre.reshape(tile_rows, tile_size, hidden_width).transpose(0, 2, 1)

    outgoing = spread_pair(
        1 - core_id, spots, tile_count, tile_stack, grad_turned, buffer_tiles, jnp.bfloat16
    )
    arrived = sibling(outgoing)
    total = spread_pair(
        core_id, spots, tile_count, tile_stack, grad_turned, buffer_tiles, jnp.float32
    )
    total = total + arrived.astype(jnp.float32)
    total = total.reshape(RING, RING, RING, rows_own, hidden_width)
    for phase in (2, 1, 0):
        total = reduce_phase(total, phase, jnp.bfloat16)
    grad_hidden = (
        total.reshape(tile_rows, hidden_width, tile_size)
        .transpose(0, 2, 1)
        .reshape(rows_own, hidden_width)
        .astype(jnp.bfloat16)
    )

    weight_term = jnp.dot(features_own, grad_hidden, preferred_element_type=jnp.float32)
    weight_part = scatter_rows(weight_term, "feat", jnp.float32)
    weight_part = weight_part + swapped(weight_part, "blk", 1)
    weight_part = weight_part + swapped(weight_part, "blk", 2)
    grad_weight = weight_part * lax.rsqrt(jnp.float32(block_rows * cycle_size))

    features_grad_local = lax.dot_general(
        weight, grad_hidden, (((1,), (1,)), ((), ())), preferred_element_type=jnp.float32
    ).astype(jnp.bfloat16)
    grad_features = lax.all_to_all(
        features_grad_local, "feat", split_axis=0, concat_axis=1, tiled=True
    )
    return (activations, grad_features, grad_weight)


def solution(mesh):
    placed = (
        P("feat", "blk"),
        P(),
        P(("blk", "feat"), None, None),
        P(("blk", "feat")),
        P(("blk", "feat")),
        P(("blk", "feat"), None),
    )
    return jax.shard_map(
        body,
        mesh=mesh,
        in_specs=placed,
        out_specs=(P(("blk", "feat"), None), P("feat", "blk"), P("feat", None)),
        check_vma=False,
    )
```

```python
import jax
import jax.numpy as jnp
from jax import lax
from jax.sharding import PartitionSpec as P
from jax.experimental import pallas as pl
from jax.experimental.pallas import tpu as pltpu

RING = 4
GATHER_ORDER = (("x", "z", "y"), ("y", "z", "x"))
BOTH = ("blk", "feat")


def place_of(blk, feat):
    return {
        "core": blk % 2,
        "y": (blk // 2) * 2 + feat // 16,
        "z": (feat // 4) % 4,
        "x": feat % 4,
    }


def linear_of(place):
    blk = (place["y"] // 2) * 2 + place["core"]
    feat = (place["y"] % 2) * 16 + place["z"] * 4 + place["x"]
    return blk * 32 + feat


def ring_shift(block, phase, distance):
    route = []
    for blk in range(4):
        for feat in range(32):
            place = place_of(blk, feat)
            axis = GATHER_ORDER[place["core"]][phase]
            target = dict(place)
            target[axis] = (place[axis] + distance) % RING
            route.append((linear_of(place), linear_of(target)))
    return lax.ppermute(block, BOTH, route)


def sibling(block):
    return lax.ppermute(block, "blk", [(i, i ^ 1) for i in range(lax.axis_size("blk"))])


def swapped(block, axis, mask):
    count = lax.axis_size(axis)
    return lax.ppermute(block, axis, [(i, i ^ mask) for i in range(count)])


def gather_phase(block, phase):
    half = block.shape[-2] // 2
    from_minus = ring_shift(block, phase, 1)
    from_plus = ring_shift(block, phase, -1)
    far_low = ring_shift(from_minus[..., :half, :], phase, 1)
    far_high = ring_shift(from_plus[..., half:, :], phase, -1)
    far = jnp.concatenate([far_low, far_high], axis=-2)
    return jnp.stack([block, from_plus, far, from_minus])


def gather_phase_direct(block, phase):
    from_minus = ring_shift(block, phase, 1)
    from_plus = ring_shift(block, phase, -1)
    far = ring_shift(block, phase, 2)
    return jnp.stack([block, from_plus, far, from_minus])


def reduce_phase_direct(total, phase, wire_type):
    from_minus = ring_shift(total[1].astype(wire_type), phase, 1)
    from_plus = ring_shift(total[3].astype(wire_type), phase, -1)
    far = ring_shift(total[2].astype(wire_type), phase, 2)
    return (
        total[0]
        + from_minus.astype(jnp.float32)
        + from_plus.astype(jnp.float32)
        + far.astype(jnp.float32)
    )


def reduce_phase(total, phase, wire_type, extra=None):
    half = total.shape[-2] // 2

    def term(k):
        if extra is None:
            return total[k]
        return total[k] + extra[k].astype(jnp.float32)

    far = term(2)
    got_minus = ring_shift(far[..., :half, :].astype(wire_type), phase, 1)
    got_plus = ring_shift(far[..., half:, :].astype(wire_type), phase, -1)
    ahead = term(1)
    ahead = jnp.concatenate(
        [ahead[..., :half, :] + got_minus.astype(jnp.float32), ahead[..., half:, :]], axis=-2
    )
    behind = term(3)
    behind = jnp.concatenate(
        [behind[..., :half, :], behind[..., half:, :] + got_plus.astype(jnp.float32)], axis=-2
    )
    from_minus = ring_shift(ahead.astype(wire_type), phase, 1)
    from_plus = ring_shift(behind.astype(wire_type), phase, -1)
    return term(0) + from_minus.astype(jnp.float32) + from_plus.astype(jnp.float32)


def scatter_rows(total, axis, wire_type):
    count = lax.axis_size(axis)
    index = lax.axis_index(axis)
    mask = count // 2
    while mask >= 1:
        half = total.shape[0] // 2
        lower, upper_part = total[:half], total[half:]
        upper = (index // mask) % 2 == 1
        keep = jnp.where(upper, upper_part, lower)
        send = jnp.where(upper, lower, upper_part)
        got = swapped(send.astype(wire_type), axis, mask)
        total = keep + got.astype(jnp.float32)
        mask //= 2
    return total


def aggregate_kernel(core_ref, where_ref, count_ref, tiles_ref, proj_ref, out_ref, wide_ref, picked_ref):
    row = pl.program_id(0)
    half_id = pl.program_id(1)
    tile_rows = pl.num_programs(0)
    slot_count, tile_size, _ = tiles_ref.shape
    base = (half_id * 2 + core_ref[0]) * tile_rows + row
    live = count_ref[base]
    for slot in range(slot_count):
        wide_ref[:, slot * tile_size:(slot + 1) * tile_size] = tiles_ref[slot]
        piece = proj_ref[where_ref[base * slot_count + slot]]
        picked_ref[slot * tile_size:(slot + 1) * tile_size, :] = jnp.where(
            slot < live, piece, jnp.zeros_like(piece)
        )
    part = jnp.dot(wide_ref[...], picked_ref[...], preferred_element_type=jnp.float32)

    @pl.when(half_id == 0)
    def _():
        out_ref[...] = part

    @pl.when(half_id != 0)
    def _():
        out_ref[...] += part


def aggregate_pair(core_id, spots, counts, tile_stack, buffer):
    blocks, tile_rows, slot_count, tile_size, _ = tile_stack.shape
    hidden_width = buffer.shape[-1]
    grid_spec = pltpu.PrefetchScalarGridSpec(
        num_scalar_prefetch=3,
        grid=(tile_rows, blocks // 2),
        in_specs=[
            pl.BlockSpec(
                (None, None, slot_count, tile_size, tile_size),
                lambda r, h, c, w, n: (h * 2 + c[0], r, 0, 0, 0),
            ),
            pl.BlockSpec(buffer.shape, lambda r, h, c, w, n: (0, 0, 0)),
        ],
        out_specs=pl.BlockSpec((None, tile_size, hidden_width), lambda r, h, c, w, n: (r, 0, 0)),
        scratch_shapes=[
            pltpu.VMEM((tile_size, slot_count * tile_size), tile_stack.dtype),
            pltpu.VMEM((slot_count * tile_size, hidden_width), buffer.dtype),
        ],
    )
    return pl.pallas_call(
        aggregate_kernel,
        grid_spec=grid_spec,
        out_shape=jax.ShapeDtypeStruct((tile_rows, tile_size, hidden_width), jnp.float32),
        compiler_params=pltpu.CompilerParams(dimension_semantics=("arbitrary", "arbitrary")),
    )(jnp.reshape(core_id, (1,)).astype(jnp.int32), spots, counts, tile_stack, buffer)


def spread_kernel(
    core_ref, where_ref, count_ref, tiles_ref, grad_ref, out_ref, total_ref, wide_ref, terms_ref
):
    row = pl.program_id(0)
    half_id = pl.program_id(1)
    tile_rows = pl.num_programs(0)
    halves = pl.num_programs(1)
    slot_count, tile_size, _ = tiles_ref.shape
    base = (half_id * 2 + core_ref[0]) * tile_rows + row
    live = count_ref[base]

    @pl.when((row == 0) & (half_id == 0))
    def _():
        total_ref[...] = jnp.zeros(total_ref.shape, jnp.float32)

    for slot in range(slot_count):
        wide_ref[:, slot * tile_size:(slot + 1) * tile_size] = tiles_ref[slot]
    terms_ref[...] = jnp.dot(grad_ref[...], wide_ref[...], preferred_element_type=jnp.float32)
    for slot in range(slot_count):
        spot = where_ref[base * slot_count + slot]

        @pl.when(slot < live)
        def _():
            total_ref[spot] += terms_ref[:, slot * tile_size:(slot + 1) * tile_size]

    @pl.when((row == tile_rows - 1) & (half_id == halves - 1))
    def _():
        out_ref[...] = total_ref[...].astype(out_ref.dtype)


def spread_pair(core_id, spots, counts, tile_stack, grad_turned, buffer_tiles, out_type):
    blocks, tile_rows, slot_count, tile_size, _ = tile_stack.shape
    hidden_width = grad_turned.shape[1]
    grid_spec = pltpu.PrefetchScalarGridSpec(
        num_scalar_prefetch=3,
        grid=(tile_rows, blocks // 2),
        in_specs=[
            pl.BlockSpec(
                (None, None, slot_count, tile_size, tile_size),
                lambda r, h, c, w, n: (h * 2 + c[0], r, 0, 0, 0),
            ),
            pl.BlockSpec((None, hidden_width, tile_size), lambda r, h, c, w, n: (r, 0, 0)),
        ],
        out_specs=pl.BlockSpec(
            (buffer_tiles, hidden_width, tile_size), lambda r, h, c, w, n: (0, 0, 0)
        ),
        scratch_shapes=[
            pltpu.VMEM((buffer_tiles, hidden_width, tile_size), jnp.float32),
            pltpu.VMEM((tile_size, slot_count * tile_size), tile_stack.dtype),
            pltpu.VMEM((hidden_width, slot_count * tile_size), jnp.float32),
        ],
    )
    return pl.pallas_call(
        spread_kernel,
        grid_spec=grid_spec,
        out_shape=jax.ShapeDtypeStruct((buffer_tiles, hidden_width, tile_size), out_type),
        compiler_params=pltpu.CompilerParams(dimension_semantics=("arbitrary", "arbitrary")),
    )(jnp.reshape(core_id, (1,)).astype(jnp.int32), spots, counts, tile_stack, grad_turned)


def buffer_spots(tile_col, blk_id, feat_id, block_tiles, tiles_per_device):
    own = place_of(blk_id, feat_id)
    block = tile_col // block_tiles
    local = tile_col % block_tiles
    source_feat = local // tiles_per_device
    part = local % tiles_per_device
    source = place_of(block, source_feat)
    rel = {axis: (source[axis] - own[axis]) % RING for axis in ("y", "z", "x")}
    chunk = jnp.where(
        source["core"] == 0,
        rel["y"] * 16 + rel["z"] * 4 + rel["x"],
        rel["x"] * 16 + rel["z"] * 4 + rel["y"],
    )
    return (chunk * tiles_per_device + part).astype(jnp.int32)


def body(features_t, weight, tile_values, tile_col, tile_count, grad_out):
    cycle_size = lax.axis_size("blk")
    hidden_width = weight.shape[1]
    tile_size = tile_values.shape[1]
    rows_own = grad_out.shape[0]
    tile_rows = rows_own // tile_size
    block_rows = features_t.shape[1]
    block_tiles = block_rows // tile_size
    slot_count = tile_values.shape[0] // (cycle_size * tile_rows)
    feat_id = lax.axis_index("feat")
    blk_id = lax.axis_index("blk")
    core_id = blk_id % 2
    tile_stack = tile_values.reshape(cycle_size, tile_rows, slot_count, tile_size, tile_size)
    spots = buffer_spots(tile_col, blk_id, feat_id, block_tiles, tile_rows)
    buffer_tiles = block_tiles * 2

    features_own = lax.all_to_all(features_t, "feat", split_axis=1, concat_axis=0, tiled=True)
    projected = lax.dot_general(
        features_own, weight, (((0,), (0,)), ((), ())), preferred_element_type=jnp.float32
    ).astype(jnp.bfloat16)

    gathered = gather_phase_direct(projected, 0)
    gathered = gather_phase_direct(gathered, 1)
    gathered = gather_phase(gathered, 2)
    own_buffer = gathered.reshape(buffer_tiles, tile_size, hidden_width)
    other_buffer = sibling(own_buffer)
    aggregate_sum = aggregate_pair(core_id, spots, tile_count, tile_stack, own_buffer)
    aggregate_sum = aggregate_sum + aggregate_pair(
        1 - core_id, spots, tile_count, tile_stack, other_buffer
    )

    pre_act = aggregate_sum.reshape(rows_own, hidden_width)
    sigmoid_y = jax.nn.sigmoid(pre_act)
    activations = (pre_act * sigmoid_y).astype(jnp.bfloat16)
    grad_pre = (
        grad_out.astype(jnp.float32) * sigmoid_y * (1.0 + pre_act * (1.0 - sigmoid_y))
    ).astype(jnp.bfloat16)
    grad_turned = grad_pre.reshape(tile_rows, tile_size, hidden_width).transpose(0, 2, 1)

    outgoing = spread_pair(
        1 - core_id, spots, tile_count, tile_stack, grad_turned, buffer_tiles, jnp.bfloat16
    )
    arrived = sibling(outgoing)
    total = spread_pair(
        core_id, spots, tile_count, tile_stack, grad_turned, buffer_tiles, jnp.float32
    )
    shape = (RING, RING, RING, rows_own, hidden_width)
    total = reduce_phase(total.reshape(shape), 2, jnp.bfloat16, arrived.reshape(shape))
    total = reduce_phase_direct(total, 1, jnp.bfloat16)
    total = reduce_phase_direct(total, 0, jnp.bfloat16)
    grad_hidden = (
        total.reshape(tile_rows, hidden_width, tile_size)
        .transpose(0, 2, 1)
        .reshape(rows_own, hidden_width)
        .astype(jnp.bfloat16)
    )

    weight_term = jnp.dot(features_own, grad_hidden, preferred_element_type=jnp.float32)
    feat_count = lax.axis_size("feat")
    weight_rows = weight_term.reshape(1, feat_count, -1, hidden_width)
    weight_rows = jnp.broadcast_to(weight_rows, (cycle_size,) + weight_rows.shape[1:])
    weight_rows = weight_rows.reshape(cycle_size * feat_count, -1, hidden_width)
    weight_got = lax.all_to_all(weight_rows, BOTH, split_axis=0, concat_axis=0, tiled=True)
    grad_weight = jnp.sum(weight_got, axis=0) * lax.rsqrt(jnp.float32(block_rows * cycle_size))

    features_grad_local = lax.dot_general(
        weight, grad_hidden, (((1,), (1,)), ((), ())), preferred_element_type=jnp.float32
    ).astype(jnp.bfloat16)
    grad_features = lax.all_to_all(
        features_grad_local, "feat", split_axis=0, concat_axis=1, tiled=True
    )
    return (activations, grad_features, grad_weight)


def solution(mesh):
    placed = (
        P("feat", "blk"),
        P(),
        P(("blk", "feat"), None, None),
        P(("blk", "feat")),
        P(("blk", "feat")),
        P(("blk", "feat"), None),
    )
    return jax.shard_map(
        body,
        mesh=mesh,
        in_specs=placed,
        out_specs=(P(("blk", "feat"), None), P("feat", "blk"), P("feat", None)),
        check_vma=False,
    )
```

```python
import jax
import jax.numpy as jnp
from jax import lax
from jax.sharding import PartitionSpec as P
from jax.experimental import pallas as pl
from jax.experimental.pallas import tpu as pltpu

RING = 4
GATHER_ORDER = (("x", "z", "y"), ("y", "z", "x"))
BOTH = ("blk", "feat")


def place_of(blk, feat):
    return {
        "core": blk % 2,
        "y": (blk // 2) * 2 + feat // 16,
        "z": (feat // 4) % 4,
        "x": feat % 4,
    }


def linear_of(place):
    blk = (place["y"] // 2) * 2 + place["core"]
    feat = (place["y"] % 2) * 16 + place["z"] * 4 + place["x"]
    return blk * 32 + feat


def ring_shift(block, phase, distance):
    route = []
    for blk in range(4):
        for feat in range(32):
            place = place_of(blk, feat)
            axis = GATHER_ORDER[place["core"]][phase]
            target = dict(place)
            target[axis] = (place[axis] + distance) % RING
            route.append((linear_of(place), linear_of(target)))
    return lax.ppermute(block, BOTH, route)


def sibling(block):
    return lax.ppermute(block, "blk", [(i, i ^ 1) for i in range(lax.axis_size("blk"))])


def swapped(block, axis, mask):
    count = lax.axis_size(axis)
    return lax.ppermute(block, axis, [(i, i ^ mask) for i in range(count)])


def gather_phase(block, phase):
    half = block.shape[-2] // 2
    from_minus = ring_shift(block, phase, 1)
    from_plus = ring_shift(block, phase, -1)
    far_low = ring_shift(from_minus[..., :half, :], phase, 1)
    far_high = ring_shift(from_plus[..., half:, :], phase, -1)
    far = jnp.concatenate([far_low, far_high], axis=-2)
    return jnp.stack([block, from_plus, far, from_minus])


def gather_phase_direct(block, phase):
    from_minus = ring_shift(block, phase, 1)
    from_plus = ring_shift(block, phase, -1)
    far = ring_shift(block, phase, 2)
    return jnp.stack([block, from_plus, far, from_minus])


def reduce_phase_direct(total, phase, wire_type):
    from_minus = ring_shift(total[1].astype(wire_type), phase, 1)
    from_plus = ring_shift(total[3].astype(wire_type), phase, -1)
    far = ring_shift(total[2].astype(wire_type), phase, 2)
    return (
        total[0]
        + from_minus.astype(jnp.float32)
        + from_plus.astype(jnp.float32)
        + far.astype(jnp.float32)
    )


def reduce_phase(total, phase, wire_type, extra=None):
    half = total.shape[-2] // 2

    def term(k):
        if extra is None:
            return total[k]
        return total[k] + extra[k].astype(jnp.float32)

    far = term(2)
    got_minus = ring_shift(far[..., :half, :].astype(wire_type), phase, 1)
    got_plus = ring_shift(far[..., half:, :].astype(wire_type), phase, -1)
    ahead = term(1)
    ahead = jnp.concatenate(
        [ahead[..., :half, :] + got_minus.astype(jnp.float32), ahead[..., half:, :]], axis=-2
    )
    behind = term(3)
    behind = jnp.concatenate(
        [behind[..., :half, :], behind[..., half:, :] + got_plus.astype(jnp.float32)], axis=-2
    )
    from_minus = ring_shift(ahead.astype(wire_type), phase, 1)
    from_plus = ring_shift(behind.astype(wire_type), phase, -1)
    return term(0) + from_minus.astype(jnp.float32) + from_plus.astype(jnp.float32)


def scatter_rows(total, axis, wire_type):
    count = lax.axis_size(axis)
    index = lax.axis_index(axis)
    mask = count // 2
    while mask >= 1:
        half = total.shape[0] // 2
        lower, upper_part = total[:half], total[half:]
        upper = (index // mask) % 2 == 1
        keep = jnp.where(upper, upper_part, lower)
        send = jnp.where(upper, lower, upper_part)
        got = swapped(send.astype(wire_type), axis, mask)
        total = keep + got.astype(jnp.float32)
        mask //= 2
    return total


def aggregate_kernel(core_ref, where_ref, count_ref, tiles_ref, proj_ref, out_ref, wide_ref, picked_ref):
    row = pl.program_id(0)
    half_id = pl.program_id(1)
    tile_rows = pl.num_programs(0)
    slot_count, tile_size, _ = tiles_ref.shape
    base = (half_id * 2 + core_ref[0]) * tile_rows + row
    live = count_ref[base]
    for slot in range(slot_count):
        wide_ref[:, slot * tile_size:(slot + 1) * tile_size] = tiles_ref[slot]
        piece = proj_ref[where_ref[base * slot_count + slot]]
        picked_ref[slot * tile_size:(slot + 1) * tile_size, :] = jnp.where(
            slot < live, piece, jnp.zeros_like(piece)
        )
    part = jnp.dot(wide_ref[...], picked_ref[...], preferred_element_type=jnp.float32)

    @pl.when(half_id == 0)
    def _():
        out_ref[...] = part

    @pl.when(half_id != 0)
    def _():
        out_ref[...] += part


def aggregate_pair(core_id, spots, counts, tile_stack, buffer):
    blocks, tile_rows, slot_count, tile_size, _ = tile_stack.shape
    hidden_width = buffer.shape[-1]
    grid_spec = pltpu.PrefetchScalarGridSpec(
        num_scalar_prefetch=3,
        grid=(tile_rows, blocks // 2),
        in_specs=[
            pl.BlockSpec(
                (None, None, slot_count, tile_size, tile_size),
                lambda r, h, c, w, n: (h * 2 + c[0], r, 0, 0, 0),
            ),
            pl.BlockSpec(buffer.shape, lambda r, h, c, w, n: (0, 0, 0)),
        ],
        out_specs=pl.BlockSpec((None, tile_size, hidden_width), lambda r, h, c, w, n: (r, 0, 0)),
        scratch_shapes=[
            pltpu.VMEM((tile_size, slot_count * tile_size), tile_stack.dtype),
            pltpu.VMEM((slot_count * tile_size, hidden_width), buffer.dtype),
        ],
    )
    return pl.pallas_call(
        aggregate_kernel,
        grid_spec=grid_spec,
        out_shape=jax.ShapeDtypeStruct((tile_rows, tile_size, hidden_width), jnp.float32),
        compiler_params=pltpu.CompilerParams(dimension_semantics=("arbitrary", "arbitrary")),
    )(jnp.reshape(core_id, (1,)).astype(jnp.int32), spots, counts, tile_stack, buffer)


def spread_kernel(core_ref, where_ref, count_ref, tiles_ref, grad_ref, *rest):
    if len(rest) == 5:
        start_ref, out_ref, total_ref, wide_ref, terms_ref = rest
    else:
        start_ref = None
        out_ref, total_ref, wide_ref, terms_ref = rest
    row = pl.program_id(0)
    half_id = pl.program_id(1)
    tile_rows = pl.num_programs(0)
    halves = pl.num_programs(1)
    slot_count, tile_size, _ = tiles_ref.shape
    base = (half_id * 2 + core_ref[0]) * tile_rows + row
    live = count_ref[base]

    @pl.when((row == 0) & (half_id == 0))
    def _():
        if start_ref is None:
            total_ref[...] = jnp.zeros(total_ref.shape, jnp.float32)
        else:
            total_ref[...] = start_ref[...].astype(jnp.float32)

    for slot in range(slot_count):
        wide_ref[:, slot * tile_size:(slot + 1) * tile_size] = tiles_ref[slot]
    terms_ref[...] = jnp.dot(grad_ref[...], wide_ref[...], preferred_element_type=jnp.float32)
    for slot in range(slot_count):
        spot = where_ref[base * slot_count + slot]

        @pl.when(slot < live)
        def _():
            total_ref[spot] += terms_ref[:, slot * tile_size:(slot + 1) * tile_size]

    @pl.when((row == tile_rows - 1) & (half_id == halves - 1))
    def _():
        out_ref[...] = total_ref[...].astype(out_ref.dtype)


def spread_pair(core_id, spots, counts, tile_stack, grad_turned, buffer_tiles, out_type, start=None):
    blocks, tile_rows, slot_count, tile_size, _ = tile_stack.shape
    hidden_width = grad_turned.shape[1]
    grid_spec = pltpu.PrefetchScalarGridSpec(
        num_scalar_prefetch=3,
        grid=(tile_rows, blocks // 2),
        in_specs=[
            pl.BlockSpec(
                (None, None, slot_count, tile_size, tile_size),
                lambda r, h, c, w, n: (h * 2 + c[0], r, 0, 0, 0),
            ),
            pl.BlockSpec((None, hidden_width, tile_size), lambda r, h, c, w, n: (r, 0, 0)),
        ]
        + ([] if start is None else [pl.BlockSpec(start.shape, lambda r, h, c, w, n: (0, 0, 0))]),
        out_specs=pl.BlockSpec(
            (buffer_tiles, hidden_width, tile_size), lambda r, h, c, w, n: (0, 0, 0)
        ),
        scratch_shapes=[
            pltpu.VMEM((buffer_tiles, hidden_width, tile_size), jnp.float32),
            pltpu.VMEM((tile_size, slot_count * tile_size), tile_stack.dtype),
            pltpu.VMEM((hidden_width, slot_count * tile_size), jnp.float32),
        ],
    )
    return pl.pallas_call(
        spread_kernel,
        grid_spec=grid_spec,
        out_shape=jax.ShapeDtypeStruct((buffer_tiles, hidden_width, tile_size), out_type),
        compiler_params=pltpu.CompilerParams(dimension_semantics=("arbitrary", "arbitrary")),
    )(
        jnp.reshape(core_id, (1,)).astype(jnp.int32),
        spots,
        counts,
        tile_stack,
        grad_turned,
        *([] if start is None else [start]),
    )


def buffer_spots(tile_col, blk_id, feat_id, block_tiles, tiles_per_device):
    own = place_of(blk_id, feat_id)
    block = tile_col // block_tiles
    local = tile_col % block_tiles
    source_feat = local // tiles_per_device
    part = local % tiles_per_device
    source = place_of(block, source_feat)
    rel = {axis: (source[axis] - own[axis]) % RING for axis in ("y", "z", "x")}
    chunk = jnp.where(
        source["core"] == 0,
        rel["y"] * 16 + rel["z"] * 4 + rel["x"],
        rel["x"] * 16 + rel["z"] * 4 + rel["y"],
    )
    return (chunk * tiles_per_device + part).astype(jnp.int32)


def body(features_t, weight, tile_values, tile_col, tile_count, grad_out):
    cycle_size = lax.axis_size("blk")
    hidden_width = weight.shape[1]
    tile_size = tile_values.shape[1]
    rows_own = grad_out.shape[0]
    tile_rows = rows_own // tile_size
    block_rows = features_t.shape[1]
    block_tiles = block_rows // tile_size
    slot_count = tile_values.shape[0] // (cycle_size * tile_rows)
    feat_id = lax.axis_index("feat")
    blk_id = lax.axis_index("blk")
    core_id = blk_id % 2
    tile_stack = tile_values.reshape(cycle_size, tile_rows, slot_count, tile_size, tile_size)
    spots = buffer_spots(tile_col, blk_id, feat_id, block_tiles, tile_rows)
    buffer_tiles = block_tiles * 2

    features_own = lax.all_to_all(features_t, "feat", split_axis=1, concat_axis=0, tiled=True)
    projected = lax.dot_general(
        features_own, weight, (((0,), (0,)), ((), ())), preferred_element_type=jnp.float32
    ).astype(jnp.bfloat16)

    gathered = gather_phase_direct(projected, 0)
    gathered = gather_phase_direct(gathered, 1)
    gathered = gather_phase(gathered, 2)
    own_buffer = gathered.reshape(buffer_tiles, tile_size, hidden_width)
    other_buffer = sibling(own_buffer)
    aggregate_sum = aggregate_pair(core_id, spots, tile_count, tile_stack, own_buffer)
    aggregate_sum = aggregate_sum + aggregate_pair(
        1 - core_id, spots, tile_count, tile_stack, other_buffer
    )

    pre_act = aggregate_sum.reshape(rows_own, hidden_width)
    sigmoid_y = jax.nn.sigmoid(pre_act)
    activations = (pre_act * sigmoid_y).astype(jnp.bfloat16)
    grad_pre = (
        grad_out.astype(jnp.float32) * sigmoid_y * (1.0 + pre_act * (1.0 - sigmoid_y))
    ).astype(jnp.bfloat16)
    grad_turned = grad_pre.reshape(tile_rows, tile_size, hidden_width).transpose(0, 2, 1)

    outgoing = spread_pair(
        1 - core_id, spots, tile_count, tile_stack, grad_turned, buffer_tiles, jnp.bfloat16
    )
    arrived = sibling(outgoing)
    total = spread_pair(
        core_id, spots, tile_count, tile_stack, grad_turned, buffer_tiles, jnp.float32, arrived
    )
    total = reduce_phase(
        total.reshape(RING, RING, RING, rows_own, hidden_width), 2, jnp.bfloat16
    )
    total = reduce_phase_direct(total, 1, jnp.bfloat16)
    total = reduce_phase_direct(total, 0, jnp.bfloat16)
    grad_hidden = (
        total.reshape(tile_rows, hidden_width, tile_size)
        .transpose(0, 2, 1)
        .reshape(rows_own, hidden_width)
        .astype(jnp.bfloat16)
    )

    weight_term = jnp.dot(features_own, grad_hidden, preferred_element_type=jnp.float32)
    features_grad_local = lax.dot_general(
        weight, grad_hidden, (((1,), (1,)), ((), ())), preferred_element_type=jnp.float32
    ).astype(jnp.bfloat16)
    feat_count = lax.axis_size("feat")
    shard_rows = weight_term.shape[0] // feat_count
    outgoing = jnp.concatenate(
        [
            weight_term.reshape(feat_count, shard_rows, hidden_width),
            features_grad_local.astype(jnp.float32).reshape(feat_count, shard_rows, rows_own),
        ],
        axis=2,
    )
    got = lax.all_to_all(outgoing, "feat", split_axis=0, concat_axis=0, tiled=True)
    weight_part = jnp.sum(got[:, :, :hidden_width], axis=0)
    grad_features = (
        got[:, :, hidden_width:].astype(jnp.bfloat16).transpose(1, 0, 2).reshape(shard_rows, -1)
    )
    weight_part = weight_part + swapped(weight_part, "blk", 1)
    weight_part = weight_part + swapped(weight_part, "blk", 2)
    grad_weight = weight_part * lax.rsqrt(jnp.float32(block_rows * cycle_size))
    return (activations, grad_features, grad_weight)


def solution(mesh):
    placed = (
        P("feat", "blk"),
        P(),
        P(("blk", "feat"), None, None),
        P(("blk", "feat")),
        P(("blk", "feat")),
        P(("blk", "feat"), None),
    )
    return jax.shard_map(
        body,
        mesh=mesh,
        in_specs=placed,
        out_specs=(P(("blk", "feat"), None), P("feat", "blk"), P("feat", None)),
        check_vma=False,
    )
```

```python
import jax
import jax.numpy as jnp
from jax import lax
from jax.sharding import PartitionSpec as P
from jax.experimental import pallas as pl
from jax.experimental.pallas import tpu as pltpu

RING = 4
GATHER_ORDER = (("x", "z", "y"), ("y", "z", "x"))
BOTH = ("blk", "feat")


def place_of(blk, feat):
    return {
        "core": blk % 2,
        "y": (blk // 2) * 2 + feat // 16,
        "z": (feat // 4) % 4,
        "x": feat % 4,
    }


def linear_of(place):
    blk = (place["y"] // 2) * 2 + place["core"]
    feat = (place["y"] % 2) * 16 + place["z"] * 4 + place["x"]
    return blk * 32 + feat


def ring_shift(block, phase, distance):
    route = []
    for blk in range(4):
        for feat in range(32):
            place = place_of(blk, feat)
            axis = GATHER_ORDER[place["core"]][phase]
            target = dict(place)
            target[axis] = (place[axis] + distance) % RING
            route.append((linear_of(place), linear_of(target)))
    return lax.ppermute(block, BOTH, route)


def sibling(block):
    return lax.ppermute(block, "blk", [(i, i ^ 1) for i in range(lax.axis_size("blk"))])


def swapped(block, axis, mask):
    count = lax.axis_size(axis)
    return lax.ppermute(block, axis, [(i, i ^ mask) for i in range(count)])


def gather_phase(block, phase):
    half = block.shape[-1] // 2
    from_minus = ring_shift(block, phase, 1)
    from_plus = ring_shift(block, phase, -1)
    far_low = ring_shift(from_minus[..., :half], phase, 1)
    far_high = ring_shift(from_plus[..., half:], phase, -1)
    far = jnp.concatenate([far_low, far_high], axis=-1)
    return jnp.stack([block, from_plus, far, from_minus])


def gather_phase_direct(block, phase):
    from_minus = ring_shift(block, phase, 1)
    from_plus = ring_shift(block, phase, -1)
    far = ring_shift(block, phase, 2)
    return jnp.stack([block, from_plus, far, from_minus])


def reduce_phase_direct(total, phase, wire_type):
    from_minus = ring_shift(total[1].astype(wire_type), phase, 1)
    from_plus = ring_shift(total[3].astype(wire_type), phase, -1)
    far = ring_shift(total[2].astype(wire_type), phase, 2)
    return (
        total[0]
        + from_minus.astype(jnp.float32)
        + from_plus.astype(jnp.float32)
        + far.astype(jnp.float32)
    )


def reduce_phase(total, phase, wire_type, extra=None):
    half = total.shape[-2] // 2

    def term(k):
        if extra is None:
            return total[k]
        return total[k] + extra[k].astype(jnp.float32)

    far = term(2)
    got_minus = ring_shift(far[..., :half, :].astype(wire_type), phase, 1)
    got_plus = ring_shift(far[..., half:, :].astype(wire_type), phase, -1)
    ahead = term(1)
    ahead = jnp.concatenate(
        [ahead[..., :half, :] + got_minus.astype(jnp.float32), ahead[..., half:, :]], axis=-2
    )
    behind = term(3)
    behind = jnp.concatenate(
        [behind[..., :half, :], behind[..., half:, :] + got_plus.astype(jnp.float32)], axis=-2
    )
    from_minus = ring_shift(ahead.astype(wire_type), phase, 1)
    from_plus = ring_shift(behind.astype(wire_type), phase, -1)
    return term(0) + from_minus.astype(jnp.float32) + from_plus.astype(jnp.float32)


def scatter_rows(total, axis, wire_type):
    count = lax.axis_size(axis)
    index = lax.axis_index(axis)
    mask = count // 2
    while mask >= 1:
        half = total.shape[0] // 2
        lower, upper_part = total[:half], total[half:]
        upper = (index // mask) % 2 == 1
        keep = jnp.where(upper, upper_part, lower)
        send = jnp.where(upper, lower, upper_part)
        got = swapped(send.astype(wire_type), axis, mask)
        total = keep + got.astype(jnp.float32)
        mask //= 2
    return total


def aggregate_kernel(core_ref, where_ref, count_ref, tiles_ref, proj_ref, out_ref, wide_ref, picked_ref):
    row = pl.program_id(0)
    half_id = pl.program_id(1)
    tile_rows = pl.num_programs(0)
    slot_count, tile_size, _ = tiles_ref.shape
    base = (half_id * 2 + core_ref[0]) * tile_rows + row
    live = count_ref[base]
    for slot in range(slot_count):
        wide_ref[:, slot * tile_size:(slot + 1) * tile_size] = tiles_ref[slot]
        piece = proj_ref[where_ref[base * slot_count + slot]]
        picked_ref[slot * tile_size:(slot + 1) * tile_size, :] = jnp.where(
            slot < live, piece, jnp.zeros_like(piece)
        )
    part = jnp.dot(wide_ref[...], picked_ref[...], preferred_element_type=jnp.float32)

    @pl.when(half_id == 0)
    def _():
        out_ref[...] = part

    @pl.when(half_id != 0)
    def _():
        out_ref[...] += part


def aggregate_pair(core_id, spots, counts, tile_stack, buffer):
    blocks, tile_rows, slot_count, tile_size, _ = tile_stack.shape
    hidden_width = buffer.shape[-1]
    grid_spec = pltpu.PrefetchScalarGridSpec(
        num_scalar_prefetch=3,
        grid=(tile_rows, blocks // 2),
        in_specs=[
            pl.BlockSpec(
                (None, None, slot_count, tile_size, tile_size),
                lambda r, h, c, w, n: (h * 2 + c[0], r, 0, 0, 0),
            ),
            pl.BlockSpec(buffer.shape, lambda r, h, c, w, n: (0, 0, 0)),
        ],
        out_specs=pl.BlockSpec((None, tile_size, hidden_width), lambda r, h, c, w, n: (r, 0, 0)),
        scratch_shapes=[
            pltpu.VMEM((tile_size, slot_count * tile_size), tile_stack.dtype),
            pltpu.VMEM((slot_count * tile_size, hidden_width), buffer.dtype),
        ],
    )
    return pl.pallas_call(
        aggregate_kernel,
        grid_spec=grid_spec,
        out_shape=jax.ShapeDtypeStruct((tile_rows, tile_size, hidden_width), jnp.float32),
        compiler_params=pltpu.CompilerParams(dimension_semantics=("arbitrary", "arbitrary")),
    )(jnp.reshape(core_id, (1,)).astype(jnp.int32), spots, counts, tile_stack, buffer)


def spread_kernel(core_ref, where_ref, count_ref, tiles_ref, grad_ref, *rest):
    if len(rest) == 5:
        start_ref, out_ref, total_ref, wide_ref, terms_ref = rest
    else:
        start_ref = None
        out_ref, total_ref, wide_ref, terms_ref = rest
    row = pl.program_id(0)
    half_id = pl.program_id(1)
    tile_rows = pl.num_programs(0)
    halves = pl.num_programs(1)
    slot_count, tile_size, _ = tiles_ref.shape
    base = (half_id * 2 + core_ref[0]) * tile_rows + row
    live = count_ref[base]

    @pl.when((row == 0) & (half_id == 0))
    def _():
        if start_ref is None:
            total_ref[...] = jnp.zeros(total_ref.shape, jnp.float32)
        else:
            total_ref[...] = start_ref[...].astype(jnp.float32)

    for slot in range(slot_count):
        wide_ref[:, slot * tile_size:(slot + 1) * tile_size] = tiles_ref[slot]
    terms_ref[...] = jnp.dot(grad_ref[...], wide_ref[...], preferred_element_type=jnp.float32)
    for slot in range(slot_count):
        spot = where_ref[base * slot_count + slot]

        @pl.when(slot < live)
        def _():
            total_ref[spot] += terms_ref[:, slot * tile_size:(slot + 1) * tile_size]

    @pl.when((row == tile_rows - 1) & (half_id == halves - 1))
    def _():
        out_ref[...] = total_ref[...].astype(out_ref.dtype)


def spread_pair(core_id, spots, counts, tile_stack, grad_turned, buffer_tiles, out_type, start=None):
    blocks, tile_rows, slot_count, tile_size, _ = tile_stack.shape
    hidden_width = grad_turned.shape[1]
    grid_spec = pltpu.PrefetchScalarGridSpec(
        num_scalar_prefetch=3,
        grid=(tile_rows, blocks // 2),
        in_specs=[
            pl.BlockSpec(
                (None, None, slot_count, tile_size, tile_size),
                lambda r, h, c, w, n: (h * 2 + c[0], r, 0, 0, 0),
            ),
            pl.BlockSpec((None, hidden_width, tile_size), lambda r, h, c, w, n: (r, 0, 0)),
        ]
        + ([] if start is None else [pl.BlockSpec(start.shape, lambda r, h, c, w, n: (0, 0, 0))]),
        out_specs=pl.BlockSpec(
            (buffer_tiles, hidden_width, tile_size), lambda r, h, c, w, n: (0, 0, 0)
        ),
        scratch_shapes=[
            pltpu.VMEM((buffer_tiles, hidden_width, tile_size), jnp.float32),
            pltpu.VMEM((tile_size, slot_count * tile_size), tile_stack.dtype),
            pltpu.VMEM((hidden_width, slot_count * tile_size), jnp.float32),
        ],
    )
    return pl.pallas_call(
        spread_kernel,
        grid_spec=grid_spec,
        out_shape=jax.ShapeDtypeStruct((buffer_tiles, hidden_width, tile_size), out_type),
        compiler_params=pltpu.CompilerParams(dimension_semantics=("arbitrary", "arbitrary")),
    )(
        jnp.reshape(core_id, (1,)).astype(jnp.int32),
        spots,
        counts,
        tile_stack,
        grad_turned,
        *([] if start is None else [start]),
    )


def chunk_sources(blk_id, feat_id):
    own = place_of(blk_id, feat_id)
    chunk = jnp.arange(RING ** 3, dtype=jnp.int32)
    lead, mid, last = chunk // 16, (chunk // 4) % 4, chunk % 4
    ry = jnp.where(own["core"] == 0, lead, last)
    rx = jnp.where(own["core"] == 0, last, lead)
    y = (own["y"] + ry) % RING
    z = (own["z"] + mid) % RING
    x = (own["x"] + rx) % RING
    return y, (y % 2) * 16 + z * 4 + x


def buffer_spots(tile_col, blk_id, feat_id, block_tiles, tiles_per_device):
    own = place_of(blk_id, feat_id)
    block = tile_col // block_tiles
    local = tile_col % block_tiles
    source_feat = local // tiles_per_device
    part = local % tiles_per_device
    source = place_of(block, source_feat)
    rel = {axis: (source[axis] - own[axis]) % RING for axis in ("y", "z", "x")}
    chunk = jnp.where(
        source["core"] == 0,
        rel["y"] * 16 + rel["z"] * 4 + rel["x"],
        rel["x"] * 16 + rel["z"] * 4 + rel["y"],
    )
    return (chunk * tiles_per_device + part).astype(jnp.int32)


def body(features_t, weight, tile_values, tile_col, tile_count, grad_out):
    cycle_size = lax.axis_size("blk")
    hidden_width = weight.shape[1]
    tile_size = tile_values.shape[1]
    rows_own = grad_out.shape[0]
    tile_rows = rows_own // tile_size
    block_rows = features_t.shape[1]
    block_tiles = block_rows // tile_size
    slot_count = tile_values.shape[0] // (cycle_size * tile_rows)
    feat_id = lax.axis_index("feat")
    blk_id = lax.axis_index("blk")
    core_id = blk_id % 2
    tile_stack = tile_values.reshape(cycle_size, tile_rows, slot_count, tile_size, tile_size)
    spots = buffer_spots(tile_col, blk_id, feat_id, block_tiles, tile_rows)
    buffer_tiles = block_tiles * 2

    gathered = gather_phase_direct(features_t, 0)
    gathered = gather_phase_direct(gathered, 1)
    gathered = gather_phase(gathered, 2)
    part_cols = features_t.shape[0]
    source_y, source_feat = chunk_sources(blk_id, feat_id)
    feature_rows = (source_feat[:, None] * part_cols + jnp.arange(part_cols)[None, :]).reshape(-1)
    weight_rows = jnp.take(weight, feature_rows, axis=0)
    stacked = gathered.reshape(-1, block_rows)
    halves = []
    for half_id in range(2):
        keep = jnp.repeat(source_y // 2 == half_id, part_cols)
        chosen = jnp.where(keep[:, None], weight_rows, jnp.zeros((), weight.dtype))
        halves.append(
            lax.dot_general(
                stacked, chosen, (((0,), (0,)), ((), ())), preferred_element_type=jnp.float32
            ).astype(jnp.bfloat16)
        )
    own_buffer = jnp.stack(halves).reshape(buffer_tiles, tile_size, hidden_width)
    other_buffer = sibling(own_buffer)
    block_spots = ((tile_col // block_tiles) // 2 * block_tiles + tile_col % block_tiles).astype(
        jnp.int32
    )
    aggregate_sum = aggregate_pair(core_id, block_spots, tile_count, tile_stack, own_buffer)
    aggregate_sum = aggregate_sum + aggregate_pair(
        1 - core_id, block_spots, tile_count, tile_stack, other_buffer
    )

    pre_act = aggregate_sum.reshape(rows_own, hidden_width)
    sigmoid_y = jax.nn.sigmoid(pre_act)
    activations = (pre_act * sigmoid_y).astype(jnp.bfloat16)
    grad_pre = (
        grad_out.astype(jnp.float32) * sigmoid_y * (1.0 + pre_act * (1.0 - sigmoid_y))
    ).astype(jnp.bfloat16)
    grad_turned = grad_pre.reshape(tile_rows, tile_size, hidden_width).transpose(0, 2, 1)

    outgoing = spread_pair(
        1 - core_id, spots, tile_count, tile_stack, grad_turned, buffer_tiles, jnp.bfloat16
    )
    arrived = sibling(outgoing)
    total = spread_pair(
        core_id, spots, tile_count, tile_stack, grad_turned, buffer_tiles, jnp.float32, arrived
    )
    total = reduce_phase(
        total.reshape(RING, RING, RING, rows_own, hidden_width), 2, jnp.bfloat16
    )
    total = reduce_phase_direct(total, 1, jnp.bfloat16)
    total = reduce_phase_direct(total, 0, jnp.bfloat16)
    grad_hidden = (
        total.reshape(tile_rows, hidden_width, tile_size)
        .transpose(0, 2, 1)
        .reshape(rows_own, hidden_width)
        .astype(jnp.bfloat16)
    )

    own_cols = lax.dynamic_slice_in_dim(gathered, feat_id * rows_own, rows_own, gathered.ndim - 1)
    chunk_terms = jnp.dot(
        own_cols.reshape(-1, rows_own), grad_hidden, preferred_element_type=jnp.float32
    )
    own_place = place_of(blk_id, feat_id)
    feat_all = jnp.arange(lax.axis_size("feat"), dtype=jnp.int32)
    home = place_of(blk_id, feat_all)
    ry = (home["y"] - own_place["y"]) % RING
    rz = (home["z"] - own_place["z"]) % RING
    rx = (home["x"] - own_place["x"]) % RING
    home_chunk = jnp.where(own_place["core"] == 0, ry * 16 + rz * 4 + rx, rx * 16 + rz * 4 + ry)
    term_rows = (home_chunk[:, None] * part_cols + jnp.arange(part_cols)[None, :]).reshape(-1)
    weight_term = jnp.take(chunk_terms, term_rows, axis=0)
    features_grad_local = lax.dot_general(
        weight, grad_hidden, (((1,), (1,)), ((), ())), preferred_element_type=jnp.float32
    ).astype(jnp.bfloat16)
    feat_count = lax.axis_size("feat")
    shard_rows = weight_term.shape[0] // feat_count
    outgoing = jnp.concatenate(
        [
            weight_term.reshape(feat_count, shard_rows, hidden_width),
            features_grad_local.astype(jnp.float32).reshape(feat_count, shard_rows, rows_own),
        ],
        axis=2,
    )
    got = lax.all_to_all(outgoing, "feat", split_axis=0, concat_axis=0, tiled=True)
    weight_part = jnp.sum(got[:, :, :hidden_width], axis=0)
    grad_features = (
        got[:, :, hidden_width:].astype(jnp.bfloat16).transpose(1, 0, 2).reshape(shard_rows, -1)
    )
    weight_part = weight_part + swapped(weight_part, "blk", 1)
    weight_part = weight_part + swapped(weight_part, "blk", 2)
    grad_weight = weight_part * lax.rsqrt(jnp.float32(block_rows * cycle_size))
    return (activations, grad_features, grad_weight)


def solution(mesh):
    placed = (
        P("feat", "blk"),
        P(),
        P(("blk", "feat"), None, None),
        P(("blk", "feat")),
        P(("blk", "feat")),
        P(("blk", "feat"), None),
    )
    return jax.shard_map(
        body,
        mesh=mesh,
        in_specs=placed,
        out_specs=(P(("blk", "feat"), None), P("feat", "blk"), P("feat", None)),
        check_vma=False,
    )
```

```python
import jax
import jax.numpy as jnp
from jax import lax
from jax.sharding import PartitionSpec as P
from jax.experimental import pallas as pl
from jax.experimental.pallas import tpu as pltpu

RING = 4
GATHER_ORDER = (("x", "z", "y"), ("y", "z", "x"))
BOTH = ("blk", "feat")


def place_of(blk, feat):
    return {
        "core": blk % 2,
        "y": (blk // 2) * 2 + feat // 16,
        "z": (feat // 4) % 4,
        "x": feat % 4,
    }


def linear_of(place):
    blk = (place["y"] // 2) * 2 + place["core"]
    feat = (place["y"] % 2) * 16 + place["z"] * 4 + place["x"]
    return blk * 32 + feat


def ring_shift(block, phase, distance):
    route = []
    for blk in range(4):
        for feat in range(32):
            place = place_of(blk, feat)
            axis = GATHER_ORDER[place["core"]][phase]
            target = dict(place)
            target[axis] = (place[axis] + distance) % RING
            route.append((linear_of(place), linear_of(target)))
    return lax.ppermute(block, BOTH, route)


def sibling(block):
    return lax.ppermute(block, "blk", [(i, i ^ 1) for i in range(lax.axis_size("blk"))])


def swapped(block, axis, mask):
    count = lax.axis_size(axis)
    return lax.ppermute(block, axis, [(i, i ^ mask) for i in range(count)])


def gather_phase(block, phase):
    half = block.shape[-2] // 2
    from_minus = ring_shift(block, phase, 1)
    from_plus = ring_shift(block, phase, -1)
    far_low = ring_shift(from_minus[..., :half, :], phase, 1)
    far_high = ring_shift(from_plus[..., half:, :], phase, -1)
    far = jnp.concatenate([far_low, far_high], axis=-2)
    return jnp.stack([block, from_plus, far, from_minus])


def gather_phase_direct(block, phase):
    from_minus = ring_shift(block, phase, 1)
    from_plus = ring_shift(block, phase, -1)
    far = ring_shift(block, phase, 2)
    return jnp.stack([block, from_plus, far, from_minus])


def reduce_phase_direct(total, phase, wire_type):
    from_minus = ring_shift(total[1].astype(wire_type), phase, 1)
    from_plus = ring_shift(total[3].astype(wire_type), phase, -1)
    far = ring_shift(total[2].astype(wire_type), phase, 2)
    return (
        total[0]
        + from_minus.astype(jnp.float32)
        + from_plus.astype(jnp.float32)
        + far.astype(jnp.float32)
    )


def reduce_phase(total, phase, wire_type, extra=None):
    half = total.shape[-2] // 2

    def term(k):
        if extra is None:
            return total[k]
        return total[k] + extra[k].astype(jnp.float32)

    far = term(2)
    got_minus = ring_shift(far[..., :half, :].astype(wire_type), phase, 1)
    got_plus = ring_shift(far[..., half:, :].astype(wire_type), phase, -1)
    ahead = term(1)
    ahead = jnp.concatenate(
        [ahead[..., :half, :] + got_minus.astype(jnp.float32), ahead[..., half:, :]], axis=-2
    )
    behind = term(3)
    behind = jnp.concatenate(
        [behind[..., :half, :], behind[..., half:, :] + got_plus.astype(jnp.float32)], axis=-2
    )
    from_minus = ring_shift(ahead.astype(wire_type), phase, 1)
    from_plus = ring_shift(behind.astype(wire_type), phase, -1)
    return term(0) + from_minus.astype(jnp.float32) + from_plus.astype(jnp.float32)


def scatter_rows(total, axis, wire_type):
    count = lax.axis_size(axis)
    index = lax.axis_index(axis)
    mask = count // 2
    while mask >= 1:
        half = total.shape[0] // 2
        lower, upper_part = total[:half], total[half:]
        upper = (index // mask) % 2 == 1
        keep = jnp.where(upper, upper_part, lower)
        send = jnp.where(upper, lower, upper_part)
        got = swapped(send.astype(wire_type), axis, mask)
        total = keep + got.astype(jnp.float32)
        mask //= 2
    return total


def aggregate_kernel(core_ref, where_ref, count_ref, tiles_ref, proj_ref, out_ref, wide_ref, picked_ref):
    row = pl.program_id(0)
    half_id = pl.program_id(1)
    tile_rows = pl.num_programs(0)
    slot_count, tile_size, _ = tiles_ref.shape
    base = (half_id * 2 + core_ref[0]) * tile_rows + row
    live = count_ref[base]
    for slot in range(slot_count):
        wide_ref[:, slot * tile_size:(slot + 1) * tile_size] = tiles_ref[slot]
        piece = proj_ref[where_ref[base * slot_count + slot]]
        picked_ref[slot * tile_size:(slot + 1) * tile_size, :] = jnp.where(
            slot < live, piece, jnp.zeros_like(piece)
        )
    part = jnp.dot(wide_ref[...], picked_ref[...], preferred_element_type=jnp.float32)

    @pl.when(half_id == 0)
    def _():
        out_ref[...] = part

    @pl.when(half_id != 0)
    def _():
        out_ref[...] += part


def aggregate_pair(core_id, spots, counts, tile_stack, buffer):
    blocks, tile_rows, slot_count, tile_size, _ = tile_stack.shape
    hidden_width = buffer.shape[-1]
    grid_spec = pltpu.PrefetchScalarGridSpec(
        num_scalar_prefetch=3,
        grid=(tile_rows, blocks // 2),
        in_specs=[
            pl.BlockSpec(
                (None, None, slot_count, tile_size, tile_size),
                lambda r, h, c, w, n: (h * 2 + c[0], r, 0, 0, 0),
            ),
            pl.BlockSpec(buffer.shape, lambda r, h, c, w, n: (0, 0, 0)),
        ],
        out_specs=pl.BlockSpec((None, tile_size, hidden_width), lambda r, h, c, w, n: (r, 0, 0)),
        scratch_shapes=[
            pltpu.VMEM((tile_size, slot_count * tile_size), tile_stack.dtype),
            pltpu.VMEM((slot_count * tile_size, hidden_width), buffer.dtype),
        ],
    )
    return pl.pallas_call(
        aggregate_kernel,
        grid_spec=grid_spec,
        out_shape=jax.ShapeDtypeStruct((tile_rows, tile_size, hidden_width), jnp.float32),
        compiler_params=pltpu.CompilerParams(dimension_semantics=("arbitrary", "arbitrary")),
    )(jnp.reshape(core_id, (1,)).astype(jnp.int32), spots, counts, tile_stack, buffer)


def spread_kernel(core_ref, where_ref, count_ref, tiles_ref, grad_ref, *rest):
    if len(rest) == 5:
        start_ref, out_ref, total_ref, wide_ref, terms_ref = rest
    else:
        start_ref = None
        out_ref, total_ref, wide_ref, terms_ref = rest
    row = pl.program_id(0)
    half_id = pl.program_id(1)
    tile_rows = pl.num_programs(0)
    halves = pl.num_programs(1)
    slot_count, tile_size, _ = tiles_ref.shape
    base = (half_id * 2 + core_ref[0]) * tile_rows + row
    live = count_ref[base]

    @pl.when((row == 0) & (half_id == 0))
    def _():
        if start_ref is None:
            total_ref[...] = jnp.zeros(total_ref.shape, jnp.float32)
        else:
            total_ref[...] = start_ref[...].astype(jnp.float32)

    for slot in range(slot_count):
        wide_ref[:, slot * tile_size:(slot + 1) * tile_size] = tiles_ref[slot]
    terms_ref[...] = jnp.dot(grad_ref[...], wide_ref[...], preferred_element_type=jnp.float32)
    for slot in range(slot_count):
        spot = where_ref[base * slot_count + slot]

        @pl.when(slot < live)
        def _():
            total_ref[spot] += terms_ref[:, slot * tile_size:(slot + 1) * tile_size]

    @pl.when((row == tile_rows - 1) & (half_id == halves - 1))
    def _():
        out_ref[...] = total_ref[...].astype(out_ref.dtype)


def spread_pair(
    core_id, spots, counts, tile_stack, grad_turned, buffer_tiles, out_type, start=None,
    block_step=2, core_step=1,
):
    _, tile_rows, slot_count, tile_size, _ = tile_stack.shape
    blocks = lax.axis_size("blk")
    hidden_width = grad_turned.shape[1]
    grid_spec = pltpu.PrefetchScalarGridSpec(
        num_scalar_prefetch=3,
        grid=(tile_rows, blocks // 2),
        in_specs=[
            pl.BlockSpec(
                (None, None, slot_count, tile_size, tile_size),
                lambda r, h, c, w, n: (h * block_step + c[0] * core_step, r, 0, 0, 0),
            ),
            pl.BlockSpec((None, hidden_width, tile_size), lambda r, h, c, w, n: (r, 0, 0)),
        ]
        + ([] if start is None else [pl.BlockSpec(start.shape, lambda r, h, c, w, n: (0, 0, 0))]),
        out_specs=pl.BlockSpec(
            (buffer_tiles, hidden_width, tile_size), lambda r, h, c, w, n: (0, 0, 0)
        ),
        scratch_shapes=[
            pltpu.VMEM((buffer_tiles, hidden_width, tile_size), jnp.float32),
            pltpu.VMEM((tile_size, slot_count * tile_size), tile_stack.dtype),
            pltpu.VMEM((hidden_width, slot_count * tile_size), jnp.float32),
        ],
    )
    return pl.pallas_call(
        spread_kernel,
        grid_spec=grid_spec,
        out_shape=jax.ShapeDtypeStruct((buffer_tiles, hidden_width, tile_size), out_type),
        compiler_params=pltpu.CompilerParams(dimension_semantics=("arbitrary", "arbitrary")),
    )(
        jnp.reshape(core_id, (1,)).astype(jnp.int32),
        spots,
        counts,
        tile_stack,
        grad_turned,
        *([] if start is None else [start]),
    )


def buffer_spots(tile_col, blk_id, feat_id, block_tiles, tiles_per_device):
    own = place_of(blk_id, feat_id)
    block = tile_col // block_tiles
    local = tile_col % block_tiles
    source_feat = local // tiles_per_device
    part = local % tiles_per_device
    source = place_of(block, source_feat)
    rel = {axis: (source[axis] - own[axis]) % RING for axis in ("y", "z", "x")}
    chunk = jnp.where(
        source["core"] == 0,
        rel["y"] * 16 + rel["z"] * 4 + rel["x"],
        rel["x"] * 16 + rel["z"] * 4 + rel["y"],
    )
    return (chunk * tiles_per_device + part).astype(jnp.int32)


def body(features_t, weight, tile_values, tile_col, tile_count, grad_out):
    cycle_size = lax.axis_size("blk")
    hidden_width = weight.shape[1]
    tile_size = tile_values.shape[1]
    rows_own = grad_out.shape[0]
    tile_rows = rows_own // tile_size
    block_rows = features_t.shape[1]
    block_tiles = block_rows // tile_size
    slot_count = tile_values.shape[0] // (cycle_size * tile_rows)
    feat_id = lax.axis_index("feat")
    blk_id = lax.axis_index("blk")
    core_id = blk_id % 2
    tile_stack = tile_values.reshape(cycle_size, tile_rows, slot_count, tile_size, tile_size)
    spots = buffer_spots(tile_col, blk_id, feat_id, block_tiles, tile_rows)
    by_core = tile_stack.reshape(cycle_size // 2, 2, tile_rows, slot_count, tile_size, tile_size)
    for_sibling = lax.dynamic_index_in_dim(by_core, 1 - core_id, 1, keepdims=False)
    sibling_tiles = sibling(for_sibling)
    sibling_spots = buffer_spots(sibling(tile_col), blk_id, feat_id, block_tiles, tile_rows)
    sibling_count = sibling(tile_count)
    buffer_tiles = block_tiles * 2

    features_own = lax.all_to_all(features_t, "feat", split_axis=1, concat_axis=0, tiled=True)
    projected = lax.dot_general(
        features_own, weight, (((0,), (0,)), ((), ())), preferred_element_type=jnp.float32
    ).astype(jnp.bfloat16)

    gathered = gather_phase_direct(projected, 0)
    gathered = gather_phase_direct(gathered, 1)
    gathered = gather_phase(gathered, 2)
    own_buffer = gathered.reshape(buffer_tiles, tile_size, hidden_width)
    other_buffer = sibling(own_buffer)
    aggregate_sum = aggregate_pair(core_id, spots, tile_count, tile_stack, own_buffer)
    aggregate_sum = aggregate_sum + aggregate_pair(
        1 - core_id, spots, tile_count, tile_stack, other_buffer
    )

    pre_act = aggregate_sum.reshape(rows_own, hidden_width)
    sigmoid_y = jax.nn.sigmoid(pre_act)
    activations = (pre_act * sigmoid_y).astype(jnp.bfloat16)
    grad_pre = (
        grad_out.astype(jnp.float32) * sigmoid_y * (1.0 + pre_act * (1.0 - sigmoid_y))
    ).astype(jnp.bfloat16)
    grad_turned = grad_pre.reshape(tile_rows, tile_size, hidden_width).transpose(0, 2, 1)

    sibling_grad = sibling(grad_turned)
    total = spread_pair(
        core_id, spots, tile_count, tile_stack, grad_turned, buffer_tiles, jnp.float32
    )
    total = spread_pair(
        core_id, sibling_spots, sibling_count, sibling_tiles, sibling_grad, buffer_tiles,
        jnp.float32, total, block_step=1, core_step=0,
    )
    total = reduce_phase(
        total.reshape(RING, RING, RING, rows_own, hidden_width), 2, jnp.bfloat16
    )
    total = reduce_phase_direct(total, 1, jnp.bfloat16)
    total = reduce_phase_direct(total, 0, jnp.bfloat16)
    grad_hidden = (
        total.reshape(tile_rows, hidden_width, tile_size)
        .transpose(0, 2, 1)
        .reshape(rows_own, hidden_width)
        .astype(jnp.bfloat16)
    )

    weight_term = jnp.dot(features_own, grad_hidden, preferred_element_type=jnp.float32)
    features_grad_local = lax.dot_general(
        weight, grad_hidden, (((1,), (1,)), ((), ())), preferred_element_type=jnp.float32
    ).astype(jnp.bfloat16)
    feat_count = lax.axis_size("feat")
    shard_rows = weight_term.shape[0] // feat_count
    outgoing = jnp.concatenate(
        [
            weight_term.reshape(feat_count, shard_rows, hidden_width),
            features_grad_local.astype(jnp.float32).reshape(feat_count, shard_rows, rows_own),
        ],
        axis=2,
    )
    got = lax.all_to_all(outgoing, "feat", split_axis=0, concat_axis=0, tiled=True)
    weight_part = jnp.sum(got[:, :, :hidden_width], axis=0)
    grad_features = (
        got[:, :, hidden_width:].astype(jnp.bfloat16).transpose(1, 0, 2).reshape(shard_rows, -1)
    )
    weight_part = weight_part + swapped(weight_part, "blk", 1)
    weight_part = weight_part + swapped(weight_part, "blk", 2)
    grad_weight = weight_part * lax.rsqrt(jnp.float32(block_rows * cycle_size))
    return (activations, grad_features, grad_weight)


def solution(mesh):
    placed = (
        P("feat", "blk"),
        P(),
        P(("blk", "feat"), None, None),
        P(("blk", "feat")),
        P(("blk", "feat")),
        P(("blk", "feat"), None),
    )
    return jax.shard_map(
        body,
        mesh=mesh,
        in_specs=placed,
        out_specs=(P(("blk", "feat"), None), P("feat", "blk"), P("feat", None)),
        check_vma=False,
    )
```

```python
import jax
import jax.numpy as jnp
from jax import lax
from jax.sharding import PartitionSpec as P
from jax.experimental import pallas as pl
from jax.experimental.pallas import tpu as pltpu

RING = 4
GATHER_ORDER = (("x", "z", "y"), ("y", "z", "x"))
BOTH = ("blk", "feat")


def place_of(blk, feat):
    return {
        "core": blk % 2,
        "y": (blk // 2) * 2 + feat // 16,
        "z": (feat // 4) % 4,
        "x": feat % 4,
    }


def linear_of(place):
    blk = (place["y"] // 2) * 2 + place["core"]
    feat = (place["y"] % 2) * 16 + place["z"] * 4 + place["x"]
    return blk * 32 + feat


def ring_shift(block, phase, distance):
    route = []
    for blk in range(4):
        for feat in range(32):
            place = place_of(blk, feat)
            axis = GATHER_ORDER[place["core"]][phase]
            target = dict(place)
            target[axis] = (place[axis] + distance) % RING
            route.append((linear_of(place), linear_of(target)))
    return lax.ppermute(block, BOTH, route)


def sibling(block):
    return lax.ppermute(block, "blk", [(i, i ^ 1) for i in range(lax.axis_size("blk"))])


def swapped(block, axis, mask):
    count = lax.axis_size(axis)
    return lax.ppermute(block, axis, [(i, i ^ mask) for i in range(count)])


def gather_phase(block, phase):
    half = block.shape[-2] // 2
    from_minus = ring_shift(block, phase, 1)
    from_plus = ring_shift(block, phase, -1)
    far_low = ring_shift(from_minus[..., :half, :], phase, 1)
    far_high = ring_shift(from_plus[..., half:, :], phase, -1)
    far = jnp.concatenate([far_low, far_high], axis=-2)
    return jnp.stack([block, from_plus, far, from_minus])


def gather_phase_direct(block, phase):
    from_minus = ring_shift(block, phase, 1)
    from_plus = ring_shift(block, phase, -1)
    far = ring_shift(block, phase, 2)
    return jnp.stack([block, from_plus, far, from_minus])


def reduce_phase_direct(total, phase, wire_type):
    from_minus = ring_shift(total[1].astype(wire_type), phase, 1)
    from_plus = ring_shift(total[3].astype(wire_type), phase, -1)
    far = ring_shift(total[2].astype(wire_type), phase, 2)
    return (
        total[0]
        + from_minus.astype(jnp.float32)
        + from_plus.astype(jnp.float32)
        + far.astype(jnp.float32)
    )


def reduce_phase(total, phase, wire_type, extra=None):
    half = total.shape[-2] // 2

    def term(k):
        if extra is None:
            return total[k]
        return total[k] + extra[k].astype(jnp.float32)

    far = term(2)
    got_minus = ring_shift(far[..., :half, :].astype(wire_type), phase, 1)
    got_plus = ring_shift(far[..., half:, :].astype(wire_type), phase, -1)
    ahead = term(1)
    ahead = jnp.concatenate(
        [ahead[..., :half, :] + got_minus.astype(jnp.float32), ahead[..., half:, :]], axis=-2
    )
    behind = term(3)
    behind = jnp.concatenate(
        [behind[..., :half, :], behind[..., half:, :] + got_plus.astype(jnp.float32)], axis=-2
    )
    from_minus = ring_shift(ahead.astype(wire_type), phase, 1)
    from_plus = ring_shift(behind.astype(wire_type), phase, -1)
    return term(0) + from_minus.astype(jnp.float32) + from_plus.astype(jnp.float32)


def scatter_rows(total, axis, wire_type):
    count = lax.axis_size(axis)
    index = lax.axis_index(axis)
    mask = count // 2
    while mask >= 1:
        half = total.shape[0] // 2
        lower, upper_part = total[:half], total[half:]
        upper = (index // mask) % 2 == 1
        keep = jnp.where(upper, upper_part, lower)
        send = jnp.where(upper, lower, upper_part)
        got = swapped(send.astype(wire_type), axis, mask)
        total = keep + got.astype(jnp.float32)
        mask //= 2
    return total


def aggregate_kernel(core_ref, where_ref, count_ref, tiles_ref, proj_ref, out_ref, wide_ref, picked_ref):
    row = pl.program_id(0)
    half_id = pl.program_id(1)
    tile_rows = pl.num_programs(0)
    slot_count, tile_size, _ = tiles_ref.shape
    base = (half_id * 2 + core_ref[0]) * tile_rows + row
    live = count_ref[base]
    for slot in range(slot_count):
        wide_ref[:, slot * tile_size:(slot + 1) * tile_size] = tiles_ref[slot]
        piece = proj_ref[where_ref[base * slot_count + slot]]
        picked_ref[slot * tile_size:(slot + 1) * tile_size, :] = jnp.where(
            slot < live, piece, jnp.zeros_like(piece)
        )
    part = jnp.dot(wide_ref[...], picked_ref[...], preferred_element_type=jnp.float32)

    @pl.when(half_id == 0)
    def _():
        out_ref[...] = part

    @pl.when(half_id != 0)
    def _():
        out_ref[...] += part


def aggregate_pair(core_id, spots, counts, tile_stack, buffer):
    blocks, tile_rows, slot_count, tile_size, _ = tile_stack.shape
    hidden_width = buffer.shape[-1]
    grid_spec = pltpu.PrefetchScalarGridSpec(
        num_scalar_prefetch=3,
        grid=(tile_rows, blocks // 2),
        in_specs=[
            pl.BlockSpec(
                (None, None, slot_count, tile_size, tile_size),
                lambda r, h, c, w, n: (h * 2 + c[0], r, 0, 0, 0),
            ),
            pl.BlockSpec(buffer.shape, lambda r, h, c, w, n: (0, 0, 0)),
        ],
        out_specs=pl.BlockSpec((None, tile_size, hidden_width), lambda r, h, c, w, n: (r, 0, 0)),
        scratch_shapes=[
            pltpu.VMEM((tile_size, slot_count * tile_size), tile_stack.dtype),
            pltpu.VMEM((slot_count * tile_size, hidden_width), buffer.dtype),
        ],
    )
    return pl.pallas_call(
        aggregate_kernel,
        grid_spec=grid_spec,
        out_shape=jax.ShapeDtypeStruct((tile_rows, tile_size, hidden_width), jnp.float32),
        compiler_params=pltpu.CompilerParams(dimension_semantics=("arbitrary", "arbitrary")),
    )(jnp.reshape(core_id, (1,)).astype(jnp.int32), spots, counts, tile_stack, buffer)


def spread_kernel(core_ref, where_ref, count_ref, tiles_ref, grad_ref, *rest):
    if len(rest) == 5:
        start_ref, out_ref, total_ref, wide_ref, terms_ref = rest
    else:
        start_ref = None
        out_ref, total_ref, wide_ref, terms_ref = rest
    row = pl.program_id(0)
    half_id = pl.program_id(1)
    tile_rows = pl.num_programs(0)
    halves = pl.num_programs(1)
    slot_count, tile_size, _ = tiles_ref.shape
    base = (half_id * 2 + core_ref[0]) * tile_rows + row
    live = count_ref[base]

    @pl.when((row == 0) & (half_id == 0))
    def _():
        if start_ref is None:
            total_ref[...] = jnp.zeros(total_ref.shape, jnp.float32)
        else:
            total_ref[...] = start_ref[...].astype(jnp.float32)

    for slot in range(slot_count):
        wide_ref[:, slot * tile_size:(slot + 1) * tile_size] = tiles_ref[slot]
    terms_ref[...] = jnp.dot(grad_ref[...], wide_ref[...], preferred_element_type=jnp.float32)
    for slot in range(slot_count):
        spot = where_ref[base * slot_count + slot]

        @pl.when(slot < live)
        def _():
            total_ref[spot] += terms_ref[:, slot * tile_size:(slot + 1) * tile_size]

    @pl.when((row == tile_rows - 1) & (half_id == halves - 1))
    def _():
        out_ref[...] = total_ref[...].astype(out_ref.dtype)


def spread_pair(
    core_id, spots, counts, tile_stack, grad_turned, buffer_tiles, out_type, start=None,
    block_step=2, core_step=1,
):
    _, tile_rows, slot_count, tile_size, _ = tile_stack.shape
    blocks = lax.axis_size("blk")
    hidden_width = grad_turned.shape[1]
    grid_spec = pltpu.PrefetchScalarGridSpec(
        num_scalar_prefetch=3,
        grid=(tile_rows, blocks // 2),
        in_specs=[
            pl.BlockSpec(
                (None, None, slot_count, tile_size, tile_size),
                lambda r, h, c, w, n: (h * block_step + c[0] * core_step, r, 0, 0, 0),
            ),
            pl.BlockSpec((None, hidden_width, tile_size), lambda r, h, c, w, n: (r, 0, 0)),
        ]
        + ([] if start is None else [pl.BlockSpec(start.shape, lambda r, h, c, w, n: (0, 0, 0))]),
        out_specs=pl.BlockSpec(
            (buffer_tiles, hidden_width, tile_size), lambda r, h, c, w, n: (0, 0, 0)
        ),
        scratch_shapes=[
            pltpu.VMEM((buffer_tiles, hidden_width, tile_size), jnp.float32),
            pltpu.VMEM((tile_size, slot_count * tile_size), tile_stack.dtype),
            pltpu.VMEM((hidden_width, slot_count * tile_size), jnp.float32),
        ],
    )
    return pl.pallas_call(
        spread_kernel,
        grid_spec=grid_spec,
        out_shape=jax.ShapeDtypeStruct((buffer_tiles, hidden_width, tile_size), out_type),
        compiler_params=pltpu.CompilerParams(dimension_semantics=("arbitrary", "arbitrary")),
    )(
        jnp.reshape(core_id, (1,)).astype(jnp.int32),
        spots,
        counts,
        tile_stack,
        grad_turned,
        *([] if start is None else [start]),
    )


def buffer_spots(tile_col, blk_id, feat_id, block_tiles, tiles_per_device):
    own = place_of(blk_id, feat_id)
    block = tile_col // block_tiles
    local = tile_col % block_tiles
    source_feat = local // tiles_per_device
    part = local % tiles_per_device
    source = place_of(block, source_feat)
    rel = {axis: (source[axis] - own[axis]) % RING for axis in ("y", "z", "x")}
    chunk = jnp.where(
        source["core"] == 0,
        rel["y"] * 16 + rel["z"] * 4 + rel["x"],
        rel["x"] * 16 + rel["z"] * 4 + rel["y"],
    )
    return (chunk * tiles_per_device + part).astype(jnp.int32)


def body(features_t, weight, tile_values, tile_col, tile_count, grad_out):
    cycle_size = lax.axis_size("blk")
    hidden_width = weight.shape[1]
    tile_size = tile_values.shape[1]
    rows_own = grad_out.shape[0]
    tile_rows = rows_own // tile_size
    block_rows = features_t.shape[1]
    block_tiles = block_rows // tile_size
    slot_count = tile_values.shape[0] // (cycle_size * tile_rows)
    feat_id = lax.axis_index("feat")
    blk_id = lax.axis_index("blk")
    core_id = blk_id % 2
    tile_stack = tile_values.reshape(cycle_size, tile_rows, slot_count, tile_size, tile_size)
    spots = buffer_spots(tile_col, blk_id, feat_id, block_tiles, tile_rows)
    sibling_tiles = sibling(tile_stack)
    sibling_spots = buffer_spots(sibling(tile_col), blk_id, feat_id, block_tiles, tile_rows)
    sibling_count = sibling(tile_count)
    buffer_tiles = block_tiles * 2

    features_own = lax.all_to_all(features_t, "feat", split_axis=1, concat_axis=0, tiled=True)
    projected = lax.dot_general(
        features_own, weight, (((0,), (0,)), ((), ())), preferred_element_type=jnp.float32
    ).astype(jnp.bfloat16)

    gathered = gather_phase_direct(projected, 0)
    gathered = gather_phase_direct(gathered, 1)
    gathered = gather_phase(gathered, 2)
    own_buffer = gathered.reshape(buffer_tiles, tile_size, hidden_width)
    other_buffer = sibling(own_buffer)
    aggregate_sum = aggregate_pair(core_id, spots, tile_count, tile_stack, own_buffer)
    aggregate_sum = aggregate_sum + aggregate_pair(
        1 - core_id, spots, tile_count, tile_stack, other_buffer
    )

    pre_act = aggregate_sum.reshape(rows_own, hidden_width)
    sigmoid_y = jax.nn.sigmoid(pre_act)
    activations = (pre_act * sigmoid_y).astype(jnp.bfloat16)
    grad_pre = (
        grad_out.astype(jnp.float32) * sigmoid_y * (1.0 + pre_act * (1.0 - sigmoid_y))
    ).astype(jnp.bfloat16)
    grad_turned = grad_pre.reshape(tile_rows, tile_size, hidden_width).transpose(0, 2, 1)

    sibling_grad = sibling(grad_turned)
    total = spread_pair(
        core_id, spots, tile_count, tile_stack, grad_turned, buffer_tiles, jnp.float32
    )
    total = spread_pair(
        core_id, sibling_spots, sibling_count, sibling_tiles, sibling_grad, buffer_tiles,
        jnp.float32, total,
    )
    total = reduce_phase(
        total.reshape(RING, RING, RING, rows_own, hidden_width), 2, jnp.bfloat16
    )
    total = reduce_phase_direct(total, 1, jnp.bfloat16)
    total = reduce_phase_direct(total, 0, jnp.bfloat16)
    grad_hidden = (
        total.reshape(tile_rows, hidden_width, tile_size)
        .transpose(0, 2, 1)
        .reshape(rows_own, hidden_width)
        .astype(jnp.bfloat16)
    )

    weight_term = jnp.dot(features_own, grad_hidden, preferred_element_type=jnp.float32)
    features_grad_local = lax.dot_general(
        weight, grad_hidden, (((1,), (1,)), ((), ())), preferred_element_type=jnp.float32
    ).astype(jnp.bfloat16)
    feat_count = lax.axis_size("feat")
    shard_rows = weight_term.shape[0] // feat_count
    outgoing = jnp.concatenate(
        [
            weight_term.reshape(feat_count, shard_rows, hidden_width),
            features_grad_local.astype(jnp.float32).reshape(feat_count, shard_rows, rows_own),
        ],
        axis=2,
    )
    got = lax.all_to_all(outgoing, "feat", split_axis=0, concat_axis=0, tiled=True)
    weight_part = jnp.sum(got[:, :, :hidden_width], axis=0)
    grad_features = (
        got[:, :, hidden_width:].astype(jnp.bfloat16).transpose(1, 0, 2).reshape(shard_rows, -1)
    )
    weight_part = weight_part + swapped(weight_part, "blk", 1)
    weight_part = weight_part + swapped(weight_part, "blk", 2)
    grad_weight = weight_part * lax.rsqrt(jnp.float32(block_rows * cycle_size))
    return (activations, grad_features, grad_weight)


def solution(mesh):
    placed = (
        P("feat", "blk"),
        P(),
        P(("blk", "feat"), None, None),
        P(("blk", "feat")),
        P(("blk", "feat")),
        P(("blk", "feat"), None),
    )
    return jax.shard_map(
        body,
        mesh=mesh,
        in_specs=placed,
        out_specs=(P(("blk", "feat"), None), P("feat", "blk"), P("feat", None)),
        check_vma=False,
    )
```

```python
import jax
import jax.numpy as jnp
from jax import lax
from jax.sharding import PartitionSpec as P
from jax.experimental import pallas as pl
from jax.experimental.pallas import tpu as pltpu

RING = 4
GATHER_ORDER = (("x", "z", "y"), ("y", "z", "x"))
BOTH = ("blk", "feat")


def place_of(blk, feat):
    return {
        "core": blk % 2,
        "y": (blk // 2) * 2 + feat // 16,
        "z": (feat // 4) % 4,
        "x": feat % 4,
    }


def linear_of(place):
    blk = (place["y"] // 2) * 2 + place["core"]
    feat = (place["y"] % 2) * 16 + place["z"] * 4 + place["x"]
    return blk * 32 + feat


def ring_shift(block, phase, distance):
    route = []
    for blk in range(4):
        for feat in range(32):
            place = place_of(blk, feat)
            axis = GATHER_ORDER[place["core"]][phase]
            target = dict(place)
            target[axis] = (place[axis] + distance) % RING
            route.append((linear_of(place), linear_of(target)))
    return lax.ppermute(block, BOTH, route)


def sibling(block):
    return lax.ppermute(block, "blk", [(i, i ^ 1) for i in range(lax.axis_size("blk"))])


def swapped(block, axis, mask):
    count = lax.axis_size(axis)
    return lax.ppermute(block, axis, [(i, i ^ mask) for i in range(count)])


def gather_phase(block, phase):
    half = block.shape[-2] // 2
    from_minus = ring_shift(block, phase, 1)
    from_plus = ring_shift(block, phase, -1)
    far_low = ring_shift(from_minus[..., :half, :], phase, 1)
    far_high = ring_shift(from_plus[..., half:, :], phase, -1)
    far = jnp.concatenate([far_low, far_high], axis=-2)
    return jnp.stack([block, from_plus, far, from_minus])


def gather_phase_direct(block, phase):
    from_minus = ring_shift(block, phase, 1)
    from_plus = ring_shift(block, phase, -1)
    far = ring_shift(block, phase, 2)
    return jnp.stack([block, from_plus, far, from_minus])


def reduce_phase_direct(total, phase, wire_type):
    from_minus = ring_shift(total[1].astype(wire_type), phase, 1)
    from_plus = ring_shift(total[3].astype(wire_type), phase, -1)
    far = ring_shift(total[2].astype(wire_type), phase, 2)
    return (
        total[0]
        + from_minus.astype(jnp.float32)
        + from_plus.astype(jnp.float32)
        + far.astype(jnp.float32)
    )


def reduce_phase(total, phase, wire_type, extra=None):
    half = total.shape[-2] // 2

    def term(k):
        if extra is None:
            return total[k]
        return total[k] + extra[k].astype(jnp.float32)

    far = term(2)
    got_minus = ring_shift(far[..., :half, :].astype(wire_type), phase, 1)
    got_plus = ring_shift(far[..., half:, :].astype(wire_type), phase, -1)
    ahead = term(1)
    ahead = jnp.concatenate(
        [ahead[..., :half, :] + got_minus.astype(jnp.float32), ahead[..., half:, :]], axis=-2
    )
    behind = term(3)
    behind = jnp.concatenate(
        [behind[..., :half, :], behind[..., half:, :] + got_plus.astype(jnp.float32)], axis=-2
    )
    from_minus = ring_shift(ahead.astype(wire_type), phase, 1)
    from_plus = ring_shift(behind.astype(wire_type), phase, -1)
    return term(0) + from_minus.astype(jnp.float32) + from_plus.astype(jnp.float32)


def scatter_rows(total, axis, wire_type):
    count = lax.axis_size(axis)
    index = lax.axis_index(axis)
    mask = count // 2
    while mask >= 1:
        half = total.shape[0] // 2
        lower, upper_part = total[:half], total[half:]
        upper = (index // mask) % 2 == 1
        keep = jnp.where(upper, upper_part, lower)
        send = jnp.where(upper, lower, upper_part)
        got = swapped(send.astype(wire_type), axis, mask)
        total = keep + got.astype(jnp.float32)
        mask //= 2
    return total


def aggregate_kernel(core_ref, where_ref, count_ref, tiles_ref, proj_ref, out_ref, wide_ref, picked_ref):
    row = pl.program_id(0)
    half_id = pl.program_id(1)
    tile_rows = pl.num_programs(0)
    slot_count, tile_size, _ = tiles_ref.shape
    base = (half_id * 2 + core_ref[0]) * tile_rows + row
    live = count_ref[base]
    for slot in range(slot_count):
        wide_ref[:, slot * tile_size:(slot + 1) * tile_size] = tiles_ref[slot]
        piece = proj_ref[where_ref[base * slot_count + slot]]
        picked_ref[slot * tile_size:(slot + 1) * tile_size, :] = jnp.where(
            slot < live, piece, jnp.zeros_like(piece)
        )
    part = jnp.dot(wide_ref[...], picked_ref[...], preferred_element_type=jnp.float32)

    @pl.when(half_id == 0)
    def _():
        out_ref[...] = part

    @pl.when(half_id != 0)
    def _():
        out_ref[...] += part


def aggregate_pair(core_id, spots, counts, tile_stack, buffer):
    blocks, tile_rows, slot_count, tile_size, _ = tile_stack.shape
    hidden_width = buffer.shape[-1]
    grid_spec = pltpu.PrefetchScalarGridSpec(
        num_scalar_prefetch=3,
        grid=(tile_rows, blocks // 2),
        in_specs=[
            pl.BlockSpec(
                (None, None, slot_count, tile_size, tile_size),
                lambda r, h, c, w, n: (h * 2 + c[0], r, 0, 0, 0),
            ),
            pl.BlockSpec(buffer.shape, lambda r, h, c, w, n: (0, 0, 0)),
        ],
        out_specs=pl.BlockSpec((None, tile_size, hidden_width), lambda r, h, c, w, n: (r, 0, 0)),
        scratch_shapes=[
            pltpu.VMEM((tile_size, slot_count * tile_size), tile_stack.dtype),
            pltpu.VMEM((slot_count * tile_size, hidden_width), buffer.dtype),
        ],
    )
    return pl.pallas_call(
        aggregate_kernel,
        grid_spec=grid_spec,
        out_shape=jax.ShapeDtypeStruct((tile_rows, tile_size, hidden_width), jnp.float32),
        compiler_params=pltpu.CompilerParams(dimension_semantics=("arbitrary", "arbitrary")),
    )(jnp.reshape(core_id, (1,)).astype(jnp.int32), spots, counts, tile_stack, buffer)


def spread_pair(core_id, spots, counts, tile_stack, sibling_tiles, grads, buffer_tiles):
    blocks, tile_rows, slot_count, tile_size, _ = tile_stack.shape
    hidden_width = grads.shape[2]
    halves = blocks // 2
    last = halves - 1

    def own_map(s, r, h, c, w, n):
        return (
            jnp.where(s == 0, h * 2 + c[0], last * 2 + c[0]),
            jnp.where(s == 0, r, tile_rows - 1),
            0, 0, 0,
        )

    def sibling_map(s, r, h, c, w, n):
        return (jnp.where(s == 1, h * 2 + c[0], c[0]), jnp.where(s == 1, r, 0), 0, 0, 0)

    def kernel(core_ref, where_ref, count_ref, own_ref, other_ref, grad_ref, out_ref, total_ref,
               wide_ref, terms_ref):
        source = pl.program_id(0)
        row = pl.program_id(1)
        half_id = pl.program_id(2)
        base = (half_id * 2 + core_ref[0]) * tile_rows + row
        live = count_ref[source * blocks * tile_rows + base]

        @pl.when((source == 0) & (row == 0) & (half_id == 0))
        def _():
            total_ref[...] = jnp.zeros(total_ref.shape, jnp.float32)

        def fill(tiles_ref):
            for slot in range(slot_count):
                wide_ref[:, slot * tile_size:(slot + 1) * tile_size] = tiles_ref[slot]

        pl.when(source == 0)(lambda: fill(own_ref))
        pl.when(source == 1)(lambda: fill(other_ref))
        terms_ref[...] = jnp.dot(grad_ref[...], wide_ref[...], preferred_element_type=jnp.float32)
        for slot in range(slot_count):
            spot = where_ref[(source * blocks * tile_rows + base) * slot_count + slot]

            @pl.when(slot < live)
            def _():
                total_ref[spot] += terms_ref[:, slot * tile_size:(slot + 1) * tile_size]

        @pl.when((source == 1) & (row == tile_rows - 1) & (half_id == halves - 1))
        def _():
            out_ref[...] = total_ref[...]

    tile_spec = (None, None, slot_count, tile_size, tile_size)
    grid_spec = pltpu.PrefetchScalarGridSpec(
        num_scalar_prefetch=3,
        grid=(2, tile_rows, halves),
        in_specs=[
            pl.BlockSpec(tile_spec, own_map),
            pl.BlockSpec(tile_spec, sibling_map),
            pl.BlockSpec(
                (None, None, hidden_width, tile_size), lambda s, r, h, c, w, n: (s, r, 0, 0)
            ),
        ],
        out_specs=pl.BlockSpec(
            (buffer_tiles, hidden_width, tile_size), lambda s, r, h, c, w, n: (0, 0, 0)
        ),
        scratch_shapes=[
            pltpu.VMEM((buffer_tiles, hidden_width, tile_size), jnp.float32),
            pltpu.VMEM((tile_size, slot_count * tile_size), tile_stack.dtype),
            pltpu.VMEM((hidden_width, slot_count * tile_size), jnp.float32),
        ],
    )
    return pl.pallas_call(
        kernel,
        grid_spec=grid_spec,
        out_shape=jax.ShapeDtypeStruct((buffer_tiles, hidden_width, tile_size), jnp.float32),
        compiler_params=pltpu.CompilerParams(
            dimension_semantics=("arbitrary", "arbitrary", "arbitrary")
        ),
    )(
        jnp.reshape(core_id, (1,)).astype(jnp.int32),
        spots,
        counts,
        tile_stack,
        sibling_tiles,
        grads,
    )


def buffer_spots(tile_col, blk_id, feat_id, block_tiles, tiles_per_device):
    own = place_of(blk_id, feat_id)
    block = tile_col // block_tiles
    local = tile_col % block_tiles
    source_feat = local // tiles_per_device
    part = local % tiles_per_device
    source = place_of(block, source_feat)
    rel = {axis: (source[axis] - own[axis]) % RING for axis in ("y", "z", "x")}
    chunk = jnp.where(
        source["core"] == 0,
        rel["y"] * 16 + rel["z"] * 4 + rel["x"],
        rel["x"] * 16 + rel["z"] * 4 + rel["y"],
    )
    return (chunk * tiles_per_device + part).astype(jnp.int32)


def body(features_t, weight, tile_values, tile_col, tile_count, grad_out):
    cycle_size = lax.axis_size("blk")
    hidden_width = weight.shape[1]
    tile_size = tile_values.shape[1]
    rows_own = grad_out.shape[0]
    tile_rows = rows_own // tile_size
    block_rows = features_t.shape[1]
    block_tiles = block_rows // tile_size
    slot_count = tile_values.shape[0] // (cycle_size * tile_rows)
    feat_id = lax.axis_index("feat")
    blk_id = lax.axis_index("blk")
    core_id = blk_id % 2
    tile_stack = tile_values.reshape(cycle_size, tile_rows, slot_count, tile_size, tile_size)
    spots = buffer_spots(tile_col, blk_id, feat_id, block_tiles, tile_rows)
    sibling_tiles = sibling(tile_stack)
    sibling_spots = buffer_spots(sibling(tile_col), blk_id, feat_id, block_tiles, tile_rows)
    sibling_count = sibling(tile_count)
    buffer_tiles = block_tiles * 2

    features_own = lax.all_to_all(features_t, "feat", split_axis=1, concat_axis=0, tiled=True)
    projected = lax.dot_general(
        features_own, weight, (((0,), (0,)), ((), ())), preferred_element_type=jnp.float32
    ).astype(jnp.bfloat16)

    gathered = gather_phase_direct(projected, 0)
    gathered = gather_phase_direct(gathered, 1)
    gathered = gather_phase(gathered, 2)
    own_buffer = gathered.reshape(buffer_tiles, tile_size, hidden_width)
    other_buffer = sibling(own_buffer)
    aggregate_sum = aggregate_pair(core_id, spots, tile_count, tile_stack, own_buffer)
    aggregate_sum = aggregate_sum + aggregate_pair(
        1 - core_id, spots, tile_count, tile_stack, other_buffer
    )

    pre_act = aggregate_sum.reshape(rows_own, hidden_width)
    sigmoid_y = jax.nn.sigmoid(pre_act)
    activations = (pre_act * sigmoid_y).astype(jnp.bfloat16)
    grad_pre = (
        grad_out.astype(jnp.float32) * sigmoid_y * (1.0 + pre_act * (1.0 - sigmoid_y))
    ).astype(jnp.bfloat16)
    grad_turned = grad_pre.reshape(tile_rows, tile_size, hidden_width).transpose(0, 2, 1)

    sibling_grad = sibling(grad_turned)
    total = spread_pair(
        core_id,
        jnp.concatenate([spots, sibling_spots]),
        jnp.concatenate([tile_count, sibling_count]),
        tile_stack,
        sibling_tiles,
        jnp.stack([grad_turned, sibling_grad]),
        buffer_tiles,
    )
    total = reduce_phase(
        total.reshape(RING, RING, RING, rows_own, hidden_width), 2, jnp.bfloat16
    )
    total = reduce_phase_direct(total, 1, jnp.bfloat16)
    total = reduce_phase_direct(total, 0, jnp.bfloat16)
    grad_hidden = (
        total.reshape(tile_rows, hidden_width, tile_size)
        .transpose(0, 2, 1)
        .reshape(rows_own, hidden_width)
        .astype(jnp.bfloat16)
    )

    weight_term = jnp.dot(features_own, grad_hidden, preferred_element_type=jnp.float32)
    features_grad_local = lax.dot_general(
        weight, grad_hidden, (((1,), (1,)), ((), ())), preferred_element_type=jnp.float32
    ).astype(jnp.bfloat16)
    feat_count = lax.axis_size("feat")
    shard_rows = weight_term.shape[0] // feat_count
    outgoing = jnp.concatenate(
        [
            weight_term.reshape(feat_count, shard_rows, hidden_width),
            features_grad_local.astype(jnp.float32).reshape(feat_count, shard_rows, rows_own),
        ],
        axis=2,
    )
    got = lax.all_to_all(outgoing, "feat", split_axis=0, concat_axis=0, tiled=True)
    weight_part = jnp.sum(got[:, :, :hidden_width], axis=0)
    grad_features = (
        got[:, :, hidden_width:].astype(jnp.bfloat16).transpose(1, 0, 2).reshape(shard_rows, -1)
    )
    weight_part = weight_part + swapped(weight_part, "blk", 1)
    weight_part = weight_part + swapped(weight_part, "blk", 2)
    grad_weight = weight_part * lax.rsqrt(jnp.float32(block_rows * cycle_size))
    return (activations, grad_features, grad_weight)


def solution(mesh):
    placed = (
        P("feat", "blk"),
        P(),
        P(("blk", "feat"), None, None),
        P(("blk", "feat")),
        P(("blk", "feat")),
        P(("blk", "feat"), None),
    )
    return jax.shard_map(
        body,
        mesh=mesh,
        in_specs=placed,
        out_specs=(P(("blk", "feat"), None), P("feat", "blk"), P("feat", None)),
        check_vma=False,
    )
```

```python
import jax
import jax.numpy as jnp
from jax import lax
from jax.sharding import PartitionSpec as P
from jax.experimental import pallas as pl
from jax.experimental.pallas import tpu as pltpu

RING = 4
GATHER_ORDER = (("x", "z", "y"), ("y", "z", "x"))
BOTH = ("blk", "feat")


def place_of(blk, feat):
    return {
        "core": blk % 2,
        "y": (blk // 2) * 2 + feat // 16,
        "z": (feat // 4) % 4,
        "x": feat % 4,
    }


def linear_of(place):
    blk = (place["y"] // 2) * 2 + place["core"]
    feat = (place["y"] % 2) * 16 + place["z"] * 4 + place["x"]
    return blk * 32 + feat


def ring_shift(block, phase, distance):
    route = []
    for blk in range(4):
        for feat in range(32):
            place = place_of(blk, feat)
            axis = GATHER_ORDER[place["core"]][phase]
            target = dict(place)
            target[axis] = (place[axis] + distance) % RING
            route.append((linear_of(place), linear_of(target)))
    return lax.ppermute(block, BOTH, route)


def sibling(block):
    return lax.ppermute(block, "blk", [(i, i ^ 1) for i in range(lax.axis_size("blk"))])


def swapped(block, axis, mask):
    count = lax.axis_size(axis)
    return lax.ppermute(block, axis, [(i, i ^ mask) for i in range(count)])


def gather_phase(block, phase):
    half = block.shape[-2] // 2
    from_minus = ring_shift(block, phase, 1)
    from_plus = ring_shift(block, phase, -1)
    far_low = ring_shift(from_minus[..., :half, :], phase, 1)
    far_high = ring_shift(from_plus[..., half:, :], phase, -1)
    far = jnp.concatenate([far_low, far_high], axis=-2)
    return jnp.stack([block, from_plus, far, from_minus])


def gather_phase_direct(block, phase):
    from_minus = ring_shift(block, phase, 1)
    from_plus = ring_shift(block, phase, -1)
    far = ring_shift(block, phase, 2)
    return jnp.stack([block, from_plus, far, from_minus])


def reduce_phase_direct(total, phase, wire_type):
    from_minus = ring_shift(total[1].astype(wire_type), phase, 1)
    from_plus = ring_shift(total[3].astype(wire_type), phase, -1)
    far = ring_shift(total[2].astype(wire_type), phase, 2)
    return (
        total[0]
        + from_minus.astype(jnp.float32)
        + from_plus.astype(jnp.float32)
        + far.astype(jnp.float32)
    )


def reduce_phase(total, phase, wire_type, extra=None):
    half = total.shape[-2] // 2

    def term(k):
        if extra is None:
            return total[k]
        return total[k] + extra[k].astype(jnp.float32)

    far = term(2)
    got_minus = ring_shift(far[..., :half, :].astype(wire_type), phase, 1)
    got_plus = ring_shift(far[..., half:, :].astype(wire_type), phase, -1)
    ahead = term(1)
    ahead = jnp.concatenate(
        [ahead[..., :half, :] + got_minus.astype(jnp.float32), ahead[..., half:, :]], axis=-2
    )
    behind = term(3)
    behind = jnp.concatenate(
        [behind[..., :half, :], behind[..., half:, :] + got_plus.astype(jnp.float32)], axis=-2
    )
    from_minus = ring_shift(ahead.astype(wire_type), phase, 1)
    from_plus = ring_shift(behind.astype(wire_type), phase, -1)
    return term(0) + from_minus.astype(jnp.float32) + from_plus.astype(jnp.float32)


def scatter_rows(total, axis, wire_type):
    count = lax.axis_size(axis)
    index = lax.axis_index(axis)
    mask = count // 2
    while mask >= 1:
        half = total.shape[0] // 2
        lower, upper_part = total[:half], total[half:]
        upper = (index // mask) % 2 == 1
        keep = jnp.where(upper, upper_part, lower)
        send = jnp.where(upper, lower, upper_part)
        got = swapped(send.astype(wire_type), axis, mask)
        total = keep + got.astype(jnp.float32)
        mask //= 2
    return total


def aggregate_kernel(core_ref, where_ref, count_ref, tiles_ref, proj_ref, out_ref, wide_ref, picked_ref):
    row = pl.program_id(0)
    half_id = pl.program_id(1)
    tile_rows = pl.num_programs(0)
    slot_count, tile_size, _ = tiles_ref.shape
    base = (half_id * 2 + core_ref[0]) * tile_rows + row
    live = count_ref[base]
    for slot in range(slot_count):
        wide_ref[:, slot * tile_size:(slot + 1) * tile_size] = tiles_ref[slot]
        piece = proj_ref[where_ref[base * slot_count + slot]]
        picked_ref[slot * tile_size:(slot + 1) * tile_size, :] = jnp.where(
            slot < live, piece, jnp.zeros_like(piece)
        )
    part = jnp.dot(wide_ref[...], picked_ref[...], preferred_element_type=jnp.float32)

    @pl.when(half_id == 0)
    def _():
        out_ref[...] = part

    @pl.when(half_id != 0)
    def _():
        out_ref[...] += part


def aggregate_pair(core_id, spots, counts, tile_stack, buffer):
    blocks, tile_rows, slot_count, tile_size, _ = tile_stack.shape
    hidden_width = buffer.shape[-1]
    grid_spec = pltpu.PrefetchScalarGridSpec(
        num_scalar_prefetch=3,
        grid=(tile_rows, blocks // 2),
        in_specs=[
            pl.BlockSpec(
                (None, None, slot_count, tile_size, tile_size),
                lambda r, h, c, w, n: (h * 2 + c[0], r, 0, 0, 0),
            ),
            pl.BlockSpec(buffer.shape, lambda r, h, c, w, n: (0, 0, 0)),
        ],
        out_specs=pl.BlockSpec((None, tile_size, hidden_width), lambda r, h, c, w, n: (r, 0, 0)),
        scratch_shapes=[
            pltpu.VMEM((tile_size, slot_count * tile_size), tile_stack.dtype),
            pltpu.VMEM((slot_count * tile_size, hidden_width), buffer.dtype),
        ],
    )
    return pl.pallas_call(
        aggregate_kernel,
        grid_spec=grid_spec,
        out_shape=jax.ShapeDtypeStruct((tile_rows, tile_size, hidden_width), jnp.float32),
        compiler_params=pltpu.CompilerParams(dimension_semantics=("arbitrary", "arbitrary")),
    )(jnp.reshape(core_id, (1,)).astype(jnp.int32), spots, counts, tile_stack, buffer)


def spread_pair(core_id, spots, counts, tile_stack, sibling_tiles, grads, buffer_tiles):
    blocks, tile_rows, slot_count, tile_size, _ = tile_stack.shape
    hidden_width = grads.shape[2]
    halves = blocks // 2
    last = halves - 1

    def own_map(s, r, h, c, w, n):
        return (
            jnp.where(s == 0, h * 2 + c[0], last * 2 + c[0]),
            jnp.where(s == 0, r, tile_rows - 1),
            0, 0, 0,
        )

    def sibling_map(s, r, h, c, w, n):
        return (jnp.where(s == 1, h * 2 + c[0], c[0]), jnp.where(s == 1, r, 0), 0, 0, 0)

    def kernel(core_ref, where_ref, count_ref, own_ref, other_ref, grad_ref, out_ref, total_ref,
               wide_ref, terms_ref):
        source = pl.program_id(0)
        row = pl.program_id(1)
        half_id = pl.program_id(2)
        base = (half_id * 2 + core_ref[0]) * tile_rows + row
        live = count_ref[source * blocks * tile_rows + base]

        @pl.when((source == 0) & (row == 0) & (half_id == 0))
        def _():
            total_ref[...] = jnp.zeros(total_ref.shape, jnp.float32)

        def fill(tiles_ref):
            for slot in range(slot_count):
                wide_ref[:, slot * tile_size:(slot + 1) * tile_size] = tiles_ref[slot]

        pl.when(source == 0)(lambda: fill(own_ref))
        pl.when(source == 1)(lambda: fill(other_ref))
        terms_ref[...] = jnp.dot(grad_ref[...], wide_ref[...], preferred_element_type=jnp.float32)
        for slot in range(slot_count):
            spot = where_ref[(source * blocks * tile_rows + base) * slot_count + slot]

            @pl.when(slot < live)
            def _():
                total_ref[spot] += terms_ref[:, slot * tile_size:(slot + 1) * tile_size]

        @pl.when((source == 1) & (row == tile_rows - 1) & (half_id == halves - 1))
        def _():
            out_ref[...] = total_ref[...]

    tile_spec = (None, None, slot_count, tile_size, tile_size)
    grid_spec = pltpu.PrefetchScalarGridSpec(
        num_scalar_prefetch=3,
        grid=(2, tile_rows, halves),
        in_specs=[
            pl.BlockSpec(tile_spec, own_map),
            pl.BlockSpec(tile_spec, sibling_map),
            pl.BlockSpec(
                (None, None, hidden_width, tile_size), lambda s, r, h, c, w, n: (s, r, 0, 0)
            ),
        ],
        out_specs=pl.BlockSpec(
            (buffer_tiles, hidden_width, tile_size), lambda s, r, h, c, w, n: (0, 0, 0)
        ),
        scratch_shapes=[
            pltpu.VMEM((buffer_tiles, hidden_width, tile_size), jnp.float32),
            pltpu.VMEM((tile_size, slot_count * tile_size), tile_stack.dtype),
            pltpu.VMEM((hidden_width, slot_count * tile_size), jnp.float32),
        ],
    )
    return pl.pallas_call(
        kernel,
        grid_spec=grid_spec,
        out_shape=jax.ShapeDtypeStruct((buffer_tiles, hidden_width, tile_size), jnp.float32),
        compiler_params=pltpu.CompilerParams(
            dimension_semantics=("arbitrary", "arbitrary", "arbitrary")
        ),
    )(
        jnp.reshape(core_id, (1,)).astype(jnp.int32),
        spots,
        counts,
        tile_stack,
        sibling_tiles,
        grads,
    )


def buffer_spots(tile_col, blk_id, feat_id, block_tiles, tiles_per_device):
    own = place_of(blk_id, feat_id)
    block = tile_col // block_tiles
    local = tile_col % block_tiles
    source_feat = local // tiles_per_device
    part = local % tiles_per_device
    source = place_of(block, source_feat)
    rel = {axis: (source[axis] - own[axis]) % RING for axis in ("y", "z", "x")}
    chunk = jnp.where(
        source["core"] == 0,
        rel["y"] * 16 + rel["z"] * 4 + rel["x"],
        rel["x"] * 16 + rel["z"] * 4 + rel["y"],
    )
    return (chunk * tiles_per_device + part).astype(jnp.int32)


def body(features_t, weight, tile_values, tile_col, tile_count, grad_out):
    cycle_size = lax.axis_size("blk")
    hidden_width = weight.shape[1]
    tile_size = tile_values.shape[1]
    rows_own = grad_out.shape[0]
    tile_rows = rows_own // tile_size
    block_rows = features_t.shape[1]
    block_tiles = block_rows // tile_size
    slot_count = tile_values.shape[0] // (cycle_size * tile_rows)
    feat_id = lax.axis_index("feat")
    blk_id = lax.axis_index("blk")
    core_id = blk_id % 2
    tile_stack = tile_values.reshape(cycle_size, tile_rows, slot_count, tile_size, tile_size)
    spots = buffer_spots(tile_col, blk_id, feat_id, block_tiles, tile_rows)
    sibling_tiles = sibling(tile_stack)
    sibling_col = sibling(tile_col)
    sibling_count = sibling(tile_count)
    buffer_tiles = block_tiles * 2

    features_own = lax.all_to_all(features_t, "feat", split_axis=1, concat_axis=0, tiled=True)
    projected = lax.dot_general(
        features_own, weight, (((0,), (0,)), ((), ())), preferred_element_type=jnp.float32
    ).astype(jnp.bfloat16)

    sibling_col, sibling_count, projected = lax.optimization_barrier(
        (sibling_col, sibling_count, projected)
    )
    sibling_spots = buffer_spots(sibling_col, blk_id, feat_id, block_tiles, tile_rows)
    gathered = gather_phase_direct(projected, 0)
    gathered = gather_phase_direct(gathered, 1)
    gathered = gather_phase(gathered, 2)
    own_buffer = gathered.reshape(buffer_tiles, tile_size, hidden_width)
    other_buffer = sibling(own_buffer)
    aggregate_sum = aggregate_pair(core_id, spots, tile_count, tile_stack, own_buffer)
    aggregate_sum = aggregate_sum + aggregate_pair(
        1 - core_id, spots, tile_count, tile_stack, other_buffer
    )

    pre_act = aggregate_sum.reshape(rows_own, hidden_width)
    sigmoid_y = jax.nn.sigmoid(pre_act)
    activations = (pre_act * sigmoid_y).astype(jnp.bfloat16)
    grad_pre = (
        grad_out.astype(jnp.float32) * sigmoid_y * (1.0 + pre_act * (1.0 - sigmoid_y))
    ).astype(jnp.bfloat16)
    grad_turned = grad_pre.reshape(tile_rows, tile_size, hidden_width).transpose(0, 2, 1)

    sibling_grad = sibling(grad_turned)
    total = spread_pair(
        core_id,
        jnp.concatenate([spots, sibling_spots]),
        jnp.concatenate([tile_count, sibling_count]),
        tile_stack,
        sibling_tiles,
        jnp.stack([grad_turned, sibling_grad]),
        buffer_tiles,
    )
    total = reduce_phase(
        total.reshape(RING, RING, RING, rows_own, hidden_width), 2, jnp.bfloat16
    )
    total = reduce_phase_direct(total, 1, jnp.bfloat16)
    total = reduce_phase_direct(total, 0, jnp.bfloat16)
    grad_hidden = (
        total.reshape(tile_rows, hidden_width, tile_size)
        .transpose(0, 2, 1)
        .reshape(rows_own, hidden_width)
        .astype(jnp.bfloat16)
    )

    weight_term = jnp.dot(features_own, grad_hidden, preferred_element_type=jnp.float32)
    features_grad_local = lax.dot_general(
        weight, grad_hidden, (((1,), (1,)), ((), ())), preferred_element_type=jnp.float32
    ).astype(jnp.bfloat16)
    feat_count = lax.axis_size("feat")
    shard_rows = weight_term.shape[0] // feat_count
    outgoing = jnp.concatenate(
        [
            weight_term.reshape(feat_count, shard_rows, hidden_width),
            features_grad_local.astype(jnp.float32).reshape(feat_count, shard_rows, rows_own),
        ],
        axis=2,
    )
    got = lax.all_to_all(outgoing, "feat", split_axis=0, concat_axis=0, tiled=True)
    weight_part = jnp.sum(got[:, :, :hidden_width], axis=0)
    grad_features = (
        got[:, :, hidden_width:].astype(jnp.bfloat16).transpose(1, 0, 2).reshape(shard_rows, -1)
    )
    weight_part = weight_part + swapped(weight_part, "blk", 1)
    weight_part = weight_part + swapped(weight_part, "blk", 2)
    grad_weight = weight_part * lax.rsqrt(jnp.float32(block_rows * cycle_size))
    return (activations, grad_features, grad_weight)


def solution(mesh):
    placed = (
        P("feat", "blk"),
        P(),
        P(("blk", "feat"), None, None),
        P(("blk", "feat")),
        P(("blk", "feat")),
        P(("blk", "feat"), None),
    )
    return jax.shard_map(
        body,
        mesh=mesh,
        in_specs=placed,
        out_specs=(P(("blk", "feat"), None), P("feat", "blk"), P("feat", None)),
        check_vma=False,
    )
```

```python
import jax
import jax.numpy as jnp
from jax import lax
from jax.sharding import PartitionSpec as P
from jax.experimental import pallas as pl
from jax.experimental.pallas import tpu as pltpu

RING = 4
GATHER_ORDER = (("x", "z", "y"), ("y", "z", "x"))
BOTH = ("blk", "feat")


def place_of(blk, feat):
    return {
        "core": blk % 2,
        "y": (blk // 2) * 2 + feat // 16,
        "z": (feat // 4) % 4,
        "x": feat % 4,
    }


def linear_of(place):
    blk = (place["y"] // 2) * 2 + place["core"]
    feat = (place["y"] % 2) * 16 + place["z"] * 4 + place["x"]
    return blk * 32 + feat


def ring_shift(block, phase, distance):
    route = []
    for blk in range(4):
        for feat in range(32):
            place = place_of(blk, feat)
            axis = GATHER_ORDER[place["core"]][phase]
            target = dict(place)
            target[axis] = (place[axis] + distance) % RING
            route.append((linear_of(place), linear_of(target)))
    return lax.ppermute(block, BOTH, route)


def sibling(block):
    return lax.ppermute(block, "blk", [(i, i ^ 1) for i in range(lax.axis_size("blk"))])


def swapped(block, axis, mask):
    count = lax.axis_size(axis)
    return lax.ppermute(block, axis, [(i, i ^ mask) for i in range(count)])


def gather_phase(block, phase):
    half = block.shape[-2] // 2
    from_minus = ring_shift(block, phase, 1)
    from_plus = ring_shift(block, phase, -1)
    far_low = ring_shift(from_minus[..., :half, :], phase, 1)
    far_high = ring_shift(from_plus[..., half:, :], phase, -1)
    far = jnp.concatenate([far_low, far_high], axis=-2)
    return jnp.stack([block, from_plus, far, from_minus])


def gather_phase_direct(block, phase):
    from_minus = ring_shift(block, phase, 1)
    from_plus = ring_shift(block, phase, -1)
    far = ring_shift(block, phase, 2)
    return jnp.stack([block, from_plus, far, from_minus])


def reduce_phase_direct(total, phase, wire_type):
    from_minus = ring_shift(total[1].astype(wire_type), phase, 1)
    from_plus = ring_shift(total[3].astype(wire_type), phase, -1)
    far = ring_shift(total[2].astype(wire_type), phase, 2)
    return (
        total[0]
        + from_minus.astype(jnp.float32)
        + from_plus.astype(jnp.float32)
        + far.astype(jnp.float32)
    )


def reduce_phase(total, phase, wire_type, extra=None):
    half = total.shape[-2] // 2

    def term(k):
        if extra is None:
            return total[k]
        return total[k] + extra[k].astype(jnp.float32)

    far = term(2)
    got_minus = ring_shift(far[..., :half, :].astype(wire_type), phase, 1)
    got_plus = ring_shift(far[..., half:, :].astype(wire_type), phase, -1)
    ahead = term(1)
    ahead = jnp.concatenate(
        [ahead[..., :half, :] + got_minus.astype(jnp.float32), ahead[..., half:, :]], axis=-2
    )
    behind = term(3)
    behind = jnp.concatenate(
        [behind[..., :half, :], behind[..., half:, :] + got_plus.astype(jnp.float32)], axis=-2
    )
    from_minus = ring_shift(ahead.astype(wire_type), phase, 1)
    from_plus = ring_shift(behind.astype(wire_type), phase, -1)
    return term(0) + from_minus.astype(jnp.float32) + from_plus.astype(jnp.float32)


def scatter_rows(total, axis, wire_type):
    count = lax.axis_size(axis)
    index = lax.axis_index(axis)
    mask = count // 2
    while mask >= 1:
        half = total.shape[0] // 2
        lower, upper_part = total[:half], total[half:]
        upper = (index // mask) % 2 == 1
        keep = jnp.where(upper, upper_part, lower)
        send = jnp.where(upper, lower, upper_part)
        got = swapped(send.astype(wire_type), axis, mask)
        total = keep + got.astype(jnp.float32)
        mask //= 2
    return total


def aggregate_kernel(core_ref, where_ref, count_ref, tiles_ref, proj_ref, out_ref, wide_ref, picked_ref):
    row = pl.program_id(0)
    half_id = pl.program_id(1)
    tile_rows = pl.num_programs(0)
    slot_count, tile_size, _ = tiles_ref.shape
    base = (half_id * 2 + core_ref[0]) * tile_rows + row
    live = count_ref[base]
    for slot in range(slot_count):
        wide_ref[:, slot * tile_size:(slot + 1) * tile_size] = tiles_ref[slot]
        piece = proj_ref[where_ref[base * slot_count + slot]]
        picked_ref[slot * tile_size:(slot + 1) * tile_size, :] = jnp.where(
            slot < live, piece, jnp.zeros_like(piece)
        )
    part = jnp.dot(wide_ref[...], picked_ref[...], preferred_element_type=jnp.float32)

    @pl.when(half_id == 0)
    def _():
        out_ref[...] = part

    @pl.when(half_id != 0)
    def _():
        out_ref[...] += part


def aggregate_pair(core_id, spots, counts, tile_stack, buffer):
    blocks, tile_rows, slot_count, tile_size, _ = tile_stack.shape
    hidden_width = buffer.shape[-1]
    grid_spec = pltpu.PrefetchScalarGridSpec(
        num_scalar_prefetch=3,
        grid=(tile_rows, blocks // 2),
        in_specs=[
            pl.BlockSpec(
                (None, None, slot_count, tile_size, tile_size),
                lambda r, h, c, w, n: (h * 2 + c[0], r, 0, 0, 0),
            ),
            pl.BlockSpec(buffer.shape, lambda r, h, c, w, n: (0, 0, 0)),
        ],
        out_specs=pl.BlockSpec((None, tile_size, hidden_width), lambda r, h, c, w, n: (r, 0, 0)),
        scratch_shapes=[
            pltpu.VMEM((tile_size, slot_count * tile_size), tile_stack.dtype),
            pltpu.VMEM((slot_count * tile_size, hidden_width), buffer.dtype),
        ],
    )
    return pl.pallas_call(
        aggregate_kernel,
        grid_spec=grid_spec,
        out_shape=jax.ShapeDtypeStruct((tile_rows, tile_size, hidden_width), jnp.float32),
        compiler_params=pltpu.CompilerParams(dimension_semantics=("arbitrary", "arbitrary")),
    )(jnp.reshape(core_id, (1,)).astype(jnp.int32), spots, counts, tile_stack, buffer)


def spread_pair(core_id, spots, counts, tile_stack, sibling_tiles, grads, buffer_tiles):
    blocks, tile_rows, slot_count, tile_size, _ = tile_stack.shape
    hidden_width = grads.shape[2]
    halves = blocks // 2
    last = halves - 1

    def own_map(s, r, h, c, w, n):
        return (
            jnp.where(s == 0, h * 2 + c[0], last * 2 + c[0]),
            jnp.where(s == 0, r, tile_rows - 1),
            0, 0, 0,
        )

    def sibling_map(s, r, h, c, w, n):
        return (jnp.where(s == 1, h * 2 + c[0], c[0]), jnp.where(s == 1, r, 0), 0, 0, 0)

    def kernel(core_ref, where_ref, count_ref, own_ref, other_ref, grad_ref, out_ref, total_ref,
               wide_ref, terms_ref):
        source = pl.program_id(0)
        row = pl.program_id(1)
        half_id = pl.program_id(2)
        base = (half_id * 2 + core_ref[0]) * tile_rows + row
        live = count_ref[source * blocks * tile_rows + base]

        @pl.when((source == 0) & (row == 0) & (half_id == 0))
        def _():
            total_ref[...] = jnp.zeros(total_ref.shape, jnp.float32)

        def fill(tiles_ref):
            for slot in range(slot_count):
                wide_ref[:, slot * tile_size:(slot + 1) * tile_size] = tiles_ref[slot]

        pl.when(source == 0)(lambda: fill(own_ref))
        pl.when(source == 1)(lambda: fill(other_ref))
        terms_ref[...] = jnp.dot(grad_ref[...], wide_ref[...], preferred_element_type=jnp.float32)
        for slot in range(slot_count):
            spot = where_ref[(source * blocks * tile_rows + base) * slot_count + slot]

            @pl.when(slot < live)
            def _():
                total_ref[spot] += terms_ref[:, slot * tile_size:(slot + 1) * tile_size]

        @pl.when((source == 1) & (row == tile_rows - 1) & (half_id == halves - 1))
        def _():
            out_ref[...] = total_ref[...]

    tile_spec = (None, None, slot_count, tile_size, tile_size)
    grid_spec = pltpu.PrefetchScalarGridSpec(
        num_scalar_prefetch=3,
        grid=(2, tile_rows, halves),
        in_specs=[
            pl.BlockSpec(tile_spec, own_map),
            pl.BlockSpec(tile_spec, sibling_map),
            pl.BlockSpec(
                (None, None, hidden_width, tile_size), lambda s, r, h, c, w, n: (s, r, 0, 0)
            ),
        ],
        out_specs=pl.BlockSpec(
            (buffer_tiles, hidden_width, tile_size), lambda s, r, h, c, w, n: (0, 0, 0)
        ),
        scratch_shapes=[
            pltpu.VMEM((buffer_tiles, hidden_width, tile_size), jnp.float32),
            pltpu.VMEM((tile_size, slot_count * tile_size), tile_stack.dtype),
            pltpu.VMEM((hidden_width, slot_count * tile_size), jnp.float32),
        ],
    )
    return pl.pallas_call(
        kernel,
        grid_spec=grid_spec,
        out_shape=jax.ShapeDtypeStruct((buffer_tiles, hidden_width, tile_size), jnp.float32),
        compiler_params=pltpu.CompilerParams(
            dimension_semantics=("arbitrary", "arbitrary", "arbitrary")
        ),
    )(
        jnp.reshape(core_id, (1,)).astype(jnp.int32),
        spots,
        counts,
        tile_stack,
        sibling_tiles,
        grads,
    )


def buffer_spots(tile_col, blk_id, feat_id, block_tiles, tiles_per_device):
    own = place_of(blk_id, feat_id)
    block = tile_col // block_tiles
    local = tile_col % block_tiles
    source_feat = local // tiles_per_device
    part = local % tiles_per_device
    source = place_of(block, source_feat)
    rel = {axis: (source[axis] - own[axis]) % RING for axis in ("y", "z", "x")}
    chunk = jnp.where(
        source["core"] == 0,
        rel["y"] * 16 + rel["z"] * 4 + rel["x"],
        rel["x"] * 16 + rel["z"] * 4 + rel["y"],
    )
    return (chunk * tiles_per_device + part).astype(jnp.int32)


def body(features_t, weight, tile_values, tile_col, tile_count, grad_out):
    cycle_size = lax.axis_size("blk")
    hidden_width = weight.shape[1]
    tile_size = tile_values.shape[1]
    rows_own = grad_out.shape[0]
    tile_rows = rows_own // tile_size
    block_rows = features_t.shape[1]
    block_tiles = block_rows // tile_size
    slot_count = tile_values.shape[0] // (cycle_size * tile_rows)
    feat_id = lax.axis_index("feat")
    blk_id = lax.axis_index("blk")
    core_id = blk_id % 2
    tile_stack = tile_values.reshape(cycle_size, tile_rows, slot_count, tile_size, tile_size)
    spots = buffer_spots(tile_col, blk_id, feat_id, block_tiles, tile_rows)
    sibling_tiles = sibling(tile_stack)
    sibling_col = sibling(tile_col)
    sibling_count = sibling(tile_count)
    buffer_tiles = block_tiles * 2

    features_own = lax.all_to_all(features_t, "feat", split_axis=1, concat_axis=0, tiled=True)
    projected = lax.dot_general(
        features_own, weight, (((0,), (0,)), ((), ())), preferred_element_type=jnp.float32
    ).astype(jnp.bfloat16)

    sibling_col, sibling_count, projected = lax.optimization_barrier(
        (sibling_col, sibling_count, projected)
    )
    sibling_spots = buffer_spots(sibling_col, blk_id, feat_id, block_tiles, tile_rows)
    gathered = gather_phase_direct(projected, 0)
    gathered = gather_phase_direct(gathered, 1)
    gathered = gather_phase(gathered, 2)
    own_buffer = gathered.reshape(buffer_tiles, tile_size, hidden_width)
    other_buffer = sibling(own_buffer)
    aggregate_sum = aggregate_pair(core_id, spots, tile_count, tile_stack, own_buffer)
    aggregate_sum = aggregate_sum + aggregate_pair(
        1 - core_id, spots, tile_count, tile_stack, other_buffer
    )

    pre_act = aggregate_sum.reshape(rows_own, hidden_width)
    sigmoid_y = jax.nn.sigmoid(pre_act)
    activations = (pre_act * sigmoid_y).astype(jnp.bfloat16)
    grad_pre = (
        grad_out.astype(jnp.float32) * sigmoid_y * (1.0 + pre_act * (1.0 - sigmoid_y))
    ).astype(jnp.bfloat16)
    grad_turned = grad_pre.reshape(tile_rows, tile_size, hidden_width).transpose(0, 2, 1)

    sibling_grad = sibling(grad_turned)
    total = spread_pair(
        core_id,
        jnp.concatenate([spots, sibling_spots]),
        jnp.concatenate([tile_count, sibling_count]),
        tile_stack,
        sibling_tiles,
        jnp.stack([grad_turned, sibling_grad]),
        buffer_tiles,
    )
    total = reduce_phase(
        total.reshape(RING, RING, RING, rows_own, hidden_width), 2, jnp.bfloat16
    )
    total = reduce_phase_direct(total, 1, jnp.bfloat16)
    total = reduce_phase_direct(total, 0, jnp.bfloat16)
    grad_hidden = (
        total.reshape(tile_rows, hidden_width, tile_size)
        .transpose(0, 2, 1)
        .reshape(rows_own, hidden_width)
        .astype(jnp.bfloat16)
    )

    weight_term = jnp.dot(features_own, grad_hidden, preferred_element_type=jnp.float32)
    features_grad_local = lax.dot_general(
        weight, grad_hidden, (((1,), (1,)), ((), ())), preferred_element_type=jnp.float32
    ).astype(jnp.bfloat16)
    feat_count = lax.axis_size("feat")
    shard_rows = weight_term.shape[0] // feat_count
    outgoing = jnp.concatenate(
        [
            weight_term.reshape(feat_count, shard_rows, hidden_width),
            features_grad_local.astype(jnp.float32).reshape(feat_count, shard_rows, rows_own),
        ],
        axis=2,
    )
    got = lax.all_to_all(outgoing, "feat", split_axis=0, concat_axis=0, tiled=True)
    weight_part = jnp.sum(got[:, :, :hidden_width], axis=0)
    grad_features = (
        got[:, :, hidden_width:].astype(jnp.bfloat16).transpose(1, 0, 2).reshape(shard_rows, -1)
    )
    parts = [weight_part] + [swapped(weight_part, "blk", mask) for mask in range(1, cycle_size)]
    by_blk = jnp.stack(parts)[jnp.bitwise_xor(jnp.arange(cycle_size), blk_id)]
    weight_part = by_blk[0]
    for index in range(1, cycle_size):
        weight_part = weight_part + by_blk[index]
    grad_weight = weight_part * lax.rsqrt(jnp.float32(block_rows * cycle_size))
    return (activations, grad_features, grad_weight)


def solution(mesh):
    placed = (
        P("feat", "blk"),
        P(),
        P(("blk", "feat"), None, None),
        P(("blk", "feat")),
        P(("blk", "feat")),
        P(("blk", "feat"), None),
    )
    return jax.shard_map(
        body,
        mesh=mesh,
        in_specs=placed,
        out_specs=(P(("blk", "feat"), None), P("feat", "blk"), P("feat", None)),
        check_vma=False,
    )
```

```python
import jax
import jax.numpy as jnp
from jax import lax
from jax.sharding import PartitionSpec as P
from jax.experimental import pallas as pl
from jax.experimental.pallas import tpu as pltpu

RING = 4
GATHER_ORDER = (("x", "z", "y"), ("y", "z", "x"))
BOTH = ("blk", "feat")


def place_of(blk, feat):
    return {
        "core": blk % 2,
        "y": (blk // 2) * 2 + feat // 16,
        "z": (feat // 4) % 4,
        "x": feat % 4,
    }


def linear_of(place):
    blk = (place["y"] // 2) * 2 + place["core"]
    feat = (place["y"] % 2) * 16 + place["z"] * 4 + place["x"]
    return blk * 32 + feat


def ring_shift(block, phase, distance):
    route = []
    for blk in range(4):
        for feat in range(32):
            place = place_of(blk, feat)
            axis = GATHER_ORDER[place["core"]][phase]
            target = dict(place)
            target[axis] = (place[axis] + distance) % RING
            route.append((linear_of(place), linear_of(target)))
    return lax.ppermute(block, BOTH, route)


def sibling(block):
    return lax.ppermute(block, "blk", [(i, i ^ 1) for i in range(lax.axis_size("blk"))])


def swapped(block, axis, mask):
    count = lax.axis_size(axis)
    return lax.ppermute(block, axis, [(i, i ^ mask) for i in range(count)])


def gather_phase(block, phase):
    half = block.shape[0] // 2
    from_minus = ring_shift(block, phase, 1)
    from_plus = ring_shift(block, phase, -1)
    far_low = ring_shift(from_minus[:half], phase, 1)
    far_high = ring_shift(from_plus[half:], phase, -1)
    far = jnp.concatenate([far_low, far_high], axis=0)
    return jnp.stack([block, from_plus, far, from_minus])


def gather_phase_direct(block, phase):
    from_minus = ring_shift(block, phase, 1)
    from_plus = ring_shift(block, phase, -1)
    far = ring_shift(block, phase, 2)
    return jnp.stack([block, from_plus, far, from_minus])


def reduce_phase_direct(total, phase, wire_type):
    from_minus = ring_shift(total[1].astype(wire_type), phase, 1)
    from_plus = ring_shift(total[3].astype(wire_type), phase, -1)
    far = ring_shift(total[2].astype(wire_type), phase, 2)
    return (
        total[0]
        + from_minus.astype(jnp.float32)
        + from_plus.astype(jnp.float32)
        + far.astype(jnp.float32)
    )


def reduce_phase(total, phase, wire_type, extra=None):
    half = total.shape[1] // 2

    def term(k):
        if extra is None:
            return total[k]
        return total[k] + extra[k].astype(jnp.float32)

    far = term(2)
    got_minus = ring_shift(far[:half].astype(wire_type), phase, 1)
    got_plus = ring_shift(far[half:].astype(wire_type), phase, -1)
    ahead = term(1)
    ahead = jnp.concatenate([ahead[:half] + got_minus.astype(jnp.float32), ahead[half:]], axis=0)
    behind = term(3)
    behind = jnp.concatenate([behind[:half], behind[half:] + got_plus.astype(jnp.float32)], axis=0)
    from_minus = ring_shift(ahead.astype(wire_type), phase, 1)
    from_plus = ring_shift(behind.astype(wire_type), phase, -1)
    return term(0) + from_minus.astype(jnp.float32) + from_plus.astype(jnp.float32)


def scatter_rows(total, axis, wire_type):
    count = lax.axis_size(axis)
    index = lax.axis_index(axis)
    mask = count // 2
    while mask >= 1:
        half = total.shape[0] // 2
        lower, upper_part = total[:half], total[half:]
        upper = (index // mask) % 2 == 1
        keep = jnp.where(upper, upper_part, lower)
        send = jnp.where(upper, lower, upper_part)
        got = swapped(send.astype(wire_type), axis, mask)
        total = keep + got.astype(jnp.float32)
        mask //= 2
    return total


def aggregate_kernel(core_ref, where_ref, count_ref, tiles_ref, proj_ref, out_ref, wide_ref, picked_ref):
    row = pl.program_id(0)
    half_id = pl.program_id(1)
    tile_rows = pl.num_programs(0)
    slot_count, tile_size, _ = tiles_ref.shape
    base = (half_id * 2 + core_ref[0]) * tile_rows + row
    live = count_ref[base]
    for slot in range(slot_count):
        wide_ref[:, slot * tile_size:(slot + 1) * tile_size] = tiles_ref[slot]
        piece = proj_ref[where_ref[base * slot_count + slot]]
        picked_ref[slot * tile_size:(slot + 1) * tile_size, :] = jnp.where(
            slot < live, piece, jnp.zeros_like(piece)
        )
    part = jnp.dot(wide_ref[...], picked_ref[...], preferred_element_type=jnp.float32)

    @pl.when(half_id == 0)
    def _():
        out_ref[...] = part

    @pl.when(half_id != 0)
    def _():
        out_ref[...] += part


def aggregate_pair(core_id, spots, counts, tile_stack, buffer):
    blocks, tile_rows, slot_count, tile_size, _ = tile_stack.shape
    hidden_width = buffer.shape[-1]
    grid_spec = pltpu.PrefetchScalarGridSpec(
        num_scalar_prefetch=3,
        grid=(tile_rows, blocks // 2),
        in_specs=[
            pl.BlockSpec(
                (None, None, slot_count, tile_size, tile_size),
                lambda r, h, c, w, n: (h * 2 + c[0], r, 0, 0, 0),
            ),
            pl.BlockSpec(buffer.shape, lambda r, h, c, w, n: (0, 0, 0)),
        ],
        out_specs=pl.BlockSpec((None, tile_size, hidden_width), lambda r, h, c, w, n: (r, 0, 0)),
        scratch_shapes=[
            pltpu.VMEM((tile_size, slot_count * tile_size), tile_stack.dtype),
            pltpu.VMEM((slot_count * tile_size, hidden_width), buffer.dtype),
        ],
    )
    return pl.pallas_call(
        aggregate_kernel,
        grid_spec=grid_spec,
        out_shape=jax.ShapeDtypeStruct((tile_rows, tile_size, hidden_width), jnp.float32),
        compiler_params=pltpu.CompilerParams(dimension_semantics=("arbitrary", "arbitrary")),
    )(jnp.reshape(core_id, (1,)).astype(jnp.int32), spots, counts, tile_stack, buffer)


def spread_pair(core_id, spots, counts, tile_stack, sibling_tiles, grads, buffer_tiles):
    blocks, tile_rows, slot_count, tile_size, _ = tile_stack.shape
    hidden_width = grads.shape[2]
    halves = blocks // 2
    last = halves - 1

    def own_map(s, r, h, c, w, n):
        return (
            jnp.where(s == 0, h * 2 + c[0], last * 2 + c[0]),
            jnp.where(s == 0, r, tile_rows - 1),
            0, 0, 0,
        )

    def sibling_map(s, r, h, c, w, n):
        return (jnp.where(s == 1, h * 2 + c[0], c[0]), jnp.where(s == 1, r, 0), 0, 0, 0)

    def kernel(core_ref, where_ref, count_ref, own_ref, other_ref, grad_ref, out_ref, total_ref,
               wide_ref, terms_ref):
        source = pl.program_id(0)
        row = pl.program_id(1)
        half_id = pl.program_id(2)
        base = (half_id * 2 + core_ref[0]) * tile_rows + row
        live = count_ref[source * blocks * tile_rows + base]

        @pl.when((source == 0) & (row == 0) & (half_id == 0))
        def _():
            total_ref[...] = jnp.zeros(total_ref.shape, jnp.float32)

        def fill(tiles_ref):
            for slot in range(slot_count):
                wide_ref[:, slot * tile_size:(slot + 1) * tile_size] = tiles_ref[slot]

        pl.when(source == 0)(lambda: fill(own_ref))
        pl.when(source == 1)(lambda: fill(other_ref))
        terms_ref[...] = jnp.dot(grad_ref[...], wide_ref[...], preferred_element_type=jnp.float32)
        for slot in range(slot_count):
            spot = where_ref[(source * blocks * tile_rows + base) * slot_count + slot]

            @pl.when(slot < live)
            def _():
                total_ref[spot] += terms_ref[:, slot * tile_size:(slot + 1) * tile_size]

        @pl.when((source == 1) & (row == tile_rows - 1) & (half_id == halves - 1))
        def _():
            out_ref[...] = total_ref[...]

    tile_spec = (None, None, slot_count, tile_size, tile_size)
    grid_spec = pltpu.PrefetchScalarGridSpec(
        num_scalar_prefetch=3,
        grid=(2, tile_rows, halves),
        in_specs=[
            pl.BlockSpec(tile_spec, own_map),
            pl.BlockSpec(tile_spec, sibling_map),
            pl.BlockSpec(
                (None, None, hidden_width, tile_size), lambda s, r, h, c, w, n: (s, r, 0, 0)
            ),
        ],
        out_specs=pl.BlockSpec(
            (buffer_tiles, hidden_width, tile_size), lambda s, r, h, c, w, n: (0, 0, 0)
        ),
        scratch_shapes=[
            pltpu.VMEM((buffer_tiles, hidden_width, tile_size), jnp.float32),
            pltpu.VMEM((tile_size, slot_count * tile_size), tile_stack.dtype),
            pltpu.VMEM((hidden_width, slot_count * tile_size), jnp.float32),
        ],
    )
    return pl.pallas_call(
        kernel,
        grid_spec=grid_spec,
        out_shape=jax.ShapeDtypeStruct((buffer_tiles, hidden_width, tile_size), jnp.float32),
        compiler_params=pltpu.CompilerParams(
            dimension_semantics=("arbitrary", "arbitrary", "arbitrary")
        ),
    )(
        jnp.reshape(core_id, (1,)).astype(jnp.int32),
        spots,
        counts,
        tile_stack,
        sibling_tiles,
        grads,
    )


def buffer_spots(tile_col, blk_id, feat_id, block_tiles, tiles_per_device):
    own = place_of(blk_id, feat_id)
    block = tile_col // block_tiles
    local = tile_col % block_tiles
    source_feat = local // tiles_per_device
    part = local % tiles_per_device
    source = place_of(block, source_feat)
    rel = {axis: (source[axis] - own[axis]) % RING for axis in ("y", "z", "x")}
    chunk = jnp.where(
        source["core"] == 0,
        rel["y"] * 16 + rel["z"] * 4 + rel["x"],
        rel["x"] * 16 + rel["z"] * 4 + rel["y"],
    )
    return (chunk * tiles_per_device + part).astype(jnp.int32)


def body(features_t, weight, tile_values, tile_col, tile_count, grad_out):
    cycle_size = lax.axis_size("blk")
    hidden_width = weight.shape[1]
    tile_size = tile_values.shape[1]
    rows_own = grad_out.shape[0]
    tile_rows = rows_own // tile_size
    block_rows = features_t.shape[1]
    block_tiles = block_rows // tile_size
    slot_count = tile_values.shape[0] // (cycle_size * tile_rows)
    feat_id = lax.axis_index("feat")
    blk_id = lax.axis_index("blk")
    core_id = blk_id % 2
    tile_stack = tile_values.reshape(cycle_size, tile_rows, slot_count, tile_size, tile_size)
    spots = buffer_spots(tile_col, blk_id, feat_id, block_tiles, tile_rows)
    sibling_tiles = sibling(tile_stack)
    sibling_col = sibling(tile_col)
    sibling_count = sibling(tile_count)
    buffer_tiles = block_tiles * 2

    features_own = lax.all_to_all(features_t, "feat", split_axis=1, concat_axis=0, tiled=True)
    projected = lax.dot_general(
        features_own, weight, (((0,), (0,)), ((), ())), preferred_element_type=jnp.float32
    ).astype(jnp.bfloat16)

    sibling_col, sibling_count, projected = lax.optimization_barrier(
        (sibling_col, sibling_count, projected)
    )
    sibling_spots = buffer_spots(sibling_col, blk_id, feat_id, block_tiles, tile_rows)
    gathered = gather_phase_direct(projected, 0)
    gathered = gather_phase_direct(gathered, 1)
    gathered = gather_phase(gathered, 2)
    own_buffer = gathered.reshape(buffer_tiles, tile_size, hidden_width)
    other_buffer = sibling(own_buffer)
    aggregate_sum = aggregate_pair(core_id, spots, tile_count, tile_stack, own_buffer)
    aggregate_sum = aggregate_sum + aggregate_pair(
        1 - core_id, spots, tile_count, tile_stack, other_buffer
    )

    pre_act = aggregate_sum.reshape(rows_own, hidden_width)
    sigmoid_y = jax.nn.sigmoid(pre_act)
    activations = (pre_act * sigmoid_y).astype(jnp.bfloat16)
    grad_pre = (
        grad_out.astype(jnp.float32) * sigmoid_y * (1.0 + pre_act * (1.0 - sigmoid_y))
    ).astype(jnp.bfloat16)
    grad_turned = grad_pre.reshape(tile_rows, tile_size, hidden_width).transpose(0, 2, 1)

    sibling_grad = sibling(grad_turned)
    total = spread_pair(
        core_id,
        jnp.concatenate([spots, sibling_spots]),
        jnp.concatenate([tile_count, sibling_count]),
        tile_stack,
        sibling_tiles,
        jnp.stack([grad_turned, sibling_grad]),
        buffer_tiles,
    )
    total = reduce_phase(
        total.reshape(RING, RING, RING, rows_own, hidden_width), 2, jnp.bfloat16
    )
    total = reduce_phase_direct(total, 1, jnp.bfloat16)
    total = reduce_phase_direct(total, 0, jnp.bfloat16)
    grad_hidden = (
        total.reshape(tile_rows, hidden_width, tile_size)
        .transpose(0, 2, 1)
        .reshape(rows_own, hidden_width)
        .astype(jnp.bfloat16)
    )

    weight_term = jnp.dot(features_own, grad_hidden, preferred_element_type=jnp.float32)
    features_grad_local = lax.dot_general(
        weight, grad_hidden, (((1,), (1,)), ((), ())), preferred_element_type=jnp.float32
    ).astype(jnp.bfloat16)
    feat_count = lax.axis_size("feat")
    shard_rows = weight_term.shape[0] // feat_count
    outgoing = jnp.concatenate(
        [
            weight_term.reshape(feat_count, shard_rows, hidden_width),
            features_grad_local.astype(jnp.float32).reshape(feat_count, shard_rows, rows_own),
        ],
        axis=2,
    )
    got = lax.all_to_all(outgoing, "feat", split_axis=0, concat_axis=0, tiled=True)
    weight_part = jnp.sum(got[:, :, :hidden_width], axis=0)
    grad_features = (
        got[:, :, hidden_width:].astype(jnp.bfloat16).transpose(1, 0, 2).reshape(shard_rows, -1)
    )
    parts = [weight_part] + [swapped(weight_part, "blk", mask) for mask in range(1, cycle_size)]
    by_blk = jnp.stack(parts)[jnp.bitwise_xor(jnp.arange(cycle_size), blk_id)]
    weight_part = by_blk[0]
    for index in range(1, cycle_size):
        weight_part = weight_part + by_blk[index]
    grad_weight = weight_part * lax.rsqrt(jnp.float32(block_rows * cycle_size))
    return (activations, grad_features, grad_weight)


def solution(mesh):
    placed = (
        P("feat", "blk"),
        P(),
        P(("blk", "feat"), None, None),
        P(("blk", "feat")),
        P(("blk", "feat")),
        P(("blk", "feat"), None),
    )
    return jax.shard_map(
        body,
        mesh=mesh,
        in_specs=placed,
        out_specs=(P(("blk", "feat"), None), P("feat", "blk"), P("feat", None)),
        check_vma=False,
    )
```

```python
import jax
import jax.numpy as jnp
from jax import lax
from jax.sharding import PartitionSpec as P
from jax.experimental import pallas as pl
from jax.experimental.pallas import tpu as pltpu

RING = 4
GATHER_ORDER = (("x", "z", "y"), ("y", "z", "x"))
BOTH = ("blk", "feat")


def place_of(blk, feat):
    return {
        "core": blk % 2,
        "y": (blk // 2) * 2 + feat // 16,
        "z": (feat // 4) % 4,
        "x": feat % 4,
    }


def linear_of(place):
    blk = (place["y"] // 2) * 2 + place["core"]
    feat = (place["y"] % 2) * 16 + place["z"] * 4 + place["x"]
    return blk * 32 + feat


def ring_shift(block, phase, distance):
    route = []
    for blk in range(4):
        for feat in range(32):
            place = place_of(blk, feat)
            axis = GATHER_ORDER[place["core"]][phase]
            target = dict(place)
            target[axis] = (place[axis] + distance) % RING
            route.append((linear_of(place), linear_of(target)))
    return lax.ppermute(block, BOTH, route)


def sibling(block):
    return lax.ppermute(block, "blk", [(i, i ^ 1) for i in range(lax.axis_size("blk"))])


def swapped(block, axis, mask):
    count = lax.axis_size(axis)
    return lax.ppermute(block, axis, [(i, i ^ mask) for i in range(count)])


def gather_phase(block, phase):
    half = block.shape[-2] // 2
    from_minus = ring_shift(block, phase, 1)
    from_plus = ring_shift(block, phase, -1)
    far_low = ring_shift(from_minus[..., :half, :], phase, 1)
    far_high = ring_shift(from_plus[..., half:, :], phase, -1)
    far = jnp.concatenate([far_low, far_high], axis=-2)
    return jnp.stack([block, from_plus, far, from_minus])


def gather_phase_direct(block, phase):
    from_minus = ring_shift(block, phase, 1)
    from_plus = ring_shift(block, phase, -1)
    far = ring_shift(block, phase, 2)
    return jnp.stack([block, from_plus, far, from_minus])


def reduce_phase_direct(total, phase, wire_type):
    from_minus = ring_shift(total[1].astype(wire_type), phase, 1)
    from_plus = ring_shift(total[3].astype(wire_type), phase, -1)
    far = ring_shift(total[2].astype(wire_type), phase, 2)
    return (
        total[0]
        + from_minus.astype(jnp.float32)
        + from_plus.astype(jnp.float32)
        + far.astype(jnp.float32)
    )


def reduce_phase(total, phase, wire_type, extra=None):
    half = total.shape[-2] // 2

    def term(k):
        if extra is None:
            return total[k]
        return total[k] + extra[k].astype(jnp.float32)

    far = term(2)
    got_minus = ring_shift(far[..., :half, :].astype(wire_type), phase, 1)
    got_plus = ring_shift(far[..., half:, :].astype(wire_type), phase, -1)
    ahead = term(1)
    ahead = jnp.concatenate(
        [ahead[..., :half, :] + got_minus.astype(jnp.float32), ahead[..., half:, :]], axis=-2
    )
    behind = term(3)
    behind = jnp.concatenate(
        [behind[..., :half, :], behind[..., half:, :] + got_plus.astype(jnp.float32)], axis=-2
    )
    from_minus = ring_shift(ahead.astype(wire_type), phase, 1)
    from_plus = ring_shift(behind.astype(wire_type), phase, -1)
    return term(0) + from_minus.astype(jnp.float32) + from_plus.astype(jnp.float32)


def scatter_rows(total, axis, wire_type):
    count = lax.axis_size(axis)
    index = lax.axis_index(axis)
    mask = count // 2
    while mask >= 1:
        half = total.shape[0] // 2
        lower, upper_part = total[:half], total[half:]
        upper = (index // mask) % 2 == 1
        keep = jnp.where(upper, upper_part, lower)
        send = jnp.where(upper, lower, upper_part)
        got = swapped(send.astype(wire_type), axis, mask)
        total = keep + got.astype(jnp.float32)
        mask //= 2
    return total


def aggregate_kernel(core_ref, where_ref, count_ref, tiles_ref, proj_ref, out_ref, wide_ref, picked_ref):
    row = pl.program_id(0)
    half_id = pl.program_id(1)
    tile_rows = pl.num_programs(0)
    slot_count, tile_size, _ = tiles_ref.shape
    base = (half_id * 2 + core_ref[0]) * tile_rows + row
    live = count_ref[base]
    for slot in range(slot_count):
        wide_ref[:, slot * tile_size:(slot + 1) * tile_size] = tiles_ref[slot]
        piece = proj_ref[where_ref[base * slot_count + slot]]
        picked_ref[slot * tile_size:(slot + 1) * tile_size, :] = jnp.where(
            slot < live, piece, jnp.zeros_like(piece)
        )
    part = jnp.dot(wide_ref[...], picked_ref[...], preferred_element_type=jnp.float32)

    @pl.when(half_id == 0)
    def _():
        out_ref[...] = part

    @pl.when(half_id != 0)
    def _():
        out_ref[...] += part


def aggregate_pair(core_id, spots, counts, tile_stack, buffer):
    blocks, tile_rows, slot_count, tile_size, _ = tile_stack.shape
    hidden_width = buffer.shape[-1]
    grid_spec = pltpu.PrefetchScalarGridSpec(
        num_scalar_prefetch=3,
        grid=(tile_rows, blocks // 2),
        in_specs=[
            pl.BlockSpec(
                (None, None, slot_count, tile_size, tile_size),
                lambda r, h, c, w, n: (h * 2 + c[0], r, 0, 0, 0),
            ),
            pl.BlockSpec(buffer.shape, lambda r, h, c, w, n: (0, 0, 0)),
        ],
        out_specs=pl.BlockSpec((None, tile_size, hidden_width), lambda r, h, c, w, n: (r, 0, 0)),
        scratch_shapes=[
            pltpu.VMEM((tile_size, slot_count * tile_size), tile_stack.dtype),
            pltpu.VMEM((slot_count * tile_size, hidden_width), buffer.dtype),
        ],
    )
    return pl.pallas_call(
        aggregate_kernel,
        grid_spec=grid_spec,
        out_shape=jax.ShapeDtypeStruct((tile_rows, tile_size, hidden_width), jnp.float32),
        compiler_params=pltpu.CompilerParams(dimension_semantics=("arbitrary", "arbitrary")),
    )(jnp.reshape(core_id, (1,)).astype(jnp.int32), spots, counts, tile_stack, buffer)


def spread_pair(core_id, spots, counts, tile_stack, sibling_tiles, grads, buffer_tiles):
    blocks, tile_rows, slot_count, tile_size, _ = tile_stack.shape
    hidden_width = grads.shape[2]
    halves = blocks // 2
    last = halves - 1

    def own_map(s, r, h, c, w, n):
        return (
            jnp.where(s == 0, h * 2 + c[0], last * 2 + c[0]),
            jnp.where(s == 0, r, tile_rows - 1),
            0, 0, 0,
        )

    def sibling_map(s, r, h, c, w, n):
        return (jnp.where(s == 1, h * 2 + c[0], c[0]), jnp.where(s == 1, r, 0), 0, 0, 0)

    def kernel(core_ref, where_ref, count_ref, own_ref, other_ref, grad_ref, out_ref, total_ref,
               wide_ref, terms_ref):
        source = pl.program_id(0)
        row = pl.program_id(1)
        half_id = pl.program_id(2)
        base = (half_id * 2 + core_ref[0]) * tile_rows + row
        live = count_ref[source * blocks * tile_rows + base]

        @pl.when((source == 0) & (row == 0) & (half_id == 0))
        def _():
            total_ref[...] = jnp.zeros(total_ref.shape, jnp.float32)

        def fill(tiles_ref):
            for slot in range(slot_count):
                wide_ref[:, slot * tile_size:(slot + 1) * tile_size] = tiles_ref[slot]

        pl.when(source == 0)(lambda: fill(own_ref))
        pl.when(source == 1)(lambda: fill(other_ref))
        terms_ref[...] = jnp.dot(grad_ref[...], wide_ref[...], preferred_element_type=jnp.float32)
        for slot in range(slot_count):
            spot = where_ref[(source * blocks * tile_rows + base) * slot_count + slot]

            @pl.when(slot < live)
            def _():
                total_ref[spot] += terms_ref[:, slot * tile_size:(slot + 1) * tile_size]

        @pl.when((source == 1) & (row == tile_rows - 1) & (half_id == halves - 1))
        def _():
            out_ref[...] = total_ref[...]

    tile_spec = (None, None, slot_count, tile_size, tile_size)
    grid_spec = pltpu.PrefetchScalarGridSpec(
        num_scalar_prefetch=3,
        grid=(2, tile_rows, halves),
        in_specs=[
            pl.BlockSpec(tile_spec, own_map),
            pl.BlockSpec(tile_spec, sibling_map),
            pl.BlockSpec(
                (None, None, hidden_width, tile_size), lambda s, r, h, c, w, n: (s, r, 0, 0)
            ),
        ],
        out_specs=pl.BlockSpec(
            (buffer_tiles, hidden_width, tile_size), lambda s, r, h, c, w, n: (0, 0, 0)
        ),
        scratch_shapes=[
            pltpu.VMEM((buffer_tiles, hidden_width, tile_size), jnp.float32),
            pltpu.VMEM((tile_size, slot_count * tile_size), tile_stack.dtype),
            pltpu.VMEM((hidden_width, slot_count * tile_size), jnp.float32),
        ],
    )
    return pl.pallas_call(
        kernel,
        grid_spec=grid_spec,
        out_shape=jax.ShapeDtypeStruct((buffer_tiles, hidden_width, tile_size), jnp.float32),
        compiler_params=pltpu.CompilerParams(
            dimension_semantics=("arbitrary", "arbitrary", "arbitrary")
        ),
    )(
        jnp.reshape(core_id, (1,)).astype(jnp.int32),
        spots,
        counts,
        tile_stack,
        sibling_tiles,
        grads,
    )


def buffer_spots(tile_col, blk_id, feat_id, block_tiles, tiles_per_device):
    own = place_of(blk_id, feat_id)
    block = tile_col // block_tiles
    local = tile_col % block_tiles
    source_feat = local // tiles_per_device
    part = local % tiles_per_device
    source = place_of(block, source_feat)
    rel = {axis: (source[axis] - own[axis]) % RING for axis in ("y", "z", "x")}
    chunk = jnp.where(
        source["core"] == 0,
        rel["y"] * 16 + rel["z"] * 4 + rel["x"],
        rel["x"] * 16 + rel["z"] * 4 + rel["y"],
    )
    return (chunk * tiles_per_device + part).astype(jnp.int32)


def body(features_t, weight, tile_values, tile_col, tile_count, grad_out):
    cycle_size = lax.axis_size("blk")
    hidden_width = weight.shape[1]
    tile_size = tile_values.shape[1]
    rows_own = grad_out.shape[0]
    tile_rows = rows_own // tile_size
    block_rows = features_t.shape[1]
    block_tiles = block_rows // tile_size
    slot_count = tile_values.shape[0] // (cycle_size * tile_rows)
    feat_id = lax.axis_index("feat")
    blk_id = lax.axis_index("blk")
    core_id = blk_id % 2
    tile_stack = tile_values.reshape(cycle_size, tile_rows, slot_count, tile_size, tile_size)
    spots = buffer_spots(tile_col, blk_id, feat_id, block_tiles, tile_rows)
    sibling_tiles = sibling(tile_stack)
    sibling_col = sibling(tile_col)
    sibling_count = sibling(tile_count)
    buffer_tiles = block_tiles * 2

    features_own = lax.all_to_all(features_t, "feat", split_axis=1, concat_axis=0, tiled=True)
    projected = lax.dot_general(
        features_own, weight, (((0,), (0,)), ((), ())), preferred_element_type=jnp.float32
    ).astype(jnp.bfloat16)

    sibling_col, sibling_count, projected = lax.optimization_barrier(
        (sibling_col, sibling_count, projected)
    )
    sibling_spots = buffer_spots(sibling_col, blk_id, feat_id, block_tiles, tile_rows)
    gathered = gather_phase_direct(projected, 0)
    gathered = gather_phase(gathered, 1)
    gathered = gather_phase(gathered, 2)
    own_buffer = gathered.reshape(buffer_tiles, tile_size, hidden_width)
    other_buffer = sibling(own_buffer)
    aggregate_sum = aggregate_pair(core_id, spots, tile_count, tile_stack, own_buffer)
    aggregate_sum = aggregate_sum + aggregate_pair(
        1 - core_id, spots, tile_count, tile_stack, other_buffer
    )

    pre_act = aggregate_sum.reshape(rows_own, hidden_width)
    sigmoid_y = jax.nn.sigmoid(pre_act)
    activations = (pre_act * sigmoid_y).astype(jnp.bfloat16)
    grad_pre = (
        grad_out.astype(jnp.float32) * sigmoid_y * (1.0 + pre_act * (1.0 - sigmoid_y))
    ).astype(jnp.bfloat16)
    grad_turned = grad_pre.reshape(tile_rows, tile_size, hidden_width).transpose(0, 2, 1)

    sibling_grad = sibling(grad_turned)
    total = spread_pair(
        core_id,
        jnp.concatenate([spots, sibling_spots]),
        jnp.concatenate([tile_count, sibling_count]),
        tile_stack,
        sibling_tiles,
        jnp.stack([grad_turned, sibling_grad]),
        buffer_tiles,
    )
    total = reduce_phase(
        total.reshape(RING, RING, RING, rows_own, hidden_width), 2, jnp.bfloat16
    )
    total = reduce_phase(total, 1, jnp.bfloat16)
    total = reduce_phase_direct(total, 0, jnp.bfloat16)
    grad_hidden = (
        total.reshape(tile_rows, hidden_width, tile_size)
        .transpose(0, 2, 1)
        .reshape(rows_own, hidden_width)
        .astype(jnp.bfloat16)
    )

    weight_term = jnp.dot(features_own, grad_hidden, preferred_element_type=jnp.float32)
    features_grad_local = lax.dot_general(
        weight, grad_hidden, (((1,), (1,)), ((), ())), preferred_element_type=jnp.float32
    ).astype(jnp.bfloat16)
    feat_count = lax.axis_size("feat")
    shard_rows = weight_term.shape[0] // feat_count
    outgoing = jnp.concatenate(
        [
            weight_term.reshape(feat_count, shard_rows, hidden_width),
            features_grad_local.astype(jnp.float32).reshape(feat_count, shard_rows, rows_own),
        ],
        axis=2,
    )
    got = lax.all_to_all(outgoing, "feat", split_axis=0, concat_axis=0, tiled=True)
    weight_part = jnp.sum(got[:, :, :hidden_width], axis=0)
    grad_features = (
        got[:, :, hidden_width:].astype(jnp.bfloat16).transpose(1, 0, 2).reshape(shard_rows, -1)
    )
    weight_part = weight_part + swapped(weight_part, "blk", 1)
    weight_part = weight_part + swapped(weight_part, "blk", 2)
    grad_weight = weight_part * lax.rsqrt(jnp.float32(block_rows * cycle_size))
    return (activations, grad_features, grad_weight)


def solution(mesh):
    placed = (
        P("feat", "blk"),
        P(),
        P(("blk", "feat"), None, None),
        P(("blk", "feat")),
        P(("blk", "feat")),
        P(("blk", "feat"), None),
    )
    return jax.shard_map(
        body,
        mesh=mesh,
        in_specs=placed,
        out_specs=(P(("blk", "feat"), None), P("feat", "blk"), P("feat", None)),
        check_vma=False,
    )
```

```python
import jax
import jax.numpy as jnp
from jax import lax
from jax.sharding import PartitionSpec as P
from jax.experimental import pallas as pl
from jax.experimental.pallas import tpu as pltpu

RING = 4
GATHER_ORDER = (("x", "z", "y"), ("y", "z", "x"))
BOTH = ("blk", "feat")


def place_of(blk, feat):
    return {
        "core": blk % 2,
        "y": (blk // 2) * 2 + feat // 16,
        "z": (feat // 4) % 4,
        "x": feat % 4,
    }


def linear_of(place):
    blk = (place["y"] // 2) * 2 + place["core"]
    feat = (place["y"] % 2) * 16 + place["z"] * 4 + place["x"]
    return blk * 32 + feat


def ring_shift(block, phase, distance):
    route = []
    for blk in range(4):
        for feat in range(32):
            place = place_of(blk, feat)
            axis = GATHER_ORDER[place["core"]][phase]
            target = dict(place)
            target[axis] = (place[axis] + distance) % RING
            route.append((linear_of(place), linear_of(target)))
    return lax.ppermute(block, BOTH, route)


def sibling(block):
    return lax.ppermute(block, "blk", [(i, i ^ 1) for i in range(lax.axis_size("blk"))])


def swapped(block, axis, mask):
    count = lax.axis_size(axis)
    return lax.ppermute(block, axis, [(i, i ^ mask) for i in range(count)])


def gather_phase(block, phase):
    half = block.shape[-2] // 2
    from_minus = ring_shift(block, phase, 1)
    from_plus = ring_shift(block, phase, -1)
    far_low = ring_shift(from_minus[..., :half, :], phase, 1)
    far_high = ring_shift(from_plus[..., half:, :], phase, -1)
    far = jnp.concatenate([far_low, far_high], axis=-2)
    return jnp.stack([block, from_plus, far, from_minus])


def gather_phase_direct(block, phase):
    from_minus = ring_shift(block, phase, 1)
    from_plus = ring_shift(block, phase, -1)
    far = ring_shift(block, phase, 2)
    return jnp.stack([block, from_plus, far, from_minus])


def reduce_phase_direct(total, phase, wire_type):
    from_minus = ring_shift(total[1].astype(wire_type), phase, 1)
    from_plus = ring_shift(total[3].astype(wire_type), phase, -1)
    far = ring_shift(total[2].astype(wire_type), phase, 2)
    return (
        total[0]
        + from_minus.astype(jnp.float32)
        + from_plus.astype(jnp.float32)
        + far.astype(jnp.float32)
    )


def reduce_phase(total, phase, wire_type, extra=None):
    half = total.shape[-2] // 2

    def term(k):
        if extra is None:
            return total[k]
        return total[k] + extra[k].astype(jnp.float32)

    far = term(2)
    got_minus = ring_shift(far[..., :half, :].astype(wire_type), phase, 1)
    got_plus = ring_shift(far[..., half:, :].astype(wire_type), phase, -1)
    ahead = term(1)
    ahead = jnp.concatenate(
        [ahead[..., :half, :] + got_minus.astype(jnp.float32), ahead[..., half:, :]], axis=-2
    )
    behind = term(3)
    behind = jnp.concatenate(
        [behind[..., :half, :], behind[..., half:, :] + got_plus.astype(jnp.float32)], axis=-2
    )
    from_minus = ring_shift(ahead.astype(wire_type), phase, 1)
    from_plus = ring_shift(behind.astype(wire_type), phase, -1)
    return term(0) + from_minus.astype(jnp.float32) + from_plus.astype(jnp.float32)


def scatter_rows(total, axis, wire_type):
    count = lax.axis_size(axis)
    index = lax.axis_index(axis)
    mask = count // 2
    while mask >= 1:
        half = total.shape[0] // 2
        lower, upper_part = total[:half], total[half:]
        upper = (index // mask) % 2 == 1
        keep = jnp.where(upper, upper_part, lower)
        send = jnp.where(upper, lower, upper_part)
        got = swapped(send.astype(wire_type), axis, mask)
        total = keep + got.astype(jnp.float32)
        mask //= 2
    return total


def aggregate_kernel(core_ref, where_ref, count_ref, tiles_ref, proj_ref, out_ref):
    row = pl.program_id(0)
    half_id = pl.program_id(1)
    tile_rows = pl.num_programs(0)
    slot_count, tile_size, _ = tiles_ref.shape
    base = (half_id * 2 + core_ref[0]) * tile_rows + row
    live = count_ref[base]
    part = jnp.zeros(out_ref.shape, jnp.float32)
    for slot in range(slot_count):
        piece = proj_ref[where_ref[base * slot_count + slot]]
        piece = jnp.where(slot < live, piece, jnp.zeros_like(piece))
        part = part + jnp.dot(tiles_ref[slot], piece, preferred_element_type=jnp.float32)

    @pl.when(half_id == 0)
    def _():
        out_ref[...] = part

    @pl.when(half_id != 0)
    def _():
        out_ref[...] += part


def aggregate_pair(core_id, spots, counts, tile_stack, buffer):
    blocks, tile_rows, slot_count, tile_size, _ = tile_stack.shape
    hidden_width = buffer.shape[-1]
    grid_spec = pltpu.PrefetchScalarGridSpec(
        num_scalar_prefetch=3,
        grid=(tile_rows, blocks // 2),
        in_specs=[
            pl.BlockSpec(
                (None, None, slot_count, tile_size, tile_size),
                lambda r, h, c, w, n: (h * 2 + c[0], r, 0, 0, 0),
            ),
            pl.BlockSpec(buffer.shape, lambda r, h, c, w, n: (0, 0, 0)),
        ],
        out_specs=pl.BlockSpec((None, tile_size, hidden_width), lambda r, h, c, w, n: (r, 0, 0)),
    )
    return pl.pallas_call(
        aggregate_kernel,
        grid_spec=grid_spec,
        out_shape=jax.ShapeDtypeStruct((tile_rows, tile_size, hidden_width), jnp.float32),
        compiler_params=pltpu.CompilerParams(dimension_semantics=("arbitrary", "arbitrary")),
    )(jnp.reshape(core_id, (1,)).astype(jnp.int32), spots, counts, tile_stack, buffer)


def spread_pair(core_id, spots, counts, tile_stack, sibling_tiles, grads, buffer_tiles):
    blocks, tile_rows, slot_count, tile_size, _ = tile_stack.shape
    hidden_width = grads.shape[2]
    halves = blocks // 2
    last = halves - 1

    def own_map(s, r, h, c, w, n):
        return (
            jnp.where(s == 0, h * 2 + c[0], last * 2 + c[0]),
            jnp.where(s == 0, r, tile_rows - 1),
            0, 0, 0,
        )

    def sibling_map(s, r, h, c, w, n):
        return (jnp.where(s == 1, h * 2 + c[0], c[0]), jnp.where(s == 1, r, 0), 0, 0, 0)

    def kernel(core_ref, where_ref, count_ref, own_ref, other_ref, grad_ref, out_ref, total_ref,
               wide_ref, terms_ref):
        source = pl.program_id(0)
        row = pl.program_id(1)
        half_id = pl.program_id(2)
        base = (half_id * 2 + core_ref[0]) * tile_rows + row
        live = count_ref[source * blocks * tile_rows + base]

        @pl.when((source == 0) & (row == 0) & (half_id == 0))
        def _():
            total_ref[...] = jnp.zeros(total_ref.shape, jnp.float32)

        def fill(tiles_ref):
            for slot in range(slot_count):
                wide_ref[:, slot * tile_size:(slot + 1) * tile_size] = tiles_ref[slot]

        pl.when(source == 0)(lambda: fill(own_ref))
        pl.when(source == 1)(lambda: fill(other_ref))
        terms_ref[...] = jnp.dot(grad_ref[...], wide_ref[...], preferred_element_type=jnp.float32)
        for slot in range(slot_count):
            spot = where_ref[(source * blocks * tile_rows + base) * slot_count + slot]

            @pl.when(slot < live)
            def _():
                total_ref[spot] += terms_ref[:, slot * tile_size:(slot + 1) * tile_size]

        @pl.when((source == 1) & (row == tile_rows - 1) & (half_id == halves - 1))
        def _():
            out_ref[...] = total_ref[...]

    tile_spec = (None, None, slot_count, tile_size, tile_size)
    grid_spec = pltpu.PrefetchScalarGridSpec(
        num_scalar_prefetch=3,
        grid=(2, tile_rows, halves),
        in_specs=[
            pl.BlockSpec(tile_spec, own_map),
            pl.BlockSpec(tile_spec, sibling_map),
            pl.BlockSpec(
                (None, None, hidden_width, tile_size), lambda s, r, h, c, w, n: (s, r, 0, 0)
            ),
        ],
        out_specs=pl.BlockSpec(
            (buffer_tiles, hidden_width, tile_size), lambda s, r, h, c, w, n: (0, 0, 0)
        ),
        scratch_shapes=[
            pltpu.VMEM((buffer_tiles, hidden_width, tile_size), jnp.float32),
            pltpu.VMEM((tile_size, slot_count * tile_size), tile_stack.dtype),
            pltpu.VMEM((hidden_width, slot_count * tile_size), jnp.float32),
        ],
    )
    return pl.pallas_call(
        kernel,
        grid_spec=grid_spec,
        out_shape=jax.ShapeDtypeStruct((buffer_tiles, hidden_width, tile_size), jnp.float32),
        compiler_params=pltpu.CompilerParams(
            dimension_semantics=("arbitrary", "arbitrary", "arbitrary")
        ),
    )(
        jnp.reshape(core_id, (1,)).astype(jnp.int32),
        spots,
        counts,
        tile_stack,
        sibling_tiles,
        grads,
    )


def buffer_spots(tile_col, blk_id, feat_id, block_tiles, tiles_per_device):
    own = place_of(blk_id, feat_id)
    block = tile_col // block_tiles
    local = tile_col % block_tiles
    source_feat = local // tiles_per_device
    part = local % tiles_per_device
    source = place_of(block, source_feat)
    rel = {axis: (source[axis] - own[axis]) % RING for axis in ("y", "z", "x")}
    chunk = jnp.where(
        source["core"] == 0,
        rel["y"] * 16 + rel["z"] * 4 + rel["x"],
        rel["x"] * 16 + rel["z"] * 4 + rel["y"],
    )
    return (chunk * tiles_per_device + part).astype(jnp.int32)


def body(features_t, weight, tile_values, tile_col, tile_count, grad_out):
    cycle_size = lax.axis_size("blk")
    hidden_width = weight.shape[1]
    tile_size = tile_values.shape[1]
    rows_own = grad_out.shape[0]
    tile_rows = rows_own // tile_size
    block_rows = features_t.shape[1]
    block_tiles = block_rows // tile_size
    slot_count = tile_values.shape[0] // (cycle_size * tile_rows)
    feat_id = lax.axis_index("feat")
    blk_id = lax.axis_index("blk")
    core_id = blk_id % 2
    tile_stack = tile_values.reshape(cycle_size, tile_rows, slot_count, tile_size, tile_size)
    spots = buffer_spots(tile_col, blk_id, feat_id, block_tiles, tile_rows)
    sibling_tiles = sibling(tile_stack)
    sibling_col = sibling(tile_col)
    sibling_count = sibling(tile_count)
    buffer_tiles = block_tiles * 2

    features_own = lax.all_to_all(features_t, "feat", split_axis=1, concat_axis=0, tiled=True)
    projected = lax.dot_general(
        features_own, weight, (((0,), (0,)), ((), ())), preferred_element_type=jnp.float32
    ).astype(jnp.bfloat16)

    sibling_col, sibling_count, projected = lax.optimization_barrier(
        (sibling_col, sibling_count, projected)
    )
    sibling_spots = buffer_spots(sibling_col, blk_id, feat_id, block_tiles, tile_rows)
    gathered = gather_phase_direct(projected, 0)
    gathered = gather_phase_direct(gathered, 1)
    gathered = gather_phase(gathered, 2)
    own_buffer = gathered.reshape(buffer_tiles, tile_size, hidden_width)
    other_buffer = sibling(own_buffer)
    aggregate_sum = aggregate_pair(core_id, spots, tile_count, tile_stack, own_buffer)
    aggregate_sum = aggregate_sum + aggregate_pair(
        1 - core_id, spots, tile_count, tile_stack, other_buffer
    )

    pre_act = aggregate_sum.reshape(rows_own, hidden_width)
    sigmoid_y = jax.nn.sigmoid(pre_act)
    activations = (pre_act * sigmoid_y).astype(jnp.bfloat16)
    grad_pre = (
        grad_out.astype(jnp.float32) * sigmoid_y * (1.0 + pre_act * (1.0 - sigmoid_y))
    ).astype(jnp.bfloat16)
    grad_turned = grad_pre.reshape(tile_rows, tile_size, hidden_width).transpose(0, 2, 1)

    sibling_grad = sibling(grad_turned)
    total = spread_pair(
        core_id,
        jnp.concatenate([spots, sibling_spots]),
        jnp.concatenate([tile_count, sibling_count]),
        tile_stack,
        sibling_tiles,
        jnp.stack([grad_turned, sibling_grad]),
        buffer_tiles,
    )
    total = reduce_phase(
        total.reshape(RING, RING, RING, rows_own, hidden_width), 2, jnp.bfloat16
    )
    total = reduce_phase_direct(total, 1, jnp.bfloat16)
    total = reduce_phase_direct(total, 0, jnp.bfloat16)
    grad_hidden = (
        total.reshape(tile_rows, hidden_width, tile_size)
        .transpose(0, 2, 1)
        .reshape(rows_own, hidden_width)
        .astype(jnp.bfloat16)
    )

    weight_term = jnp.dot(features_own, grad_hidden, preferred_element_type=jnp.float32)
    features_grad_local = lax.dot_general(
        weight, grad_hidden, (((1,), (1,)), ((), ())), preferred_element_type=jnp.float32
    ).astype(jnp.bfloat16)
    feat_count = lax.axis_size("feat")
    shard_rows = weight_term.shape[0] // feat_count
    outgoing = jnp.concatenate(
        [
            weight_term.reshape(feat_count, shard_rows, hidden_width),
            features_grad_local.astype(jnp.float32).reshape(feat_count, shard_rows, rows_own),
        ],
        axis=2,
    )
    got = lax.all_to_all(outgoing, "feat", split_axis=0, concat_axis=0, tiled=True)
    weight_part = jnp.sum(got[:, :, :hidden_width], axis=0)
    grad_features = (
        got[:, :, hidden_width:].astype(jnp.bfloat16).transpose(1, 0, 2).reshape(shard_rows, -1)
    )
    weight_part = weight_part + swapped(weight_part, "blk", 1)
    weight_part = weight_part + swapped(weight_part, "blk", 2)
    grad_weight = weight_part * lax.rsqrt(jnp.float32(block_rows * cycle_size))
    return (activations, grad_features, grad_weight)


def solution(mesh):
    placed = (
        P("feat", "blk"),
        P(),
        P(("blk", "feat"), None, None),
        P(("blk", "feat")),
        P(("blk", "feat")),
        P(("blk", "feat"), None),
    )
    return jax.shard_map(
        body,
        mesh=mesh,
        in_specs=placed,
        out_specs=(P(("blk", "feat"), None), P("feat", "blk"), P("feat", None)),
        check_vma=False,
    )
```

```python
import jax
import jax.numpy as jnp
from jax import lax
from jax.sharding import PartitionSpec as P
from jax.experimental import pallas as pl
from jax.experimental.pallas import tpu as pltpu

RING = 4
GATHER_ORDER = (("x", "z", "y"), ("y", "z", "x"))
BOTH = ("blk", "feat")


def place_of(blk, feat):
    return {
        "core": blk % 2,
        "y": (blk // 2) * 2 + feat // 16,
        "z": (feat // 4) % 4,
        "x": feat % 4,
    }


def linear_of(place):
    blk = (place["y"] // 2) * 2 + place["core"]
    feat = (place["y"] % 2) * 16 + place["z"] * 4 + place["x"]
    return blk * 32 + feat


def ring_shift(block, phase, distance):
    route = []
    for blk in range(4):
        for feat in range(32):
            place = place_of(blk, feat)
            axis = GATHER_ORDER[place["core"]][phase]
            target = dict(place)
            target[axis] = (place[axis] + distance) % RING
            route.append((linear_of(place), linear_of(target)))
    return lax.ppermute(block, BOTH, route)


def sibling(block):
    return lax.ppermute(block, "blk", [(i, i ^ 1) for i in range(lax.axis_size("blk"))])


def swapped(block, axis, mask):
    count = lax.axis_size(axis)
    return lax.ppermute(block, axis, [(i, i ^ mask) for i in range(count)])


def gather_phase(block, phase):
    half = block.shape[-2] // 2
    from_minus = ring_shift(block, phase, 1)
    from_plus = ring_shift(block, phase, -1)
    far_low = ring_shift(from_minus[..., :half, :], phase, 1)
    far_high = ring_shift(from_plus[..., half:, :], phase, -1)
    far = jnp.concatenate([far_low, far_high], axis=-2)
    return jnp.stack([block, from_plus, far, from_minus])


def gather_phase_direct(block, phase):
    from_minus = ring_shift(block, phase, 1)
    from_plus = ring_shift(block, phase, -1)
    far = ring_shift(block, phase, 2)
    return jnp.stack([block, from_plus, far, from_minus])


def reduce_phase_direct(total, phase, wire_type):
    from_minus = ring_shift(total[1].astype(wire_type), phase, 1)
    from_plus = ring_shift(total[3].astype(wire_type), phase, -1)
    far = ring_shift(total[2].astype(wire_type), phase, 2)
    return (
        total[0]
        + from_minus.astype(jnp.float32)
        + from_plus.astype(jnp.float32)
        + far.astype(jnp.float32)
    )


def reduce_phase(total, phase, wire_type, extra=None):
    half = total.shape[-2] // 2

    def term(k):
        if extra is None:
            return total[k]
        return total[k] + extra[k].astype(jnp.float32)

    far = term(2)
    got_minus = ring_shift(far[..., :half, :].astype(wire_type), phase, 1)
    got_plus = ring_shift(far[..., half:, :].astype(wire_type), phase, -1)
    ahead = term(1)
    ahead = jnp.concatenate(
        [ahead[..., :half, :] + got_minus.astype(jnp.float32), ahead[..., half:, :]], axis=-2
    )
    behind = term(3)
    behind = jnp.concatenate(
        [behind[..., :half, :], behind[..., half:, :] + got_plus.astype(jnp.float32)], axis=-2
    )
    from_minus = ring_shift(ahead.astype(wire_type), phase, 1)
    from_plus = ring_shift(behind.astype(wire_type), phase, -1)
    return term(0) + from_minus.astype(jnp.float32) + from_plus.astype(jnp.float32)


def scatter_rows(total, axis, wire_type):
    count = lax.axis_size(axis)
    index = lax.axis_index(axis)
    mask = count // 2
    while mask >= 1:
        half = total.shape[0] // 2
        lower, upper_part = total[:half], total[half:]
        upper = (index // mask) % 2 == 1
        keep = jnp.where(upper, upper_part, lower)
        send = jnp.where(upper, lower, upper_part)
        got = swapped(send.astype(wire_type), axis, mask)
        total = keep + got.astype(jnp.float32)
        mask //= 2
    return total


def aggregate_kernel(core_ref, where_ref, count_ref, tiles_ref, proj_ref, out_ref):
    row = pl.program_id(0)
    half_id = pl.program_id(1)
    tile_rows = pl.num_programs(0)
    slot_count, tile_size, _ = tiles_ref.shape
    base = (half_id * 2 + core_ref[0]) * tile_rows + row
    live = count_ref[base]
    part = jnp.zeros(out_ref.shape, jnp.float32)
    for slot in range(slot_count):
        piece = proj_ref[where_ref[base * slot_count + slot]]
        piece = jnp.where(slot < live, piece, jnp.zeros_like(piece))
        part = part + jnp.dot(tiles_ref[slot], piece, preferred_element_type=jnp.float32)

    @pl.when(half_id == 0)
    def _():
        out_ref[...] = part

    @pl.when(half_id != 0)
    def _():
        out_ref[...] += part


def aggregate_pair(core_id, spots, counts, tile_stack, buffer):
    blocks, tile_rows, slot_count, tile_size, _ = tile_stack.shape
    hidden_width = buffer.shape[-1]
    grid_spec = pltpu.PrefetchScalarGridSpec(
        num_scalar_prefetch=3,
        grid=(tile_rows, blocks // 2),
        in_specs=[
            pl.BlockSpec(
                (None, None, slot_count, tile_size, tile_size),
                lambda r, h, c, w, n: (h * 2 + c[0], r, 0, 0, 0),
            ),
            pl.BlockSpec(buffer.shape, lambda r, h, c, w, n: (0, 0, 0)),
        ],
        out_specs=pl.BlockSpec((None, tile_size, hidden_width), lambda r, h, c, w, n: (r, 0, 0)),
    )
    return pl.pallas_call(
        aggregate_kernel,
        grid_spec=grid_spec,
        out_shape=jax.ShapeDtypeStruct((tile_rows, tile_size, hidden_width), jnp.float32),
        compiler_params=pltpu.CompilerParams(dimension_semantics=("arbitrary", "arbitrary")),
    )(jnp.reshape(core_id, (1,)).astype(jnp.int32), spots, counts, tile_stack, buffer)


def spread_pair(core_id, spots, counts, tile_stack, sibling_tiles, grads, buffer_tiles):
    blocks, tile_rows, slot_count, tile_size, _ = tile_stack.shape
    hidden_width = grads.shape[2]
    halves = blocks // 2
    last = halves - 1

    def own_map(s, r, h, c, w, n):
        return (
            jnp.where(s == 0, h * 2 + c[0], last * 2 + c[0]),
            jnp.where(s == 0, r, tile_rows - 1),
            0, 0, 0,
        )

    def sibling_map(s, r, h, c, w, n):
        return (jnp.where(s == 1, h * 2 + c[0], c[0]), jnp.where(s == 1, r, 0), 0, 0, 0)

    def kernel(core_ref, where_ref, count_ref, own_ref, other_ref, grad_ref, out_ref, total_ref):
        source = pl.program_id(0)
        row = pl.program_id(1)
        half_id = pl.program_id(2)
        base = (half_id * 2 + core_ref[0]) * tile_rows + row
        live = count_ref[source * blocks * tile_rows + base]

        @pl.when((source == 0) & (row == 0) & (half_id == 0))
        def _():
            total_ref[...] = jnp.zeros(total_ref.shape, jnp.float32)

        def spread(tiles_ref):
            grad_rows = grad_ref[...]
            for slot in range(slot_count):
                spot = where_ref[(source * blocks * tile_rows + base) * slot_count + slot]
                term = jnp.dot(grad_rows, tiles_ref[slot], preferred_element_type=jnp.float32)

                @pl.when(slot < live)
                def _():
                    total_ref[spot] += term

        pl.when(source == 0)(lambda: spread(own_ref))
        pl.when(source == 1)(lambda: spread(other_ref))

        @pl.when((source == 1) & (row == tile_rows - 1) & (half_id == halves - 1))
        def _():
            out_ref[...] = total_ref[...]

    tile_spec = (None, None, slot_count, tile_size, tile_size)
    grid_spec = pltpu.PrefetchScalarGridSpec(
        num_scalar_prefetch=3,
        grid=(2, tile_rows, halves),
        in_specs=[
            pl.BlockSpec(tile_spec, own_map),
            pl.BlockSpec(tile_spec, sibling_map),
            pl.BlockSpec(
                (None, None, hidden_width, tile_size), lambda s, r, h, c, w, n: (s, r, 0, 0)
            ),
        ],
        out_specs=pl.BlockSpec(
            (buffer_tiles, hidden_width, tile_size), lambda s, r, h, c, w, n: (0, 0, 0)
        ),
        scratch_shapes=[
            pltpu.VMEM((buffer_tiles, hidden_width, tile_size), jnp.float32),
        ],
    )
    return pl.pallas_call(
        kernel,
        grid_spec=grid_spec,
        out_shape=jax.ShapeDtypeStruct((buffer_tiles, hidden_width, tile_size), jnp.float32),
        compiler_params=pltpu.CompilerParams(
            dimension_semantics=("arbitrary", "arbitrary", "arbitrary")
        ),
    )(
        jnp.reshape(core_id, (1,)).astype(jnp.int32),
        spots,
        counts,
        tile_stack,
        sibling_tiles,
        grads,
    )


def buffer_spots(tile_col, blk_id, feat_id, block_tiles, tiles_per_device):
    own = place_of(blk_id, feat_id)
    block = tile_col // block_tiles
    local = tile_col % block_tiles
    source_feat = local // tiles_per_device
    part = local % tiles_per_device
    source = place_of(block, source_feat)
    rel = {axis: (source[axis] - own[axis]) % RING for axis in ("y", "z", "x")}
    chunk = jnp.where(
        source["core"] == 0,
        rel["y"] * 16 + rel["z"] * 4 + rel["x"],
        rel["x"] * 16 + rel["z"] * 4 + rel["y"],
    )
    return (chunk * tiles_per_device + part).astype(jnp.int32)


def body(features_t, weight, tile_values, tile_col, tile_count, grad_out):
    cycle_size = lax.axis_size("blk")
    hidden_width = weight.shape[1]
    tile_size = tile_values.shape[1]
    rows_own = grad_out.shape[0]
    tile_rows = rows_own // tile_size
    block_rows = features_t.shape[1]
    block_tiles = block_rows // tile_size
    slot_count = tile_values.shape[0] // (cycle_size * tile_rows)
    feat_id = lax.axis_index("feat")
    blk_id = lax.axis_index("blk")
    core_id = blk_id % 2
    tile_stack = tile_values.reshape(cycle_size, tile_rows, slot_count, tile_size, tile_size)
    spots = buffer_spots(tile_col, blk_id, feat_id, block_tiles, tile_rows)
    sibling_tiles = sibling(tile_stack)
    sibling_col = sibling(tile_col)
    sibling_count = sibling(tile_count)
    buffer_tiles = block_tiles * 2

    features_own = lax.all_to_all(features_t, "feat", split_axis=1, concat_axis=0, tiled=True)
    projected = lax.dot_general(
        features_own, weight, (((0,), (0,)), ((), ())), preferred_element_type=jnp.float32
    ).astype(jnp.bfloat16)

    sibling_col, sibling_count, projected = lax.optimization_barrier(
        (sibling_col, sibling_count, projected)
    )
    sibling_spots = buffer_spots(sibling_col, blk_id, feat_id, block_tiles, tile_rows)
    gathered = gather_phase_direct(projected, 0)
    gathered = gather_phase_direct(gathered, 1)
    gathered = gather_phase(gathered, 2)
    own_buffer = gathered.reshape(buffer_tiles, tile_size, hidden_width)
    other_buffer = sibling(own_buffer)
    aggregate_sum = aggregate_pair(core_id, spots, tile_count, tile_stack, own_buffer)
    aggregate_sum = aggregate_sum + aggregate_pair(
        1 - core_id, spots, tile_count, tile_stack, other_buffer
    )

    pre_act = aggregate_sum.reshape(rows_own, hidden_width)
    sigmoid_y = jax.nn.sigmoid(pre_act)
    activations = (pre_act * sigmoid_y).astype(jnp.bfloat16)
    grad_pre = (
        grad_out.astype(jnp.float32) * sigmoid_y * (1.0 + pre_act * (1.0 - sigmoid_y))
    ).astype(jnp.bfloat16)
    grad_turned = grad_pre.reshape(tile_rows, tile_size, hidden_width).transpose(0, 2, 1)

    sibling_grad = sibling(grad_turned)
    total = spread_pair(
        core_id,
        jnp.concatenate([spots, sibling_spots]),
        jnp.concatenate([tile_count, sibling_count]),
        tile_stack,
        sibling_tiles,
        jnp.stack([grad_turned, sibling_grad]),
        buffer_tiles,
    )
    total = reduce_phase(
        total.reshape(RING, RING, RING, rows_own, hidden_width), 2, jnp.bfloat16
    )
    total = reduce_phase_direct(total, 1, jnp.bfloat16)
    total = reduce_phase_direct(total, 0, jnp.bfloat16)
    grad_hidden = (
        total.reshape(tile_rows, hidden_width, tile_size)
        .transpose(0, 2, 1)
        .reshape(rows_own, hidden_width)
        .astype(jnp.bfloat16)
    )

    weight_term = jnp.dot(features_own, grad_hidden, preferred_element_type=jnp.float32)
    features_grad_local = lax.dot_general(
        weight, grad_hidden, (((1,), (1,)), ((), ())), preferred_element_type=jnp.float32
    ).astype(jnp.bfloat16)
    feat_count = lax.axis_size("feat")
    shard_rows = weight_term.shape[0] // feat_count
    outgoing = jnp.concatenate(
        [
            weight_term.reshape(feat_count, shard_rows, hidden_width),
            features_grad_local.astype(jnp.float32).reshape(feat_count, shard_rows, rows_own),
        ],
        axis=2,
    )
    got = lax.all_to_all(outgoing, "feat", split_axis=0, concat_axis=0, tiled=True)
    weight_part = jnp.sum(got[:, :, :hidden_width], axis=0)
    grad_features = (
        got[:, :, hidden_width:].astype(jnp.bfloat16).transpose(1, 0, 2).reshape(shard_rows, -1)
    )
    weight_part = weight_part + swapped(weight_part, "blk", 1)
    weight_part = weight_part + swapped(weight_part, "blk", 2)
    grad_weight = weight_part * lax.rsqrt(jnp.float32(block_rows * cycle_size))
    return (activations, grad_features, grad_weight)


def solution(mesh):
    placed = (
        P("feat", "blk"),
        P(),
        P(("blk", "feat"), None, None),
        P(("blk", "feat")),
        P(("blk", "feat")),
        P(("blk", "feat"), None),
    )
    return jax.shard_map(
        body,
        mesh=mesh,
        in_specs=placed,
        out_specs=(P(("blk", "feat"), None), P("feat", "blk"), P("feat", None)),
        check_vma=False,
    )
```

```python
import jax
import jax.numpy as jnp
from jax import lax
from jax.sharding import PartitionSpec as P
from jax.experimental import pallas as pl
from jax.experimental.pallas import tpu as pltpu

RING = 4
GATHER_ORDER = (("x", "z", "y"), ("y", "z", "x"))
BOTH = ("blk", "feat")


def place_of(blk, feat):
    return {
        "core": blk % 2,
        "y": (blk // 2) * 2 + feat // 16,
        "z": (feat // 4) % 4,
        "x": feat % 4,
    }


def linear_of(place):
    blk = (place["y"] // 2) * 2 + place["core"]
    feat = (place["y"] % 2) * 16 + place["z"] * 4 + place["x"]
    return blk * 32 + feat


def ring_shift(block, phase, distance):
    route = []
    for blk in range(4):
        for feat in range(32):
            place = place_of(blk, feat)
            axis = GATHER_ORDER[place["core"]][phase]
            target = dict(place)
            target[axis] = (place[axis] + distance) % RING
            route.append((linear_of(place), linear_of(target)))
    return lax.ppermute(block, BOTH, route)


def sibling(block):
    return lax.ppermute(block, "blk", [(i, i ^ 1) for i in range(lax.axis_size("blk"))])


def swapped(block, axis, mask):
    count = lax.axis_size(axis)
    return lax.ppermute(block, axis, [(i, i ^ mask) for i in range(count)])


def gather_phase(block, phase):
    half = block.shape[-2] // 2
    from_minus = ring_shift(block, phase, 1)
    from_plus = ring_shift(block, phase, -1)
    far_low = ring_shift(from_minus[..., :half, :], phase, 1)
    far_high = ring_shift(from_plus[..., half:, :], phase, -1)
    far = jnp.concatenate([far_low, far_high], axis=-2)
    return jnp.stack([block, from_plus, far, from_minus])


def gather_phase_direct(block, phase):
    from_minus = ring_shift(block, phase, 1)
    from_plus = ring_shift(block, phase, -1)
    far = ring_shift(block, phase, 2)
    return jnp.stack([block, from_plus, far, from_minus])


def reduce_phase_direct(total, phase, wire_type):
    from_minus = ring_shift(total[1].astype(wire_type), phase, 1)
    from_plus = ring_shift(total[3].astype(wire_type), phase, -1)
    far = ring_shift(total[2].astype(wire_type), phase, 2)
    return (
        total[0]
        + from_minus.astype(jnp.float32)
        + from_plus.astype(jnp.float32)
        + far.astype(jnp.float32)
    )


def reduce_phase(total, phase, wire_type, extra=None):
    half = total.shape[-2] // 2

    def term(k):
        if extra is None:
            return total[k]
        return total[k] + extra[k].astype(jnp.float32)

    far = term(2)
    got_minus = ring_shift(far[..., :half, :].astype(wire_type), phase, 1)
    got_plus = ring_shift(far[..., half:, :].astype(wire_type), phase, -1)
    ahead = term(1)
    ahead = jnp.concatenate(
        [ahead[..., :half, :] + got_minus.astype(jnp.float32), ahead[..., half:, :]], axis=-2
    )
    behind = term(3)
    behind = jnp.concatenate(
        [behind[..., :half, :], behind[..., half:, :] + got_plus.astype(jnp.float32)], axis=-2
    )
    from_minus = ring_shift(ahead.astype(wire_type), phase, 1)
    from_plus = ring_shift(behind.astype(wire_type), phase, -1)
    return term(0) + from_minus.astype(jnp.float32) + from_plus.astype(jnp.float32)


def scatter_rows(total, axis, wire_type):
    count = lax.axis_size(axis)
    index = lax.axis_index(axis)
    mask = count // 2
    while mask >= 1:
        half = total.shape[0] // 2
        lower, upper_part = total[:half], total[half:]
        upper = (index // mask) % 2 == 1
        keep = jnp.where(upper, upper_part, lower)
        send = jnp.where(upper, lower, upper_part)
        got = swapped(send.astype(wire_type), axis, mask)
        total = keep + got.astype(jnp.float32)
        mask //= 2
    return total


def aggregate_kernel(core_ref, where_ref, count_ref, tiles_ref, proj_ref, out_ref):
    row = pl.program_id(0)
    half_id = pl.program_id(1)
    tile_rows = pl.num_programs(0)
    slot_count, tile_size, _ = tiles_ref.shape
    base = (half_id * 2 + core_ref[0]) * tile_rows + row
    live = count_ref[base]
    part = jnp.zeros(out_ref.shape, jnp.float32)
    for slot in range(slot_count):
        piece = proj_ref[where_ref[base * slot_count + slot]]
        piece = jnp.where(slot < live, piece, jnp.zeros_like(piece))
        part = part + jnp.dot(tiles_ref[slot], piece, preferred_element_type=jnp.float32)

    @pl.when(half_id == 0)
    def _():
        out_ref[...] = part

    @pl.when(half_id != 0)
    def _():
        out_ref[...] += part


def aggregate_pair(core_id, spots, counts, tile_stack, buffer):
    blocks, tile_rows, slot_count, tile_size, _ = tile_stack.shape
    hidden_width = buffer.shape[-1]
    grid_spec = pltpu.PrefetchScalarGridSpec(
        num_scalar_prefetch=3,
        grid=(tile_rows, blocks // 2),
        in_specs=[
            pl.BlockSpec(
                (None, None, slot_count, tile_size, tile_size),
                lambda r, h, c, w, n: (h * 2 + c[0], r, 0, 0, 0),
            ),
            pl.BlockSpec(buffer.shape, lambda r, h, c, w, n: (0, 0, 0)),
        ],
        out_specs=pl.BlockSpec((None, tile_size, hidden_width), lambda r, h, c, w, n: (r, 0, 0)),
    )
    return pl.pallas_call(
        aggregate_kernel,
        grid_spec=grid_spec,
        out_shape=jax.ShapeDtypeStruct((tile_rows, tile_size, hidden_width), jnp.float32),
        compiler_params=pltpu.CompilerParams(dimension_semantics=("arbitrary", "arbitrary")),
    )(jnp.reshape(core_id, (1,)).astype(jnp.int32), spots, counts, tile_stack, buffer)


def spread_pair(core_id, spots, counts, tile_stack, sibling_tiles, grads, buffer_tiles):
    blocks, tile_rows, slot_count, tile_size, _ = tile_stack.shape
    hidden_width = grads.shape[2]
    halves = blocks // 2
    last = halves - 1

    def own_map(s, r, h, c, w, n):
        return (
            jnp.where(s == 0, h * 2 + c[0], last * 2 + c[0]),
            jnp.where(s == 0, r, tile_rows - 1),
            0, 0, 0,
        )

    def sibling_map(s, r, h, c, w, n):
        return (jnp.where(s == 1, h * 2 + c[0], c[0]), jnp.where(s == 1, r, 0), 0, 0, 0)

    def kernel(core_ref, where_ref, count_ref, own_ref, other_ref, grad_ref, out_ref, total_ref):
        source = pl.program_id(0)
        row = pl.program_id(1)
        half_id = pl.program_id(2)
        base = (half_id * 2 + core_ref[0]) * tile_rows + row
        live = count_ref[source * blocks * tile_rows + base]

        @pl.when((source == 0) & (row == 0) & (half_id == 0))
        def _():
            total_ref[...] = jnp.zeros(total_ref.shape, jnp.float32)

        def spread(tiles_ref):
            grad_rows = grad_ref[...]
            for slot in range(slot_count):
                spot = where_ref[(source * blocks * tile_rows + base) * slot_count + slot]
                term = jnp.dot(grad_rows, tiles_ref[slot], preferred_element_type=jnp.float32)
                total_ref[spot] += jnp.where(slot < live, term, jnp.zeros_like(term))

        pl.when(source == 0)(lambda: spread(own_ref))
        pl.when(source == 1)(lambda: spread(other_ref))

        @pl.when((source == 1) & (row == tile_rows - 1) & (half_id == halves - 1))
        def _():
            out_ref[...] = total_ref[...]

    tile_spec = (None, None, slot_count, tile_size, tile_size)
    grid_spec = pltpu.PrefetchScalarGridSpec(
        num_scalar_prefetch=3,
        grid=(2, tile_rows, halves),
        in_specs=[
            pl.BlockSpec(tile_spec, own_map),
            pl.BlockSpec(tile_spec, sibling_map),
            pl.BlockSpec(
                (None, None, hidden_width, tile_size), lambda s, r, h, c, w, n: (s, r, 0, 0)
            ),
        ],
        out_specs=pl.BlockSpec(
            (buffer_tiles, hidden_width, tile_size), lambda s, r, h, c, w, n: (0, 0, 0)
        ),
        scratch_shapes=[
            pltpu.VMEM((buffer_tiles, hidden_width, tile_size), jnp.float32),
        ],
    )
    return pl.pallas_call(
        kernel,
        grid_spec=grid_spec,
        out_shape=jax.ShapeDtypeStruct((buffer_tiles, hidden_width, tile_size), jnp.float32),
        compiler_params=pltpu.CompilerParams(
            dimension_semantics=("arbitrary", "arbitrary", "arbitrary")
        ),
    )(
        jnp.reshape(core_id, (1,)).astype(jnp.int32),
        spots,
        counts,
        tile_stack,
        sibling_tiles,
        grads,
    )


def buffer_spots(tile_col, blk_id, feat_id, block_tiles, tiles_per_device):
    own = place_of(blk_id, feat_id)
    block = tile_col // block_tiles
    local = tile_col % block_tiles
    source_feat = local // tiles_per_device
    part = local % tiles_per_device
    source = place_of(block, source_feat)
    rel = {axis: (source[axis] - own[axis]) % RING for axis in ("y", "z", "x")}
    chunk = jnp.where(
        source["core"] == 0,
        rel["y"] * 16 + rel["z"] * 4 + rel["x"],
        rel["x"] * 16 + rel["z"] * 4 + rel["y"],
    )
    return (chunk * tiles_per_device + part).astype(jnp.int32)


def body(features_t, weight, tile_values, tile_col, tile_count, grad_out):
    cycle_size = lax.axis_size("blk")
    hidden_width = weight.shape[1]
    tile_size = tile_values.shape[1]
    rows_own = grad_out.shape[0]
    tile_rows = rows_own // tile_size
    block_rows = features_t.shape[1]
    block_tiles = block_rows // tile_size
    slot_count = tile_values.shape[0] // (cycle_size * tile_rows)
    feat_id = lax.axis_index("feat")
    blk_id = lax.axis_index("blk")
    core_id = blk_id % 2
    tile_stack = tile_values.reshape(cycle_size, tile_rows, slot_count, tile_size, tile_size)
    spots = buffer_spots(tile_col, blk_id, feat_id, block_tiles, tile_rows)
    sibling_tiles = sibling(tile_stack)
    sibling_col = sibling(tile_col)
    sibling_count = sibling(tile_count)
    buffer_tiles = block_tiles * 2

    features_own = lax.all_to_all(features_t, "feat", split_axis=1, concat_axis=0, tiled=True)
    projected = lax.dot_general(
        features_own, weight, (((0,), (0,)), ((), ())), preferred_element_type=jnp.float32
    ).astype(jnp.bfloat16)

    sibling_col, sibling_count, projected = lax.optimization_barrier(
        (sibling_col, sibling_count, projected)
    )
    sibling_spots = buffer_spots(sibling_col, blk_id, feat_id, block_tiles, tile_rows)
    gathered = gather_phase_direct(projected, 0)
    gathered = gather_phase_direct(gathered, 1)
    gathered = gather_phase(gathered, 2)
    own_buffer = gathered.reshape(buffer_tiles, tile_size, hidden_width)
    other_buffer = sibling(own_buffer)
    aggregate_sum = aggregate_pair(core_id, spots, tile_count, tile_stack, own_buffer)
    aggregate_sum = aggregate_sum + aggregate_pair(
        1 - core_id, spots, tile_count, tile_stack, other_buffer
    )

    pre_act = aggregate_sum.reshape(rows_own, hidden_width)
    sigmoid_y = jax.nn.sigmoid(pre_act)
    activations = (pre_act * sigmoid_y).astype(jnp.bfloat16)
    grad_pre = (
        grad_out.astype(jnp.float32) * sigmoid_y * (1.0 + pre_act * (1.0 - sigmoid_y))
    ).astype(jnp.bfloat16)
    grad_turned = grad_pre.reshape(tile_rows, tile_size, hidden_width).transpose(0, 2, 1)

    sibling_grad = sibling(grad_turned)
    total = spread_pair(
        core_id,
        jnp.concatenate([spots, sibling_spots]),
        jnp.concatenate([tile_count, sibling_count]),
        tile_stack,
        sibling_tiles,
        jnp.stack([grad_turned, sibling_grad]),
        buffer_tiles,
    )
    total = reduce_phase(
        total.reshape(RING, RING, RING, rows_own, hidden_width), 2, jnp.bfloat16
    )
    total = reduce_phase_direct(total, 1, jnp.bfloat16)
    total = reduce_phase_direct(total, 0, jnp.bfloat16)
    grad_hidden = (
        total.reshape(tile_rows, hidden_width, tile_size)
        .transpose(0, 2, 1)
        .reshape(rows_own, hidden_width)
        .astype(jnp.bfloat16)
    )

    weight_term = jnp.dot(features_own, grad_hidden, preferred_element_type=jnp.float32)
    features_grad_local = lax.dot_general(
        weight, grad_hidden, (((1,), (1,)), ((), ())), preferred_element_type=jnp.float32
    ).astype(jnp.bfloat16)
    feat_count = lax.axis_size("feat")
    shard_rows = weight_term.shape[0] // feat_count
    outgoing = jnp.concatenate(
        [
            weight_term.reshape(feat_count, shard_rows, hidden_width),
            features_grad_local.astype(jnp.float32).reshape(feat_count, shard_rows, rows_own),
        ],
        axis=2,
    )
    got = lax.all_to_all(outgoing, "feat", split_axis=0, concat_axis=0, tiled=True)
    weight_part = jnp.sum(got[:, :, :hidden_width], axis=0)
    grad_features = (
        got[:, :, hidden_width:].astype(jnp.bfloat16).transpose(1, 0, 2).reshape(shard_rows, -1)
    )
    weight_part = weight_part + swapped(weight_part, "blk", 1)
    weight_part = weight_part + swapped(weight_part, "blk", 2)
    grad_weight = weight_part * lax.rsqrt(jnp.float32(block_rows * cycle_size))
    return (activations, grad_features, grad_weight)


def solution(mesh):
    placed = (
        P("feat", "blk"),
        P(),
        P(("blk", "feat"), None, None),
        P(("blk", "feat")),
        P(("blk", "feat")),
        P(("blk", "feat"), None),
    )
    return jax.shard_map(
        body,
        mesh=mesh,
        in_specs=placed,
        out_specs=(P(("blk", "feat"), None), P("feat", "blk"), P("feat", None)),
        check_vma=False,
    )
```

```python
import jax
import jax.numpy as jnp
from jax import lax
from jax.sharding import PartitionSpec as P
from jax.experimental import pallas as pl
from jax.experimental.pallas import tpu as pltpu

RING = 4
GATHER_ORDER = (("x", "z", "y"), ("y", "z", "x"))
BOTH = ("blk", "feat")


def place_of(blk, feat):
    return {
        "core": blk % 2,
        "y": (blk // 2) * 2 + feat // 16,
        "z": (feat // 4) % 4,
        "x": feat % 4,
    }


def linear_of(place):
    blk = (place["y"] // 2) * 2 + place["core"]
    feat = (place["y"] % 2) * 16 + place["z"] * 4 + place["x"]
    return blk * 32 + feat


def ring_shift(block, phase, distance):
    route = []
    for blk in range(4):
        for feat in range(32):
            place = place_of(blk, feat)
            axis = GATHER_ORDER[place["core"]][phase]
            target = dict(place)
            target[axis] = (place[axis] + distance) % RING
            route.append((linear_of(place), linear_of(target)))
    return lax.ppermute(block, BOTH, route)


def sibling(block):
    return lax.ppermute(block, "blk", [(i, i ^ 1) for i in range(lax.axis_size("blk"))])


def swapped(block, axis, mask):
    count = lax.axis_size(axis)
    return lax.ppermute(block, axis, [(i, i ^ mask) for i in range(count)])


def gather_phase(block, phase):
    half = block.shape[-2] // 2
    from_minus = ring_shift(block, phase, 1)
    from_plus = ring_shift(block, phase, -1)
    far_low = ring_shift(from_minus[..., :half, :], phase, 1)
    far_high = ring_shift(from_plus[..., half:, :], phase, -1)
    far = jnp.concatenate([far_low, far_high], axis=-2)
    return jnp.stack([block, from_plus, far, from_minus])


def gather_phase_direct(block, phase):
    from_minus = ring_shift(block, phase, 1)
    from_plus = ring_shift(block, phase, -1)
    far = ring_shift(block, phase, 2)
    return jnp.stack([block, from_plus, far, from_minus])


def reduce_phase_direct(total, phase, wire_type):
    from_minus = ring_shift(total[1].astype(wire_type), phase, 1)
    from_plus = ring_shift(total[3].astype(wire_type), phase, -1)
    far = ring_shift(total[2].astype(wire_type), phase, 2)
    return (
        total[0]
        + from_minus.astype(jnp.float32)
        + from_plus.astype(jnp.float32)
        + far.astype(jnp.float32)
    )


def reduce_phase(total, phase, wire_type, extra=None):
    half = total.shape[-2] // 2

    def term(k):
        if extra is None:
            return total[k]
        return total[k] + extra[k].astype(jnp.float32)

    far = term(2)
    got_minus = ring_shift(far[..., :half, :].astype(wire_type), phase, 1)
    got_plus = ring_shift(far[..., half:, :].astype(wire_type), phase, -1)
    ahead = term(1)
    ahead = jnp.concatenate(
        [ahead[..., :half, :] + got_minus.astype(jnp.float32), ahead[..., half:, :]], axis=-2
    )
    behind = term(3)
    behind = jnp.concatenate(
        [behind[..., :half, :], behind[..., half:, :] + got_plus.astype(jnp.float32)], axis=-2
    )
    from_minus = ring_shift(ahead.astype(wire_type), phase, 1)
    from_plus = ring_shift(behind.astype(wire_type), phase, -1)
    return term(0) + from_minus.astype(jnp.float32) + from_plus.astype(jnp.float32)


def scatter_rows(total, axis, wire_type):
    count = lax.axis_size(axis)
    index = lax.axis_index(axis)
    mask = count // 2
    while mask >= 1:
        half = total.shape[0] // 2
        lower, upper_part = total[:half], total[half:]
        upper = (index // mask) % 2 == 1
        keep = jnp.where(upper, upper_part, lower)
        send = jnp.where(upper, lower, upper_part)
        got = swapped(send.astype(wire_type), axis, mask)
        total = keep + got.astype(jnp.float32)
        mask //= 2
    return total


def aggregate_kernel(core_ref, where_ref, count_ref, tiles_ref, proj_ref, out_ref):
    row = pl.program_id(0)
    half_id = pl.program_id(1)
    tile_rows = pl.num_programs(0)
    slot_count, tile_size, _ = tiles_ref.shape
    base = (half_id * 2 + core_ref[0]) * tile_rows + row
    live = count_ref[base]
    part = jnp.zeros(out_ref.shape, jnp.float32)
    for slot in range(slot_count):
        piece = proj_ref[where_ref[base * slot_count + slot]]
        piece = jnp.where(slot < live, piece, jnp.zeros_like(piece))
        part = part + jnp.dot(tiles_ref[slot], piece, preferred_element_type=jnp.float32)

    @pl.when(half_id == 0)
    def _():
        out_ref[...] = part

    @pl.when(half_id != 0)
    def _():
        out_ref[...] += part


def aggregate_pair(core_id, spots, counts, tile_stack, buffer):
    blocks, tile_rows, slot_count, tile_size, _ = tile_stack.shape
    hidden_width = buffer.shape[-1]
    grid_spec = pltpu.PrefetchScalarGridSpec(
        num_scalar_prefetch=3,
        grid=(tile_rows, blocks // 2),
        in_specs=[
            pl.BlockSpec(
                (None, None, slot_count, tile_size, tile_size),
                lambda r, h, c, w, n: (h * 2 + c[0], r, 0, 0, 0),
            ),
            pl.BlockSpec(buffer.shape, lambda r, h, c, w, n: (0, 0, 0)),
        ],
        out_specs=pl.BlockSpec((None, tile_size, hidden_width), lambda r, h, c, w, n: (r, 0, 0)),
    )
    return pl.pallas_call(
        aggregate_kernel,
        grid_spec=grid_spec,
        out_shape=jax.ShapeDtypeStruct((tile_rows, tile_size, hidden_width), jnp.float32),
        compiler_params=pltpu.CompilerParams(dimension_semantics=("arbitrary", "arbitrary")),
    )(jnp.reshape(core_id, (1,)).astype(jnp.int32), spots, counts, tile_stack, buffer)


def spread_pair(core_id, spots, counts, tile_stack, sibling_tiles, grads, buffer_tiles):
    blocks, tile_rows, slot_count, tile_size, _ = tile_stack.shape
    hidden_width = grads.shape[2]
    halves = blocks // 2
    last = halves - 1

    def own_map(s, r, h, c, w, n):
        return (
            jnp.where(s == 0, h * 2 + c[0], last * 2 + c[0]),
            jnp.where(s == 0, r, tile_rows - 1),
            0, 0, 0,
        )

    def sibling_map(s, r, h, c, w, n):
        return (jnp.where(s == 1, h * 2 + c[0], c[0]), jnp.where(s == 1, r, 0), 0, 0, 0)

    def kernel(core_ref, where_ref, count_ref, own_ref, other_ref, grad_ref, out_ref, total_ref):
        source = pl.program_id(0)
        row = pl.program_id(1)
        half_id = pl.program_id(2)
        base = (half_id * 2 + core_ref[0]) * tile_rows + row
        live = count_ref[source * blocks * tile_rows + base]

        @pl.when((source == 0) & (row == 0) & (half_id == 0))
        def _():
            total_ref[...] = jnp.zeros(total_ref.shape, jnp.float32)

        def spread(tiles_ref):
            grad_rows = grad_ref[...]
            for slot in range(slot_count):
                spot = where_ref[(source * blocks * tile_rows + base) * slot_count + slot]
                term = jnp.dot(grad_rows, tiles_ref[slot], preferred_element_type=jnp.float32)
                total_ref[spot] += jnp.where(slot < live, term, jnp.zeros_like(term))

        pl.when(source == 0)(lambda: spread(own_ref))
        pl.when(source == 1)(lambda: spread(other_ref))

        @pl.when((source == 1) & (row == tile_rows - 1) & (half_id == halves - 1))
        def _():
            out_ref[...] = total_ref[...].astype(out_ref.dtype)

    tile_spec = (None, None, slot_count, tile_size, tile_size)
    grid_spec = pltpu.PrefetchScalarGridSpec(
        num_scalar_prefetch=3,
        grid=(2, tile_rows, halves),
        in_specs=[
            pl.BlockSpec(tile_spec, own_map),
            pl.BlockSpec(tile_spec, sibling_map),
            pl.BlockSpec(
                (None, None, hidden_width, tile_size), lambda s, r, h, c, w, n: (s, r, 0, 0)
            ),
        ],
        out_specs=pl.BlockSpec(
            (buffer_tiles, hidden_width, tile_size), lambda s, r, h, c, w, n: (0, 0, 0)
        ),
        scratch_shapes=[
            pltpu.VMEM((buffer_tiles, hidden_width, tile_size), jnp.float32),
        ],
    )
    return pl.pallas_call(
        kernel,
        grid_spec=grid_spec,
        out_shape=jax.ShapeDtypeStruct((buffer_tiles, hidden_width, tile_size), jnp.bfloat16),
        compiler_params=pltpu.CompilerParams(
            dimension_semantics=("arbitrary", "arbitrary", "arbitrary")
        ),
    )(
        jnp.reshape(core_id, (1,)).astype(jnp.int32),
        spots,
        counts,
        tile_stack,
        sibling_tiles,
        grads,
    )


def buffer_spots(tile_col, blk_id, feat_id, block_tiles, tiles_per_device):
    own = place_of(blk_id, feat_id)
    block = tile_col // block_tiles
    local = tile_col % block_tiles
    source_feat = local // tiles_per_device
    part = local % tiles_per_device
    source = place_of(block, source_feat)
    rel = {axis: (source[axis] - own[axis]) % RING for axis in ("y", "z", "x")}
    chunk = jnp.where(
        source["core"] == 0,
        rel["y"] * 16 + rel["z"] * 4 + rel["x"],
        rel["x"] * 16 + rel["z"] * 4 + rel["y"],
    )
    return (chunk * tiles_per_device + part).astype(jnp.int32)


def body(features_t, weight, tile_values, tile_col, tile_count, grad_out):
    cycle_size = lax.axis_size("blk")
    hidden_width = weight.shape[1]
    tile_size = tile_values.shape[1]
    rows_own = grad_out.shape[0]
    tile_rows = rows_own // tile_size
    block_rows = features_t.shape[1]
    block_tiles = block_rows // tile_size
    slot_count = tile_values.shape[0] // (cycle_size * tile_rows)
    feat_id = lax.axis_index("feat")
    blk_id = lax.axis_index("blk")
    core_id = blk_id % 2
    tile_stack = tile_values.reshape(cycle_size, tile_rows, slot_count, tile_size, tile_size)
    spots = buffer_spots(tile_col, blk_id, feat_id, block_tiles, tile_rows)
    sibling_tiles = sibling(tile_stack)
    sibling_col = sibling(tile_col)
    sibling_count = sibling(tile_count)
    buffer_tiles = block_tiles * 2

    features_own = lax.all_to_all(features_t, "feat", split_axis=1, concat_axis=0, tiled=True)
    projected = lax.dot_general(
        features_own, weight, (((0,), (0,)), ((), ())), preferred_element_type=jnp.float32
    ).astype(jnp.bfloat16)

    sibling_col, sibling_count, projected = lax.optimization_barrier(
        (sibling_col, sibling_count, projected)
    )
    sibling_spots = buffer_spots(sibling_col, blk_id, feat_id, block_tiles, tile_rows)
    gathered = gather_phase_direct(projected, 0)
    gathered = gather_phase_direct(gathered, 1)
    gathered = gather_phase(gathered, 2)
    own_buffer = gathered.reshape(buffer_tiles, tile_size, hidden_width)
    other_buffer = sibling(own_buffer)
    aggregate_sum = aggregate_pair(core_id, spots, tile_count, tile_stack, own_buffer)
    aggregate_sum = aggregate_sum + aggregate_pair(
        1 - core_id, spots, tile_count, tile_stack, other_buffer
    )

    pre_act = aggregate_sum.reshape(rows_own, hidden_width)
    sigmoid_y = jax.nn.sigmoid(pre_act)
    activations = (pre_act * sigmoid_y).astype(jnp.bfloat16)
    grad_pre = (
        grad_out.astype(jnp.float32) * sigmoid_y * (1.0 + pre_act * (1.0 - sigmoid_y))
    ).astype(jnp.bfloat16)
    grad_turned = grad_pre.reshape(tile_rows, tile_size, hidden_width).transpose(0, 2, 1)

    sibling_grad = sibling(grad_turned)
    total = spread_pair(
        core_id,
        jnp.concatenate([spots, sibling_spots]),
        jnp.concatenate([tile_count, sibling_count]),
        tile_stack,
        sibling_tiles,
        jnp.stack([grad_turned, sibling_grad]),
        buffer_tiles,
    )
    total = reduce_phase(
        total.reshape(RING, RING, RING, rows_own, hidden_width), 2, jnp.bfloat16
    )
    total = reduce_phase_direct(total, 1, jnp.bfloat16)
    total = reduce_phase_direct(total, 0, jnp.bfloat16)
    grad_hidden = (
        total.reshape(tile_rows, hidden_width, tile_size)
        .transpose(0, 2, 1)
        .reshape(rows_own, hidden_width)
        .astype(jnp.bfloat16)
    )

    weight_term = jnp.dot(features_own, grad_hidden, preferred_element_type=jnp.float32)
    features_grad_local = lax.dot_general(
        weight, grad_hidden, (((1,), (1,)), ((), ())), preferred_element_type=jnp.float32
    ).astype(jnp.bfloat16)
    feat_count = lax.axis_size("feat")
    shard_rows = weight_term.shape[0] // feat_count
    outgoing = jnp.concatenate(
        [
            weight_term.reshape(feat_count, shard_rows, hidden_width),
            features_grad_local.astype(jnp.float32).reshape(feat_count, shard_rows, rows_own),
        ],
        axis=2,
    )
    got = lax.all_to_all(outgoing, "feat", split_axis=0, concat_axis=0, tiled=True)
    weight_part = jnp.sum(got[:, :, :hidden_width], axis=0)
    grad_features = (
        got[:, :, hidden_width:].astype(jnp.bfloat16).transpose(1, 0, 2).reshape(shard_rows, -1)
    )
    weight_part = weight_part + swapped(weight_part, "blk", 1)
    weight_part = weight_part + swapped(weight_part, "blk", 2)
    grad_weight = weight_part * lax.rsqrt(jnp.float32(block_rows * cycle_size))
    return (activations, grad_features, grad_weight)


def solution(mesh):
    placed = (
        P("feat", "blk"),
        P(),
        P(("blk", "feat"), None, None),
        P(("blk", "feat")),
        P(("blk", "feat")),
        P(("blk", "feat"), None),
    )
    return jax.shard_map(
        body,
        mesh=mesh,
        in_specs=placed,
        out_specs=(P(("blk", "feat"), None), P("feat", "blk"), P("feat", None)),
        check_vma=False,
    )
```
